32 devices in a mesh: grp: 4 (over y, x), mem: 2 (over core), row: 4 (over z).
Axes of the slice: x: 2, y: 2, z: 4, core: 2. Of those that a mesh axis runs over, the one named last changes fastest.
Arguments:
- field: bfloat16 [4, 512, 16384], P(None, ('grp', 'mem', 'row')), may hold values from -60 to 60
- counts: int32 [32], P(('grp', 'mem', 'row')), may hold values from 1 to 6, as said below
- kappa_rows: float32 [512], P(('grp', 'mem', 'row')), may hold values from 0.7 to 1
- kappa_cols: bfloat16 [16384], replicated, may hold values from 0.69921875 to 1
- drift_rows: float32 [2, 512], P(None, ('grp', 'mem', 'row')), may hold values from -0.95 to 0.95
- drift_cols: bfloat16 [2, 16384], replicated, may hold values from -0.94921875 to 0.94921875
- assign: int32 [32], replicated, may hold values from 0 to 3
- buffer: bfloat16 [4, 32, 4, 1024], P('grp', 'mem'), may hold values from -30 to 30
- lift_weight: bfloat16 [4, 32], replicated, may hold values from -3 to 3
- lift_bias: float32 [32], replicated, may hold values from -3 to 3
- point_weight: bfloat16 [32, 32], P(None, 'row'), may hold values from -1 to 1
- point_bias: float32 [32], P('row'), may hold values from -3 to 3
- spectral_weight: bfloat16 [2, 32, 32, 32, 16], P(None, None, 'row'), may hold values from -1 to 1
- cotangent: bfloat16 [4, 32, 32, 1024], P('grp', 'mem', 'row'), may hold values from -6 to 6
Outputs:
- fresh_sample: float32 [32, 4, 1024], P(('grp', 'mem', 'row'))
- layer_out: bfloat16 [4, 32, 32, 1024], P('grp', 'mem', 'row')
- grad_spectral: float32 [2, 32, 32, 32, 16], P(None, 'mem', 'row', 'grp')
The draws below stay inside these ranges and needn't reach their ends.
Inputs may be any that keep to these rules, and one draw needn't show every extreme that they name: The counts sum to 96, and a quarter of the slabs take exactly 6.
All inputs are finite; a program needn't handle non-finite values.
Results may differ from the reference program's by a relative error of at most 0.0049.
Values may be sent and summed in bfloat16 or wider, within the bound.
No kernel may reach another device: no remote copies, remote signals or barrier semaphores. Data moves between devices by JAX's collectives and lax.ppermute only.
A program may use at most 64 MiB of HBM per device.

```python
import math
import jax
import jax.numpy as jnp
import numpy as np
from jax import lax

C = 4
SW = 1024
FACTOR = 16
HID = 32
MODES = 16
SLABS = 32
H = 512
W = 16384
SH = 32
KY = 32
GROUPS = 4


def smooth_wave(key, leading, length, period):
    keys = jax.random.split(key, 2)
    amplitude = 0.25 * jax.random.normal(keys[0], leading + (MODES, 1), jnp.float32)
    phase_shift = jax.random.uniform(keys[1], leading + (MODES, 1), jnp.float32, 0.0, 2.0 * math.pi)
    orders = jnp.arange(MODES, dtype=jnp.int32)
    places = jnp.arange(length, dtype=jnp.int32)
    phase_angle = 2.0 * math.pi / period * (orders[:, None] * places[None, :] % period).astype(jnp.float32)
    return jnp.sum(amplitude * jnp.cos(phase_angle + phase_shift), axis=-2)


def draw_field(key, part):
    keys = jax.random.split(jax.random.fold_in(key, 11), 3)
    along_rows = smooth_wave(keys[0], (C,), H, H)
    along_cols = smooth_wave(keys[1], (C,), W, W)
    rough = 2.5 * jax.random.normal(keys[2], (C, H, W), jnp.float32)
    smooth = 1.5 * along_rows[:, :, None] * along_cols[:, None, :]
    return (smooth + rough).astype(jnp.bfloat16)


def draw_buffer(key, part):
    keys = jax.random.split(jax.random.fold_in(key, 23), 3)
    along_rows = smooth_wave(keys[0], (GROUPS, C), SH, SH)
    along_cols = smooth_wave(keys[1], (GROUPS, C), SW, SW)
    product = jnp.transpose(along_rows, (0, 2, 1))[:, :, :, None] * along_cols[:, None, :, :]
    rough = 0.3 * jax.random.normal(keys[2], (GROUPS, SH, C, SW), jnp.float32)
    smooth = 1.5 * product
    return (smooth + rough).astype(jnp.bfloat16)


def draw_counts(key, part):
    keys = jax.random.split(jax.random.fold_in(key, 37), 2)
    patterns = jnp.asarray(np.array([[6, 1, 2, 3], [6, 2, 2, 2], [6, 1, 1, 4], [6, 3, 2, 1], [6, 4, 1, 1]], dtype=np.int32))
    pattern_ids = jax.random.randint(keys[0], (SLABS // 4,), 0, 5)
    values = patterns[pattern_ids].reshape(-1)
    order = jax.random.permutation(keys[1], SLABS)
    return jnp.zeros((SLABS,), jnp.int32).at[order].set(values)


def set_ends(result, rng, smallest, high):
    dims = result.shape
    index_at = [jax.random.randint(jax.random.fold_in(rng, axis), (), 0, dims[axis]) for axis in range(len(dims))]
    result = result.at[tuple(index_at)].set(smallest)
    longest = dims.index(max(dims))
    index_at[longest] = (index_at[longest] + 1) % dims[longest]
    return result.at[tuple(index_at)].set(high)


def block_levels(stream_key, dims, cuts, smallest, largest):
    loudness = 1.0
    for axis_at, shards_of in cuts:
        heights = jax.random.uniform(jax.random.fold_in(jax.random.fold_in(stream_key, 6), axis_at), (shards_of,), jnp.float32, smallest / len(cuts), largest / len(cuts))
        loudness = loudness * jnp.repeat(jnp.exp(heights), dims[axis_at] // shards_of).reshape((-1,) + (1,) * (len(dims) - 1 - axis_at))
    return loudness


def scatter_about(stream_key, shape, deviation, most, pieces=(), held_as=jnp.bfloat16):
    values = deviation * jax.random.normal(stream_key, shape, jnp.float32)
    if pieces:
        values = values * block_levels(stream_key, shape, pieces, -0.22, 0.18)
    return jnp.clip(values, -most, most).astype(held_as)


def setup_inputs(seed: int = 0) -> dict:
    key_list = jax.random.split(jax.random.key(seed), 15)
    return {
        "field": draw_field(jax.random.fold_in(key_list[14], 71), 0),
        "counts": draw_counts(jax.random.fold_in(key_list[14], 71), 0),
        "kappa_rows": jnp.clip(jnp.exp(math.log(1.0) - 0.35667496 * jax.random.uniform(key_list[2], (H,), jnp.float32) ** block_levels(key_list[2], (H,), ((0, 32),), -0.2, 0.2)), 0.7, 1.0),
        "kappa_cols": jnp.clip(jnp.exp(jax.random.uniform(key_list[3], (W,), jnp.float32, math.log(0.69921875), math.log(1.0))), 0.69921875, 1.0).astype(jnp.bfloat16),
        "drift_rows": jnp.clip(jax.random.uniform(key_list[4], (2, H), jnp.float32, -0.95, 0.95) * block_levels(key_list[4], (2, H), ((1, 32),), -0.4, 0.0), -0.95, 0.95),
        "drift_cols": jnp.clip(jax.random.uniform(key_list[5], (2, W), jnp.float32, -0.94921875, 0.94921875), -0.94921875, 0.94921875).astype(jnp.bfloat16),
        "assign": set_ends(jax.random.randint(key_list[6], (SLABS,), 0, GROUPS), jax.random.fold_in(key_list[6], 1), 0, GROUPS - 1).astype(jnp.int32),
        "buffer": draw_buffer(jax.random.fold_in(key_list[14], 71), 0),
        "lift_weight": scatter_about(key_list[8], (C, HID), C ** -0.5, 3.0),
        "lift_bias": scatter_about(key_list[9], (HID,), 0.5, 3.0, (), jnp.float32),
        "point_weight": scatter_about(key_list[10], (HID, HID), HID ** -0.5, 1.0, ((1, 4),)),
        "point_bias": scatter_about(key_list[11], (HID,), 0.5, 3.0, ((0, 4),), jnp.float32),
        "spectral_weight": scatter_about(key_list[12], (2, HID, HID, KY, MODES), HID ** -0.5, 1.0, ((2, 4),)),
        "cotangent": scatter_about(key_list[13], (GROUPS, SH, HID, SW), 1.0, 6.0, ((0, 4), (1, 2), (2, 4))),
    }


window_time = 0.24

def slab_solve(slab_rows, above_row, below_row, substeps, kappa_row, drift_row, kappa_col, drift_col):
    diffusion = kappa_row[:, None] * kappa_col[None, :]
    drift_along = drift_row[0][:, None] * drift_col[0][None, :]
    drift_across = drift_row[1][:, None] * drift_col[1][None, :]
    step_size = window_time / substeps.astype(jnp.float32)

    def advance(number, current):
        stacked = jnp.concatenate([above_row, current, below_row], axis=1)
        upper_rows = stacked[:, :-2]
        lower_rows = stacked[:, 2:]
        right_cells = jnp.roll(current, -1, axis=2)
        left_cells = jnp.roll(current, 1, axis=2)
        change = diffusion * (right_cells + left_cells + upper_rows + lower_rows - 4.0 * current)
        change = change - 0.5 * drift_along * (right_cells - left_cells) - 0.5 * drift_across * (lower_rows - upper_rows)
        return current + step_size * change
    return lax.fori_loop(jnp.zeros((), jnp.int32), substeps, advance, slab_rows)

def coarsen(stepped):
    return stepped.reshape(C, FACTOR, SW, FACTOR).mean(axis=(1, 3))

def column_table():
    columns = jnp.arange(SW, dtype=jnp.int32)
    orders = jnp.arange(MODES, dtype=jnp.int32)
    phase_angle = 2.0 * math.pi / SW * (columns[:, None] * orders[None, :] % SW).astype(jnp.float32)
    return jnp.concatenate([jnp.cos(phase_angle), -jnp.sin(phase_angle)], axis=1).astype(jnp.bfloat16)

def inverse_table():
    columns = jnp.arange(SW, dtype=jnp.int32)
    orders = jnp.arange(MODES, dtype=jnp.int32)
    phase_angle = 2.0 * math.pi / SW * (orders[:, None] * columns[None, :] % SW).astype(jnp.float32)
    weights = jnp.where(orders == 0, 1.0, 2.0).astype(jnp.float32)[:, None]
    return jnp.concatenate([weights * jnp.cos(phase_angle), -weights * jnp.sin(phase_angle)], axis=0)

def row_tables(row_ids, total_rows):
    orders = jnp.arange(2 * MODES, dtype=jnp.int32)
    wave_numbers = jnp.where(orders < MODES, orders, total_rows - 2 * MODES + orders)
    phase_angle = 2.0 * math.pi / total_rows * (wave_numbers[:, None] * row_ids[None, :] % total_rows).astype(jnp.float32)
    return (jnp.cos(phase_angle), jnp.sin(phase_angle))

def rows_forward(part_real, part_imag, cosine_table, sine_table):
    highest = lax.Precision.HIGHEST
    real_part = jnp.einsum('jy,yhl->hjl', cosine_table, part_real, precision=highest) + jnp.einsum('jy,yhl->hjl', sine_table, part_imag, precision=highest)
    imag_part = jnp.einsum('jy,yhl->hjl', cosine_table, part_imag, precision=highest) - jnp.einsum('jy,yhl->hjl', sine_table, part_real, precision=highest)
    return (real_part, imag_part)

def rows_inverse(mixed_real, mixed_imag, cosine_table, sine_table):
    highest = lax.Precision.HIGHEST
    rows_real = jnp.einsum('jy,ojl->yol', cosine_table, mixed_real, precision=highest) - jnp.einsum('jy,ojl->yol', sine_table, mixed_imag, precision=highest)
    rows_imag = jnp.einsum('jy,ojl->yol', sine_table, mixed_real, precision=highest) + jnp.einsum('jy,ojl->yol', cosine_table, mixed_imag, precision=highest)
    return jnp.concatenate([rows_real, rows_imag], axis=2)

def mix_modes(spectral, mode_real, mode_imag):
    highest = lax.Precision.HIGHEST
    mixed_real = jnp.einsum('hojl,hjl->ojl', spectral[0], mode_real, precision=highest) - jnp.einsum('hojl,hjl->ojl', spectral[1], mode_imag, precision=highest)
    mixed_imag = jnp.einsum('hojl,hjl->ojl', spectral[0], mode_imag, precision=highest) + jnp.einsum('hojl,hjl->ojl', spectral[1], mode_real, precision=highest)
    return (mixed_real, mixed_imag)

def gelu_slope(pre_act):
    normal_cdf = 0.5 * (1.0 + lax.erf(pre_act * (1.0 / math.sqrt(2.0))))
    density = jnp.exp(-0.5 * pre_act * pre_act) * (1.0 / math.sqrt(2.0 * math.pi))
    return normal_cdf + pre_act * density

def weight_grads(back_real, back_imag, mode_real, mode_imag):
    highest = lax.Precision.HIGHEST
    grad_real = jnp.einsum('ojl,hjl->hojl', back_real, mode_real, precision=highest) + jnp.einsum('ojl,hjl->hojl', back_imag, mode_imag, precision=highest)
    grad_imag = jnp.einsum('ojl,hjl->hojl', back_imag, mode_real, precision=highest) - jnp.einsum('ojl,hjl->hojl', back_real, mode_imag, precision=highest)
    return jnp.stack([grad_real, grad_imag])

def reference(field, counts, kappa_rows, kappa_cols, drift_rows, drift_cols, assign, buffer, lift_weight, lift_bias, point_weight, point_bias, spectral_weight, cotangent):
    kappa_col = kappa_cols.astype(jnp.float32)
    drift_col = drift_cols.astype(jnp.float32)

    def one_slab(slab_index):
        first_row = (slab_index * FACTOR).astype(jnp.int32)
        slab_rows = lax.dynamic_slice_in_dim(field, first_row, FACTOR, 1).astype(jnp.float32)
        above_row = lax.dynamic_slice_in_dim(field, ((first_row + H - 1) % H).astype(jnp.int32), 1, 1).astype(jnp.float32)
        below_row = lax.dynamic_slice_in_dim(field, ((first_row + FACTOR) % H).astype(jnp.int32), 1, 1).astype(jnp.float32)
        kappa_row = lax.dynamic_slice_in_dim(kappa_rows, first_row, FACTOR, 0)
        drift_row = lax.dynamic_slice_in_dim(drift_rows, first_row, FACTOR, 1)
        stepped = slab_solve(slab_rows, above_row, below_row, counts[slab_index], kappa_row, drift_row, kappa_col, drift_col)
        return coarsen(stepped)
    fresh_sample = lax.map(one_slab, jnp.arange(SLABS, dtype=jnp.int32))
    coarse_low = fresh_sample.astype(jnp.bfloat16)
    norm_scale = 1.0 / math.sqrt(SH * SW)
    forward_table = column_table().astype(jnp.float32)
    inverse_cols = inverse_table()
    cosine_table, sine_table = row_tables(jnp.arange(SH, dtype=jnp.int32), SH)
    weights_mode = jnp.where(jnp.arange(MODES) == 0, 1.0, 2.0).astype(jnp.float32) * norm_scale
    spectral = spectral_weight.astype(jnp.float32)

    def one_group(group_index):
        chosen = (assign == group_index)[:, None, None]
        sample = jnp.where(chosen, coarse_low, buffer[group_index])
        hidden = (jnp.einsum('ycx,ch->yhx', sample.astype(jnp.float32), lift_weight.astype(jnp.float32)) + lift_bias[None, :, None]).astype(jnp.bfloat16)
        column_part = jnp.einsum('yhx,xk->yhk', hidden.astype(jnp.float32), forward_table)
        mode_real, mode_imag = rows_forward(column_part[:, :, :MODES], column_part[:, :, MODES:], cosine_table, sine_table)
        mode_real = mode_real * norm_scale
        mode_imag = mode_imag * norm_scale
        mixed_real, mixed_imag = mix_modes(spectral, mode_real, mode_imag)
        spatial = jnp.einsum('yok,kx->yox', rows_inverse(mixed_real, mixed_imag, cosine_table, sine_table), inverse_cols, precision=lax.Precision.HIGHEST) * norm_scale
        pre_act = spatial + jnp.einsum('yhx,ho->yox', hidden.astype(jnp.float32), point_weight.astype(jnp.float32)) + point_bias[None, :, None]
        layer_rows = jax.nn.gelu(pre_act, approximate=False).astype(jnp.bfloat16)
        back_signal = (cotangent[group_index].astype(jnp.float32) * gelu_slope(pre_act)).astype(jnp.bfloat16)
        back_part = jnp.einsum('yox,xk->yok', back_signal.astype(jnp.float32), forward_table)
        back_real, back_imag = rows_forward(back_part[:, :, :MODES], back_part[:, :, MODES:], cosine_table, sine_table)
        return (layer_rows, weight_grads(back_real * weights_mode, back_imag * weights_mode, mode_real, mode_imag))
    layers, group_grads = lax.map(one_group, jnp.arange(GROUPS, dtype=jnp.int32))
    return (fresh_sample, layers, lax.optimization_barrier(jnp.sum(group_grads, axis=0)) / GROUPS)
```

```python
import math

import jax
import jax.numpy as jnp
from jax import lax
from jax.sharding import PartitionSpec as P

C = 4
SW = 1024
FACTOR = 16
HID = 32
MODES = 16


window_time = 0.24


def with_halo(block, sides, width):
    for axis, dim in sides:
        count = lax.axis_size(axis)
        forward = [(i, i + 1) for i in range(count - 1)]
        forward.append((count - 1, 0))
        backward = [(target, source) for source, target in forward]
        low = lax.ppermute(
            lax.slice_in_dim(block, block.shape[dim] - width, None, axis=dim), axis, forward
        )
        high = lax.ppermute(lax.slice_in_dim(block, 0, width, axis=dim), axis, backward)
        block = jnp.concatenate([low, block, high], axis=dim)
    return block


def slab_solve(
    slab_rows, above_row, below_row, substeps, kappa_row, drift_row, kappa_col, drift_col
):
    diffusion = kappa_row[:, None] * kappa_col[None, :]
    drift_along = drift_row[0][:, None] * drift_col[0][None, :]
    drift_across = drift_row[1][:, None] * drift_col[1][None, :]
    step_size = window_time / substeps.astype(jnp.float32)

    def advance(number, current):
        stacked = jnp.concatenate([above_row, current, below_row], axis=1)
        upper_rows = stacked[:, :-2]
        lower_rows = stacked[:, 2:]
        right_cells = jnp.roll(current, -1, axis=2)
        left_cells = jnp.roll(current, 1, axis=2)
        change = diffusion * (right_cells + left_cells + upper_rows + lower_rows - 4.0 * current)
        change = (
            change
            - 0.5 * drift_along * (right_cells - left_cells)
            - 0.5 * drift_across * (lower_rows - upper_rows)
        )
        return current + step_size * change

    return lax.fori_loop(jnp.zeros((), jnp.int32), substeps, advance, slab_rows)


def coarsen(stepped):
    return stepped.reshape(C, FACTOR, SW, FACTOR).mean(axis=(1, 3))


def column_table():
    columns = jnp.arange(SW, dtype=jnp.int32)
    orders = jnp.arange(MODES, dtype=jnp.int32)
    phase_angle = 2.0 * math.pi / SW * (columns[:, None] * orders[None, :] % SW).astype(jnp.float32)
    return jnp.concatenate([jnp.cos(phase_angle), -jnp.sin(phase_angle)], axis=1).astype(
        jnp.bfloat16
    )


def inverse_table():
    columns = jnp.arange(SW, dtype=jnp.int32)
    orders = jnp.arange(MODES, dtype=jnp.int32)
    phase_angle = 2.0 * math.pi / SW * (orders[:, None] * columns[None, :] % SW).astype(jnp.float32)
    weights = jnp.where(orders == 0, 1.0, 2.0).astype(jnp.float32)[:, None]
    return jnp.concatenate(
        [weights * jnp.cos(phase_angle), -weights * jnp.sin(phase_angle)], axis=0
    )


def row_tables(row_ids, total_rows):
    orders = jnp.arange(2 * MODES, dtype=jnp.int32)
    wave_numbers = jnp.where(orders < MODES, orders, total_rows - 2 * MODES + orders)
    phase_angle = (
        2.0
        * math.pi
        / total_rows
        * (wave_numbers[:, None] * row_ids[None, :] % total_rows).astype(jnp.float32)
    )
    return (jnp.cos(phase_angle), jnp.sin(phase_angle))


def rows_forward(part_real, part_imag, cosine_table, sine_table):
    highest = lax.Precision.HIGHEST
    real_part = jnp.einsum("jy,yhl->hjl", cosine_table, part_real, precision=highest) + jnp.einsum(
        "jy,yhl->hjl", sine_table, part_imag, precision=highest
    )
    imag_part = jnp.einsum("jy,yhl->hjl", cosine_table, part_imag, precision=highest) - jnp.einsum(
        "jy,yhl->hjl", sine_table, part_real, precision=highest
    )
    return (real_part, imag_part)


def rows_inverse(mixed_real, mixed_imag, cosine_table, sine_table):
    highest = lax.Precision.HIGHEST
    rows_real = jnp.einsum("jy,ojl->yol", cosine_table, mixed_real, precision=highest) - jnp.einsum(
        "jy,ojl->yol", sine_table, mixed_imag, precision=highest
    )
    rows_imag = jnp.einsum("jy,ojl->yol", sine_table, mixed_real, precision=highest) + jnp.einsum(
        "jy,ojl->yol", cosine_table, mixed_imag, precision=highest
    )
    return jnp.concatenate([rows_real, rows_imag], axis=2)


def mix_modes(spectral, mode_real, mode_imag):
    highest = lax.Precision.HIGHEST
    mixed_real = jnp.einsum(
        "hojl,hjl->ojl", spectral[0], mode_real, precision=highest
    ) - jnp.einsum("hojl,hjl->ojl", spectral[1], mode_imag, precision=highest)
    mixed_imag = jnp.einsum(
        "hojl,hjl->ojl", spectral[0], mode_imag, precision=highest
    ) + jnp.einsum("hojl,hjl->ojl", spectral[1], mode_real, precision=highest)
    return (mixed_real, mixed_imag)


def gelu_slope(pre_act):
    normal_cdf = 0.5 * (1.0 + lax.erf(pre_act * (1.0 / math.sqrt(2.0))))
    density = jnp.exp(-0.5 * pre_act * pre_act) * (1.0 / math.sqrt(2.0 * math.pi))
    return normal_cdf + pre_act * density


def weight_grads(back_real, back_imag, mode_real, mode_imag):
    highest = lax.Precision.HIGHEST
    grad_real = jnp.einsum("ojl,hjl->hojl", back_real, mode_real, precision=highest) + jnp.einsum(
        "ojl,hjl->hojl", back_imag, mode_imag, precision=highest
    )
    grad_imag = jnp.einsum("ojl,hjl->hojl", back_imag, mode_real, precision=highest) - jnp.einsum(
        "ojl,hjl->hojl", back_real, mode_imag, precision=highest
    )
    return jnp.stack([grad_real, grad_imag])


def lift_rows(sample, lift_weight, lift_bias):
    lifted = jnp.einsum("ycx,ch->yhx", sample, lift_weight, preferred_element_type=jnp.float32)
    return (lifted + lift_bias[None, :, None]).astype(jnp.bfloat16)


def gather_along(block, axis):
    count = lax.axis_size(axis)
    index = lax.axis_index(axis)
    gathered = jnp.zeros((count,) + block.shape, block.dtype)
    for shift in range(count):
        if shift == 0:
            piece = block
        else:
            piece = lax.ppermute(block, axis, [(i, (i + shift) % count) for i in range(count)])
        gathered = lax.dynamic_update_index_in_dim(gathered, piece, (index - shift) % count, 0)
    return gathered


def gather_rows(block, axes):
    for axis in reversed(axes):
        block = gather_along(block, axis)
    return block.reshape((-1,) + block.shape[len(axes):])


def pair_sum(values, axis):
    if lax.axis_size(axis) != 2:
        return lax.psum(values, axis)
    other = lax.ppermute(values, axis, [(0, 1), (1, 0)])
    return jax.tree.map(lambda mine, theirs: mine + theirs, values, other)


def group_grads(back_real, back_imag, mode_real, mode_imag, axis):
    count = lax.axis_size(axis)
    index = lax.axis_index(axis)
    block = mode_real.shape[1] // count
    total = None
    for shift in range(count):
        target = (index + shift) % count
        piece = tuple(
            lax.dynamic_slice_in_dim(part, target * block, block, 1)
            for part in (back_real, back_imag, mode_real, mode_imag)
        )
        if shift:
            piece = lax.ppermute(piece, axis, [(i, (i + shift) % count) for i in range(count)])
        term = weight_grads(*piece)
        total = term if total is None else total + term
    return total


def body(
    field,
    counts,
    kappa_rows,
    kappa_cols,
    drift_rows,
    drift_cols,
    assign,
    buffer,
    lift_weight,
    lift_bias,
    point_weight,
    point_bias,
    spectral_weight,
    cotangent,
):
    padded = with_halo(field, ((("grp", "mem", "row"), 1),), 1)
    stepped = slab_solve(
        padded[:, 1:-1].astype(jnp.float32),
        padded[:, :1].astype(jnp.float32),
        padded[:, -1:].astype(jnp.float32),
        counts[0],
        kappa_rows,
        drift_rows,
        kappa_cols.astype(jnp.float32),
        drift_cols.astype(jnp.float32),
    )
    coarse_rows = coarsen(stepped)[None]
    coarse_low = coarse_rows.astype(jnp.bfloat16)
    member = lax.axis_index("mem")
    member_rows = buffer.shape[1]
    total_rows = member_rows * lax.axis_size("mem")
    row_ids = member * member_rows + jnp.arange(member_rows, dtype=jnp.int32)
    owners = lax.dynamic_slice_in_dim(assign, member * member_rows, member_rows, 0)
    chosen = (owners == lax.axis_index("grp"))[:, None, None]
    forward_table = column_table()
    every_row = gather_rows(coarse_low[0], ("grp", "mem", "row"))
    fresh_rows = lax.dynamic_slice_in_dim(every_row, member * member_rows, member_rows, 0)
    sample = jnp.where(chosen, fresh_rows, buffer[0])
    hidden = lift_rows(sample, lift_weight, lift_bias)
    column_part = jnp.einsum(
        "yhx,xk->yhk", hidden, forward_table, preferred_element_type=jnp.float32
    )
    norm_scale = 1.0 / math.sqrt(total_rows * SW)
    cosine_table, sine_table = row_tables(row_ids, total_rows)
    part_real, part_imag = rows_forward(
        column_part[:, :, :MODES], column_part[:, :, MODES:], cosine_table, sine_table
    )
    mode_real, mode_imag = pair_sum((part_real * norm_scale, part_imag * norm_scale), "mem")
    mixed_real, mixed_imag = mix_modes(spectral_weight.astype(jnp.float32), mode_real, mode_imag)
    spatial = (
        jnp.einsum(
            "yok,kx->yox",
            rows_inverse(mixed_real, mixed_imag, cosine_table, sine_table),
            inverse_table(),
            precision=lax.Precision.HIGHEST,
        )
        * norm_scale
    )
    pre_act = (
        spatial
        + jnp.einsum("yhx,ho->yox", hidden, point_weight, preferred_element_type=jnp.float32)
        + point_bias[None, :, None]
    )
    layer_rows = jax.nn.gelu(pre_act, approximate=False).astype(jnp.bfloat16)[None]
    back_signal = (cotangent[0].astype(jnp.float32) * gelu_slope(pre_act)).astype(jnp.bfloat16)
    back_part = jnp.einsum(
        "yox,xk->yok", back_signal, forward_table, preferred_element_type=jnp.float32
    )
    back_real, back_imag = rows_forward(
        back_part[:, :, :MODES], back_part[:, :, MODES:], cosine_table, sine_table
    )
    weights_mode = jnp.where(jnp.arange(MODES) == 0, 1.0, 2.0).astype(jnp.float32) * norm_scale
    back_real, back_imag = pair_sum((back_real * weights_mode, back_imag * weights_mode), "mem")
    block_size = HID // lax.axis_size("mem")
    block_real = lax.dynamic_slice_in_dim(mode_real, member * block_size, block_size, 0)
    block_imag = lax.dynamic_slice_in_dim(mode_imag, member * block_size, block_size, 0)
    summed = group_grads(back_real, back_imag, block_real, block_imag, "grp")
    return (coarse_rows, layer_rows, summed / lax.axis_size("grp"))


def solution(mesh):
    in_specs = (
        P(None, ("grp", "mem", "row"), None),
        P(("grp", "mem", "row")),
        P(("grp", "mem", "row")),
        P(),
        P(None, ("grp", "mem", "row")),
        P(),
        P(),
        P("grp", "mem", None, None),
        P(),
        P(),
        P(None, "row"),
        P("row"),
        P(None, None, "row", None, None),
        P("grp", "mem", "row", None),
    )
    out_specs = (
        P(("grp", "mem", "row"), None, None),
        P("grp", "mem", "row", None),
        P(None, "mem", "row", "grp", None),
    )
    return jax.shard_map(body, mesh=mesh, in_specs=in_specs, out_specs=out_specs, check_vma=False)
```

```python
import math

import jax
import jax.numpy as jnp
from jax import lax
from jax.experimental import pallas as pl
from jax.experimental.pallas import tpu as pltpu
from jax.sharding import PartitionSpec as P

C = 4
SW = 1024
FACTOR = 16
HID = 32
MODES = 16


window_time = 0.24


def with_halo(block, sides, width):
    for axis, dim in sides:
        count = lax.axis_size(axis)
        forward = [(i, i + 1) for i in range(count - 1)]
        forward.append((count - 1, 0))
        backward = [(target, source) for source, target in forward]
        low = lax.ppermute(
            lax.slice_in_dim(block, block.shape[dim] - width, None, axis=dim), axis, forward
        )
        high = lax.ppermute(lax.slice_in_dim(block, 0, width, axis=dim), axis, backward)
        block = jnp.concatenate([low, block, high], axis=dim)
    return block


def halo_rows(block, axis):
    count = lax.axis_size(axis)
    forward = [(i, (i + 1) % count) for i in range(count)]
    backward = [((i + 1) % count, i) for i in range(count)]
    above = lax.ppermute(block[:, -1:], axis, forward)
    below = lax.ppermute(block[:, :1], axis, backward)
    return above, below


def slab_solve(
    slab_rows, above_row, below_row, substeps, kappa_row, drift_row, kappa_col, drift_col
):
    diffusion = kappa_row[:, None] * kappa_col[None, :]
    drift_along = drift_row[0][:, None] * drift_col[0][None, :]
    drift_across = drift_row[1][:, None] * drift_col[1][None, :]
    step_size = window_time / substeps.astype(jnp.float32)

    def advance(number, current):
        stacked = jnp.concatenate([above_row, current, below_row], axis=1)
        upper_rows = stacked[:, :-2]
        lower_rows = stacked[:, 2:]
        right_cells = jnp.roll(current, -1, axis=2)
        left_cells = jnp.roll(current, 1, axis=2)
        change = diffusion * (right_cells + left_cells + upper_rows + lower_rows - 4.0 * current)
        change = (
            change
            - 0.5 * drift_along * (right_cells - left_cells)
            - 0.5 * drift_across * (lower_rows - upper_rows)
        )
        return current + step_size * change

    return lax.fori_loop(jnp.zeros((), jnp.int32), substeps, advance, slab_rows)


CHUNK = 512


def solve_kernel(
    step_ref, count_ref, field_ref, above_ref, below_ref, krow_ref, drow_ref, kcol_ref, dcol_ref,
    out_ref, state_ref, coef_ref,
):
    tracers, rows, width = field_ref.shape
    chunks = width // CHUNK

    def chunk_at(index):
        return pl.ds(pl.multiple_of(index * CHUNK, CHUNK), CHUNK)

    def prepare(index, carry):
        cols = chunk_at(index)
        coef_ref[0, :, cols] = krow_ref[...] * kcol_ref[:, cols].astype(jnp.float32)
        coef_ref[1, :, cols] = 0.5 * (drow_ref[0] * dcol_ref[0, :, cols].astype(jnp.float32))
        coef_ref[2, :, cols] = 0.5 * (drow_ref[1] * dcol_ref[1, :, cols].astype(jnp.float32))
        for tracer in range(tracers):
            state_ref[0, tracer, :, cols] = field_ref[tracer, :, cols].astype(jnp.float32)
        return carry

    lax.fori_loop(0, chunks, prepare, 0)
    step = step_ref[0]
    row_ids = lax.broadcasted_iota(jnp.int32, (rows, CHUNK), 0)

    def substep(number, carry):
        source = number % 2
        target = 1 - source

        def update(index, inner):
            tracer = index // chunks
            column = index % chunks
            cols = chunk_at(column)
            before = pl.ds(pl.multiple_of(((column * CHUNK - 128) % width), 128), 128)
            after = pl.ds(pl.multiple_of((((column + 1) * CHUNK) % width), 128), 128)
            current = state_ref[source, tracer, :, cols]
            extended = jnp.concatenate(
                [state_ref[source, tracer, :, before], current, state_ref[source, tracer, :, after]],
                axis=1,
            )
            span = CHUNK + 256
            right_cells = pltpu.roll(extended, span - 1, 1)[:, 128 : 128 + CHUNK]
            left_cells = pltpu.roll(extended, 1, 1)[:, 128 : 128 + CHUNK]
            upper_rows = jnp.where(
                row_ids == 0, above_ref[tracer, :, cols], pltpu.roll(current, 1, 0)
            )
            lower_rows = jnp.where(
                row_ids == rows - 1, below_ref[tracer, :, cols], pltpu.roll(current, rows - 1, 0)
            )
            change = coef_ref[0, :, cols] * (
                right_cells + left_cells + upper_rows + lower_rows - 4.0 * current
            )
            change = (
                change
                - coef_ref[1, :, cols] * (right_cells - left_cells)
                - coef_ref[2, :, cols] * (lower_rows - upper_rows)
            )
            state_ref[target, tracer, :, cols] = current + step * change
            return inner

        lax.fori_loop(0, tracers * chunks, update, 0)
        return carry

    total = count_ref[0]
    lax.fori_loop(0, total, substep, 0)
    final = total % 2

    def collect(index, carry):
        tracer = index // chunks
        cols = chunk_at(index % chunks)
        out_ref[tracer, :, cols] = jnp.sum(state_ref[final, tracer, :, cols], axis=0, keepdims=True)
        return carry

    lax.fori_loop(0, tracers * chunks, collect, 0)


def solve_rows(field, above_row, below_row, substeps, kappa_row, drift_row, kappa_col, drift_col):
    tracers, rows, width = field.shape
    step = (window_time / substeps.astype(jnp.float32)).reshape(1)
    smem = pl.BlockSpec(memory_space=pltpu.SMEM)
    vmem = pl.BlockSpec(memory_space=pltpu.VMEM)
    return pl.pallas_call(
        solve_kernel,
        out_shape=jax.ShapeDtypeStruct((tracers, 1, width), jnp.float32),
        in_specs=[smem, smem] + [vmem] * 7,
        out_specs=vmem,
        scratch_shapes=[
            pltpu.VMEM((2, tracers, rows, width), jnp.float32),
            pltpu.VMEM((3, rows, width), jnp.float32),
        ],
        compiler_params=pltpu.CompilerParams(vmem_limit_bytes=56 * 1024 * 1024),
    )(
        step,
        substeps.reshape(1),
        field,
        above_row.astype(jnp.float32),
        below_row.astype(jnp.float32),
        kappa_row.reshape(rows, 1),
        drift_row.reshape(2, rows, 1),
        kappa_col.reshape(1, width),
        drift_col.reshape(2, 1, width),
    )


def coarsen(stepped):
    return stepped.reshape(C, FACTOR, SW, FACTOR).mean(axis=(1, 3))


def column_table():
    columns = jnp.arange(SW, dtype=jnp.int32)
    orders = jnp.arange(MODES, dtype=jnp.int32)
    phase_angle = 2.0 * math.pi / SW * (columns[:, None] * orders[None, :] % SW).astype(jnp.float32)
    return jnp.concatenate([jnp.cos(phase_angle), -jnp.sin(phase_angle)], axis=1).astype(
        jnp.bfloat16
    )


def inverse_table():
    columns = jnp.arange(SW, dtype=jnp.int32)
    orders = jnp.arange(MODES, dtype=jnp.int32)
    phase_angle = 2.0 * math.pi / SW * (orders[:, None] * columns[None, :] % SW).astype(jnp.float32)
    weights = jnp.where(orders == 0, 1.0, 2.0).astype(jnp.float32)[:, None]
    return jnp.concatenate(
        [weights * jnp.cos(phase_angle), -weights * jnp.sin(phase_angle)], axis=0
    )


def row_tables(row_ids, total_rows):
    orders = jnp.arange(2 * MODES, dtype=jnp.int32)
    wave_numbers = jnp.where(orders < MODES, orders, total_rows - 2 * MODES + orders)
    phase_angle = (
        2.0
        * math.pi
        / total_rows
        * (wave_numbers[:, None] * row_ids[None, :] % total_rows).astype(jnp.float32)
    )
    return (jnp.cos(phase_angle), jnp.sin(phase_angle))


def rows_forward(part_real, part_imag, cosine_table, sine_table):
    highest = lax.Precision.HIGHEST
    real_part = jnp.einsum("jy,yhl->hjl", cosine_table, part_real, precision=highest) + jnp.einsum(
        "jy,yhl->hjl", sine_table, part_imag, precision=highest
    )
    imag_part = jnp.einsum("jy,yhl->hjl", cosine_table, part_imag, precision=highest) - jnp.einsum(
        "jy,yhl->hjl", sine_table, part_real, precision=highest
    )
    return (real_part, imag_part)


def rows_inverse(mixed_real, mixed_imag, cosine_table, sine_table):
    highest = lax.Precision.HIGHEST
    rows_real = jnp.einsum("jy,ojl->yol", cosine_table, mixed_real, precision=highest) - jnp.einsum(
        "jy,ojl->yol", sine_table, mixed_imag, precision=highest
    )
    rows_imag = jnp.einsum("jy,ojl->yol", sine_table, mixed_real, precision=highest) + jnp.einsum(
        "jy,ojl->yol", cosine_table, mixed_imag, precision=highest
    )
    return jnp.concatenate([rows_real, rows_imag], axis=2)


def mix_modes(spectral, mode_real, mode_imag):
    highest = lax.Precision.HIGHEST
    mixed_real = jnp.einsum(
        "hojl,hjl->ojl", spectral[0], mode_real, precision=highest
    ) - jnp.einsum("hojl,hjl->ojl", spectral[1], mode_imag, precision=highest)
    mixed_imag = jnp.einsum(
        "hojl,hjl->ojl", spectral[0], mode_imag, precision=highest
    ) + jnp.einsum("hojl,hjl->ojl", spectral[1], mode_real, precision=highest)
    return (mixed_real, mixed_imag)


def gelu_slope(pre_act):
    normal_cdf = 0.5 * (1.0 + lax.erf(pre_act * (1.0 / math.sqrt(2.0))))
    density = jnp.exp(-0.5 * pre_act * pre_act) * (1.0 / math.sqrt(2.0 * math.pi))
    return normal_cdf + pre_act * density


def weight_grads(back_real, back_imag, mode_real, mode_imag):
    highest = lax.Precision.HIGHEST
    grad_real = jnp.einsum("ojl,hjl->hojl", back_real, mode_real, precision=highest) + jnp.einsum(
        "ojl,hjl->hojl", back_imag, mode_imag, precision=highest
    )
    grad_imag = jnp.einsum("ojl,hjl->hojl", back_imag, mode_real, precision=highest) - jnp.einsum(
        "ojl,hjl->hojl", back_real, mode_imag, precision=highest
    )
    return jnp.stack([grad_real, grad_imag])


def lift_rows(sample, lift_weight, lift_bias):
    lifted = jnp.einsum("ycx,ch->yhx", sample, lift_weight, preferred_element_type=jnp.float32)
    return (lifted + lift_bias[None, :, None]).astype(jnp.bfloat16)


def gather_along(block, axis):
    count = lax.axis_size(axis)
    index = lax.axis_index(axis)
    gathered = jnp.zeros((count,) + block.shape, block.dtype)
    for shift in range(count):
        if shift == 0:
            piece = block
        else:
            piece = lax.ppermute(block, axis, [(i, (i + shift) % count) for i in range(count)])
        gathered = lax.dynamic_update_index_in_dim(gathered, piece, (index - shift) % count, 0)
    return gathered


def gather_rows(block, axes):
    for axis in reversed(axes):
        block = gather_along(block, axis)
    return block.reshape((-1,) + block.shape[len(axes):])


def pair_sum(values, axis):
    if lax.axis_size(axis) != 2:
        return lax.psum(values, axis)
    other = lax.ppermute(values, axis, [(0, 1), (1, 0)])
    return jax.tree.map(lambda mine, theirs: mine + theirs, values, other)


def group_grads(back_real, back_imag, mode_real, mode_imag, axis):
    count = lax.axis_size(axis)
    index = lax.axis_index(axis)
    block = mode_real.shape[1] // count
    total = None
    for shift in range(count):
        target = (index + shift) % count
        piece = tuple(
            lax.dynamic_slice_in_dim(part, target * block, block, 1)
            for part in (back_real, back_imag, mode_real, mode_imag)
        )
        if shift:
            piece = lax.ppermute(piece, axis, [(i, (i + shift) % count) for i in range(count)])
        term = weight_grads(*piece)
        total = term if total is None else total + term
    return total


def body(
    field,
    counts,
    kappa_rows,
    kappa_cols,
    drift_rows,
    drift_cols,
    assign,
    buffer,
    lift_weight,
    lift_bias,
    point_weight,
    point_bias,
    spectral_weight,
    cotangent,
):
    above_row, below_row = halo_rows(field, ("grp", "mem", "row"))
    row_sums = solve_rows(
        field,
        above_row,
        below_row,
        counts[0],
        kappa_rows,
        drift_rows,
        kappa_cols,
        drift_cols,
    )
    coarse_rows = (row_sums.reshape(C, SW, FACTOR).sum(axis=2) * (1.0 / (FACTOR * FACTOR)))[None]
    coarse_low = coarse_rows.astype(jnp.bfloat16)
    member = lax.axis_index("mem")
    member_rows = buffer.shape[1]
    total_rows = member_rows * lax.axis_size("mem")
    row_ids = member * member_rows + jnp.arange(member_rows, dtype=jnp.int32)
    owners = lax.dynamic_slice_in_dim(assign, member * member_rows, member_rows, 0)
    chosen = (owners == lax.axis_index("grp"))[:, None, None]
    forward_table = column_table()
    every_row = gather_rows(coarse_low[0], ("grp", "mem", "row"))
    fresh_rows = lax.dynamic_slice_in_dim(every_row, member * member_rows, member_rows, 0)
    sample = jnp.where(chosen, fresh_rows, buffer[0])
    hidden = lift_rows(sample, lift_weight, lift_bias)
    column_part = jnp.einsum(
        "yhx,xk->yhk", hidden, forward_table, preferred_element_type=jnp.float32
    )
    norm_scale = 1.0 / math.sqrt(total_rows * SW)
    cosine_table, sine_table = row_tables(row_ids, total_rows)
    part_real, part_imag = rows_forward(
        column_part[:, :, :MODES], column_part[:, :, MODES:], cosine_table, sine_table
    )
    mode_real, mode_imag = pair_sum((part_real * norm_scale, part_imag * norm_scale), "mem")
    mixed_real, mixed_imag = mix_modes(spectral_weight.astype(jnp.float32), mode_real, mode_imag)
    spatial = (
        jnp.einsum(
            "yok,kx->yox",
            rows_inverse(mixed_real, mixed_imag, cosine_table, sine_table),
            inverse_table(),
            precision=lax.Precision.HIGHEST,
        )
        * norm_scale
    )
    pre_act = (
        spatial
        + jnp.einsum("yhx,ho->yox", hidden, point_weight, preferred_element_type=jnp.float32)
        + point_bias[None, :, None]
    )
    layer_rows = jax.nn.gelu(pre_act, approximate=False).astype(jnp.bfloat16)[None]
    back_signal = (cotangent[0].astype(jnp.float32) * gelu_slope(pre_act)).astype(jnp.bfloat16)
    back_part = jnp.einsum(
        "yox,xk->yok", back_signal, forward_table, preferred_element_type=jnp.float32
    )
    back_real, back_imag = rows_forward(
        back_part[:, :, :MODES], back_part[:, :, MODES:], cosine_table, sine_table
    )
    weights_mode = jnp.where(jnp.arange(MODES) == 0, 1.0, 2.0).astype(jnp.float32) * norm_scale
    back_real, back_imag = pair_sum((back_real * weights_mode, back_imag * weights_mode), "mem")
    block_size = HID // lax.axis_size("mem")
    block_real = lax.dynamic_slice_in_dim(mode_real, member * block_size, block_size, 0)
    block_imag = lax.dynamic_slice_in_dim(mode_imag, member * block_size, block_size, 0)
    summed = group_grads(back_real, back_imag, block_real, block_imag, "grp")
    return (coarse_rows, layer_rows, summed / lax.axis_size("grp"))


def solution(mesh):
    in_specs = (
        P(None, ("grp", "mem", "row"), None),
        P(("grp", "mem", "row")),
        P(("grp", "mem", "row")),
        P(),
        P(None, ("grp", "mem", "row")),
        P(),
        P(),
        P("grp", "mem", None, None),
        P(),
        P(),
        P(None, "row"),
        P("row"),
        P(None, None, "row", None, None),
        P("grp", "mem", "row", None),
    )
    out_specs = (
        P(("grp", "mem", "row"), None, None),
        P("grp", "mem", "row", None),
        P(None, "mem", "row", "grp", None),
    )
    return jax.shard_map(body, mesh=mesh, in_specs=in_specs, out_specs=out_specs, check_vma=False)
```

```python
import math

import jax
import jax.numpy as jnp
from jax import lax
from jax.experimental import pallas as pl
from jax.experimental.pallas import tpu as pltpu
from jax.sharding import PartitionSpec as P

C = 4
SW = 1024
FACTOR = 16
HID = 32
MODES = 16


window_time = 0.24


def with_halo(block, sides, width):
    for axis, dim in sides:
        count = lax.axis_size(axis)
        forward = [(i, i + 1) for i in range(count - 1)]
        forward.append((count - 1, 0))
        backward = [(target, source) for source, target in forward]
        low = lax.ppermute(
            lax.slice_in_dim(block, block.shape[dim] - width, None, axis=dim), axis, forward
        )
        high = lax.ppermute(lax.slice_in_dim(block, 0, width, axis=dim), axis, backward)
        block = jnp.concatenate([low, block, high], axis=dim)
    return block


def halo_rows(block, axis):
    count = lax.axis_size(axis)
    forward = [(i, (i + 1) % count) for i in range(count)]
    backward = [((i + 1) % count, i) for i in range(count)]
    above = lax.ppermute(block[:, -1:], axis, forward)
    below = lax.ppermute(block[:, :1], axis, backward)
    return above, below


def slab_solve(
    slab_rows, above_row, below_row, substeps, kappa_row, drift_row, kappa_col, drift_col
):
    diffusion = kappa_row[:, None] * kappa_col[None, :]
    drift_along = drift_row[0][:, None] * drift_col[0][None, :]
    drift_across = drift_row[1][:, None] * drift_col[1][None, :]
    step_size = window_time / substeps.astype(jnp.float32)

    def advance(number, current):
        stacked = jnp.concatenate([above_row, current, below_row], axis=1)
        upper_rows = stacked[:, :-2]
        lower_rows = stacked[:, 2:]
        right_cells = jnp.roll(current, -1, axis=2)
        left_cells = jnp.roll(current, 1, axis=2)
        change = diffusion * (right_cells + left_cells + upper_rows + lower_rows - 4.0 * current)
        change = (
            change
            - 0.5 * drift_along * (right_cells - left_cells)
            - 0.5 * drift_across * (lower_rows - upper_rows)
        )
        return current + step_size * change

    return lax.fori_loop(jnp.zeros((), jnp.int32), substeps, advance, slab_rows)


CHUNK = 512
UNROLL = 4


def solve_kernel(
    step_ref, count_ref, field_ref, above_ref, below_ref, coef_ref, out_ref, first_ref, second_ref
):
    tracers, rows, width = field_ref.shape
    chunks = width // CHUNK

    def chunk_at(index):
        return pl.ds(pl.multiple_of(index * CHUNK, CHUNK), CHUNK)

    def prepare(index, carry):
        cols = chunk_at(index)
        for tracer in range(tracers):
            first_ref[tracer, :, cols] = field_ref[tracer, :, cols].astype(jnp.float32)
        return carry

    lax.fori_loop(0, chunks, prepare, 0)
    step = step_ref[0]
    row_ids = lax.broadcasted_iota(jnp.int32, (rows, CHUNK), 0)

    def sweep(source_ref, target_ref):
        def update(index, inner):
            tracer = index // chunks
            column = index % chunks
            cols = chunk_at(column)
            before = pl.ds(pl.multiple_of(((column * CHUNK - 128) % width), 128), 128)
            after = pl.ds(pl.multiple_of((((column + 1) * CHUNK) % width), 128), 128)
            current = source_ref[tracer, :, cols]
            extended = jnp.concatenate(
                [source_ref[tracer, :, before], current, source_ref[tracer, :, after]], axis=1
            )
            span = CHUNK + 256
            right_cells = pltpu.roll(extended, span - 1, 1)[:, 128 : 128 + CHUNK]
            left_cells = pltpu.roll(extended, 1, 1)[:, 128 : 128 + CHUNK]
            upper_rows = jnp.where(
                row_ids == 0, above_ref[tracer, :, cols], pltpu.roll(current, 1, 0)
            )
            lower_rows = jnp.where(
                row_ids == rows - 1, below_ref[tracer, :, cols], pltpu.roll(current, rows - 1, 0)
            )
            change = coef_ref[0, :, cols] * (
                right_cells + left_cells + upper_rows + lower_rows - 4.0 * current
            )
            change = (
                change
                - coef_ref[1, :, cols] * (right_cells - left_cells)
                - coef_ref[2, :, cols] * (lower_rows - upper_rows)
            )
            target_ref[tracer, :, cols] = current + step * change
            return inner

        lax.fori_loop(0, tracers * chunks, update, 0, unroll=UNROLL)

    def two_steps(number, carry):
        sweep(first_ref, second_ref)
        sweep(second_ref, first_ref)
        return carry

    total = count_ref[0]
    lax.fori_loop(0, total // 2, two_steps, 0)

    def collect(final_ref):
        def store(index, carry):
            tracer = index // chunks
            cols = chunk_at(index % chunks)
            out_ref[tracer, :, cols] = jnp.sum(final_ref[tracer, :, cols], axis=0, keepdims=True)
            return carry

        lax.fori_loop(0, tracers * chunks, store, 0)

    @pl.when(total % 2 == 1)
    def _():
        sweep(first_ref, second_ref)
        collect(second_ref)

    @pl.when(total % 2 == 0)
    def _():
        collect(first_ref)


def solve_rows(field, above_row, below_row, substeps, kappa_row, drift_row, kappa_col, drift_col):
    tracers, rows, width = field.shape
    step = (window_time / substeps.astype(jnp.float32)).reshape(1)
    kappa_col = kappa_col.astype(jnp.float32)
    drift_col = drift_col.astype(jnp.float32)
    coefficients = jnp.stack(
        [
            kappa_row[:, None] * kappa_col[None, :],
            0.5 * (drift_row[0][:, None] * drift_col[0][None, :]),
            0.5 * (drift_row[1][:, None] * drift_col[1][None, :]),
        ]
    )
    smem = pl.BlockSpec(memory_space=pltpu.SMEM)
    vmem = pl.BlockSpec(memory_space=pltpu.VMEM)
    return pl.pallas_call(
        solve_kernel,
        out_shape=jax.ShapeDtypeStruct((tracers, 1, width), jnp.float32),
        in_specs=[smem, smem] + [vmem] * 4,
        out_specs=vmem,
        scratch_shapes=[
            pltpu.VMEM((tracers, rows, width), jnp.float32),
            pltpu.VMEM((tracers, rows, width), jnp.float32),
        ],
        compiler_params=pltpu.CompilerParams(vmem_limit_bytes=56 * 1024 * 1024),
    )(
        step,
        substeps.reshape(1),
        field,
        above_row.astype(jnp.float32),
        below_row.astype(jnp.float32),
        coefficients,
    )


def coarsen(stepped):
    return stepped.reshape(C, FACTOR, SW, FACTOR).mean(axis=(1, 3))


def column_table():
    columns = jnp.arange(SW, dtype=jnp.int32)
    orders = jnp.arange(MODES, dtype=jnp.int32)
    phase_angle = 2.0 * math.pi / SW * (columns[:, None] * orders[None, :] % SW).astype(jnp.float32)
    return jnp.concatenate([jnp.cos(phase_angle), -jnp.sin(phase_angle)], axis=1).astype(
        jnp.bfloat16
    )


def inverse_table():
    columns = jnp.arange(SW, dtype=jnp.int32)
    orders = jnp.arange(MODES, dtype=jnp.int32)
    phase_angle = 2.0 * math.pi / SW * (orders[:, None] * columns[None, :] % SW).astype(jnp.float32)
    weights = jnp.where(orders == 0, 1.0, 2.0).astype(jnp.float32)[:, None]
    return jnp.concatenate(
        [weights * jnp.cos(phase_angle), -weights * jnp.sin(phase_angle)], axis=0
    )


def row_tables(row_ids, total_rows):
    orders = jnp.arange(2 * MODES, dtype=jnp.int32)
    wave_numbers = jnp.where(orders < MODES, orders, total_rows - 2 * MODES + orders)
    phase_angle = (
        2.0
        * math.pi
        / total_rows
        * (wave_numbers[:, None] * row_ids[None, :] % total_rows).astype(jnp.float32)
    )
    return (jnp.cos(phase_angle), jnp.sin(phase_angle))


def rows_forward(part_real, part_imag, cosine_table, sine_table):
    highest = lax.Precision.HIGHEST
    real_part = jnp.einsum("jy,yhl->hjl", cosine_table, part_real, precision=highest) + jnp.einsum(
        "jy,yhl->hjl", sine_table, part_imag, precision=highest
    )
    imag_part = jnp.einsum("jy,yhl->hjl", cosine_table, part_imag, precision=highest) - jnp.einsum(
        "jy,yhl->hjl", sine_table, part_real, precision=highest
    )
    return (real_part, imag_part)


def rows_inverse(mixed_real, mixed_imag, cosine_table, sine_table):
    highest = lax.Precision.HIGHEST
    rows_real = jnp.einsum("jy,ojl->yol", cosine_table, mixed_real, precision=highest) - jnp.einsum(
        "jy,ojl->yol", sine_table, mixed_imag, precision=highest
    )
    rows_imag = jnp.einsum("jy,ojl->yol", sine_table, mixed_real, precision=highest) + jnp.einsum(
        "jy,ojl->yol", cosine_table, mixed_imag, precision=highest
    )
    return jnp.concatenate([rows_real, rows_imag], axis=2)


def mix_modes(spectral, mode_real, mode_imag):
    highest = lax.Precision.HIGHEST
    mixed_real = jnp.einsum(
        "hojl,hjl->ojl", spectral[0], mode_real, precision=highest
    ) - jnp.einsum("hojl,hjl->ojl", spectral[1], mode_imag, precision=highest)
    mixed_imag = jnp.einsum(
        "hojl,hjl->ojl", spectral[0], mode_imag, precision=highest
    ) + jnp.einsum("hojl,hjl->ojl", spectral[1], mode_real, precision=highest)
    return (mixed_real, mixed_imag)


def gelu_slope(pre_act):
    normal_cdf = 0.5 * (1.0 + lax.erf(pre_act * (1.0 / math.sqrt(2.0))))
    density = jnp.exp(-0.5 * pre_act * pre_act) * (1.0 / math.sqrt(2.0 * math.pi))
    return normal_cdf + pre_act * density


def weight_grads(back_real, back_imag, mode_real, mode_imag):
    highest = lax.Precision.HIGHEST
    grad_real = jnp.einsum("ojl,hjl->hojl", back_real, mode_real, precision=highest) + jnp.einsum(
        "ojl,hjl->hojl", back_imag, mode_imag, precision=highest
    )
    grad_imag = jnp.einsum("ojl,hjl->hojl", back_imag, mode_real, precision=highest) - jnp.einsum(
        "ojl,hjl->hojl", back_real, mode_imag, precision=highest
    )
    return jnp.stack([grad_real, grad_imag])


def lift_rows(sample, lift_weight, lift_bias):
    lifted = jnp.einsum("ycx,ch->yhx", sample, lift_weight, preferred_element_type=jnp.float32)
    return (lifted + lift_bias[None, :, None]).astype(jnp.bfloat16)


def gather_along(block, axis):
    count = lax.axis_size(axis)
    index = lax.axis_index(axis)
    gathered = jnp.zeros((count,) + block.shape, block.dtype)
    for shift in range(count):
        if shift == 0:
            piece = block
        else:
            piece = lax.ppermute(block, axis, [(i, (i + shift) % count) for i in range(count)])
        gathered = lax.dynamic_update_index_in_dim(gathered, piece, (index - shift) % count, 0)
    return gathered


def gather_rows(block, axes):
    for axis in reversed(axes):
        block = gather_along(block, axis)
    return block.reshape((-1,) + block.shape[len(axes):])


def pair_sum(values, axis):
    if lax.axis_size(axis) != 2:
        return lax.psum(values, axis)
    other = lax.ppermute(values, axis, [(0, 1), (1, 0)])
    return jax.tree.map(lambda mine, theirs: mine + theirs, values, other)


def group_grads(back_real, back_imag, mode_real, mode_imag, axis):
    count = lax.axis_size(axis)
    index = lax.axis_index(axis)
    block = mode_real.shape[1] // count
    total = None
    for shift in range(count):
        target = (index + shift) % count
        piece = tuple(
            lax.dynamic_slice_in_dim(part, target * block, block, 1)
            for part in (back_real, back_imag, mode_real, mode_imag)
        )
        if shift:
            piece = lax.ppermute(piece, axis, [(i, (i + shift) % count) for i in range(count)])
        term = weight_grads(*piece)
        total = term if total is None else total + term
    return total


def body(
    field,
    counts,
    kappa_rows,
    kappa_cols,
    drift_rows,
    drift_cols,
    assign,
    buffer,
    lift_weight,
    lift_bias,
    point_weight,
    point_bias,
    spectral_weight,
    cotangent,
):
    above_row, below_row = halo_rows(field, ("grp", "mem", "row"))
    row_sums = solve_rows(
        field,
        above_row,
        below_row,
        counts[0],
        kappa_rows,
        drift_rows,
        kappa_cols,
        drift_cols,
    )
    coarse_rows = (row_sums.reshape(C, SW, FACTOR).sum(axis=2) * (1.0 / (FACTOR * FACTOR)))[None]
    coarse_low = coarse_rows.astype(jnp.bfloat16)
    member = lax.axis_index("mem")
    member_rows = buffer.shape[1]
    total_rows = member_rows * lax.axis_size("mem")
    row_ids = member * member_rows + jnp.arange(member_rows, dtype=jnp.int32)
    owners = lax.dynamic_slice_in_dim(assign, member * member_rows, member_rows, 0)
    chosen = (owners == lax.axis_index("grp"))[:, None, None]
    forward_table = column_table()
    every_row = gather_rows(coarse_low[0], ("grp", "mem", "row"))
    fresh_rows = lax.dynamic_slice_in_dim(every_row, member * member_rows, member_rows, 0)
    sample = jnp.where(chosen, fresh_rows, buffer[0])
    hidden = lift_rows(sample, lift_weight, lift_bias)
    column_part = jnp.einsum(
        "yhx,xk->yhk", hidden, forward_table, preferred_element_type=jnp.float32
    )
    norm_scale = 1.0 / math.sqrt(total_rows * SW)
    cosine_table, sine_table = row_tables(row_ids, total_rows)
    part_real, part_imag = rows_forward(
        column_part[:, :, :MODES], column_part[:, :, MODES:], cosine_table, sine_table
    )
    mode_real, mode_imag = pair_sum((part_real * norm_scale, part_imag * norm_scale), "mem")
    mixed_real, mixed_imag = mix_modes(spectral_weight.astype(jnp.float32), mode_real, mode_imag)
    spatial = (
        jnp.einsum(
            "yok,kx->yox",
            rows_inverse(mixed_real, mixed_imag, cosine_table, sine_table),
            inverse_table(),
            precision=lax.Precision.HIGHEST,
        )
        * norm_scale
    )
    pre_act = (
        spatial
        + jnp.einsum("yhx,ho->yox", hidden, point_weight, preferred_element_type=jnp.float32)
        + point_bias[None, :, None]
    )
    layer_rows = jax.nn.gelu(pre_act, approximate=False).astype(jnp.bfloat16)[None]
    back_signal = (cotangent[0].astype(jnp.float32) * gelu_slope(pre_act)).astype(jnp.bfloat16)
    back_part = jnp.einsum(
        "yox,xk->yok", back_signal, forward_table, preferred_element_type=jnp.float32
    )
    back_real, back_imag = rows_forward(
        back_part[:, :, :MODES], back_part[:, :, MODES:], cosine_table, sine_table
    )
    weights_mode = jnp.where(jnp.arange(MODES) == 0, 1.0, 2.0).astype(jnp.float32) * norm_scale
    back_real, back_imag = pair_sum((back_real * weights_mode, back_imag * weights_mode), "mem")
    block_size = HID // lax.axis_size("mem")
    block_real = lax.dynamic_slice_in_dim(mode_real, member * block_size, block_size, 0)
    block_imag = lax.dynamic_slice_in_dim(mode_imag, member * block_size, block_size, 0)
    summed = group_grads(back_real, back_imag, block_real, block_imag, "grp")
    return (coarse_rows, layer_rows, summed / lax.axis_size("grp"))


def solution(mesh):
    in_specs = (
        P(None, ("grp", "mem", "row"), None),
        P(("grp", "mem", "row")),
        P(("grp", "mem", "row")),
        P(),
        P(None, ("grp", "mem", "row")),
        P(),
        P(),
        P("grp", "mem", None, None),
        P(),
        P(),
        P(None, "row"),
        P("row"),
        P(None, None, "row", None, None),
        P("grp", "mem", "row", None),
    )
    out_specs = (
        P(("grp", "mem", "row"), None, None),
        P("grp", "mem", "row", None),
        P(None, "mem", "row", "grp", None),
    )
    return jax.shard_map(body, mesh=mesh, in_specs=in_specs, out_specs=out_specs, check_vma=False)
```

```python
import math

import jax
import jax.numpy as jnp
from jax import lax
from jax.experimental import pallas as pl
from jax.experimental.pallas import tpu as pltpu
from jax.sharding import PartitionSpec as P

C = 4
SW = 1024
FACTOR = 16
HID = 32
MODES = 16


window_time = 0.24


def with_halo(block, sides, width):
    for axis, dim in sides:
        count = lax.axis_size(axis)
        forward = [(i, i + 1) for i in range(count - 1)]
        forward.append((count - 1, 0))
        backward = [(target, source) for source, target in forward]
        low = lax.ppermute(
            lax.slice_in_dim(block, block.shape[dim] - width, None, axis=dim), axis, forward
        )
        high = lax.ppermute(lax.slice_in_dim(block, 0, width, axis=dim), axis, backward)
        block = jnp.concatenate([low, block, high], axis=dim)
    return block


def halo_rows(block, axis):
    count = lax.axis_size(axis)
    forward = [(i, (i + 1) % count) for i in range(count)]
    backward = [((i + 1) % count, i) for i in range(count)]
    above = lax.ppermute(block[:, -1:], axis, forward)
    below = lax.ppermute(block[:, :1], axis, backward)
    return above, below


def slab_solve(
    slab_rows, above_row, below_row, substeps, kappa_row, drift_row, kappa_col, drift_col
):
    diffusion = kappa_row[:, None] * kappa_col[None, :]
    drift_along = drift_row[0][:, None] * drift_col[0][None, :]
    drift_across = drift_row[1][:, None] * drift_col[1][None, :]
    step_size = window_time / substeps.astype(jnp.float32)

    def advance(number, current):
        stacked = jnp.concatenate([above_row, current, below_row], axis=1)
        upper_rows = stacked[:, :-2]
        lower_rows = stacked[:, 2:]
        right_cells = jnp.roll(current, -1, axis=2)
        left_cells = jnp.roll(current, 1, axis=2)
        change = diffusion * (right_cells + left_cells + upper_rows + lower_rows - 4.0 * current)
        change = (
            change
            - 0.5 * drift_along * (right_cells - left_cells)
            - 0.5 * drift_across * (lower_rows - upper_rows)
        )
        return current + step_size * change

    return lax.fori_loop(jnp.zeros((), jnp.int32), substeps, advance, slab_rows)


CHUNK = 512
UNROLL = 4


def solve_kernel(
    step_ref, count_ref, field_ref, above_ref, below_ref, coef_ref, out_ref, first_ref, second_ref
):
    tracers, rows, width = field_ref.shape
    chunks = width // CHUNK

    def chunk_at(index):
        return pl.ds(pl.multiple_of(index * CHUNK, CHUNK), CHUNK)

    def prepare(index, carry):
        cols = chunk_at(index)
        for tracer in range(tracers):
            first_ref[tracer, :, cols] = field_ref[tracer, :, cols].astype(jnp.float32)
        return carry

    lax.fori_loop(0, chunks, prepare, 0)
    step = step_ref[0]
    row_ids = lax.broadcasted_iota(jnp.int32, (rows, CHUNK), 0)

    def sweep(source_ref, target_ref):
        def update(index, inner):
            tracer = index // chunks
            column = index % chunks
            cols = chunk_at(column)
            before = pl.ds(pl.multiple_of(((column * CHUNK - 128) % width), 128), 128)
            after = pl.ds(pl.multiple_of((((column + 1) * CHUNK) % width), 128), 128)
            current = source_ref[tracer, :, cols]
            extended = jnp.concatenate(
                [source_ref[tracer, :, before], current, source_ref[tracer, :, after]], axis=1
            )
            span = CHUNK + 256
            right_cells = pltpu.roll(extended, span - 1, 1)[:, 128 : 128 + CHUNK]
            left_cells = pltpu.roll(extended, 1, 1)[:, 128 : 128 + CHUNK]
            upper_rows = jnp.where(
                row_ids == 0, above_ref[tracer, :, cols], pltpu.roll(current, 1, 0)
            )
            lower_rows = jnp.where(
                row_ids == rows - 1, below_ref[tracer, :, cols], pltpu.roll(current, rows - 1, 0)
            )
            change = coef_ref[0, :, cols] * (
                right_cells + left_cells + upper_rows + lower_rows - 4.0 * current
            )
            change = (
                change
                - coef_ref[1, :, cols] * (right_cells - left_cells)
                - coef_ref[2, :, cols] * (lower_rows - upper_rows)
            )
            target_ref[tracer, :, cols] = current + step * change
            return inner

        lax.fori_loop(0, tracers * chunks, update, 0, unroll=UNROLL)

    def two_steps(number, carry):
        sweep(first_ref, second_ref)
        sweep(second_ref, first_ref)
        return carry

    total = count_ref[0]
    lax.fori_loop(0, total // 2, two_steps, 0)

    def collect(final_ref):
        def store(index, carry):
            tracer = index // chunks
            cols = chunk_at(index % chunks)
            out_ref[tracer, :, cols] = jnp.sum(final_ref[tracer, :, cols], axis=0, keepdims=True)
            return carry

        lax.fori_loop(0, tracers * chunks, store, 0)

    @pl.when(total % 2 == 1)
    def _():
        sweep(first_ref, second_ref)
        collect(second_ref)

    @pl.when(total % 2 == 0)
    def _():
        collect(first_ref)


def solve_rows(field, above_row, below_row, substeps, kappa_row, drift_row, kappa_col, drift_col):
    tracers, rows, width = field.shape
    step = (window_time / substeps.astype(jnp.float32)).reshape(1)
    kappa_col = kappa_col.astype(jnp.float32)
    drift_col = drift_col.astype(jnp.float32)
    coefficients = jnp.stack(
        [
            kappa_row[:, None] * kappa_col[None, :],
            0.5 * (drift_row[0][:, None] * drift_col[0][None, :]),
            0.5 * (drift_row[1][:, None] * drift_col[1][None, :]),
        ]
    )
    smem = pl.BlockSpec(memory_space=pltpu.SMEM)
    vmem = pl.BlockSpec(memory_space=pltpu.VMEM)
    return pl.pallas_call(
        solve_kernel,
        out_shape=jax.ShapeDtypeStruct((tracers, 1, width), jnp.float32),
        in_specs=[smem, smem] + [vmem] * 4,
        out_specs=vmem,
        scratch_shapes=[
            pltpu.VMEM((tracers, rows, width), jnp.float32),
            pltpu.VMEM((tracers, rows, width), jnp.float32),
        ],
        compiler_params=pltpu.CompilerParams(vmem_limit_bytes=56 * 1024 * 1024),
    )(
        step,
        substeps.reshape(1),
        field,
        above_row.astype(jnp.float32),
        below_row.astype(jnp.float32),
        coefficients,
    )


def coarsen(stepped):
    return stepped.reshape(C, FACTOR, SW, FACTOR).mean(axis=(1, 3))


def column_table():
    columns = jnp.arange(SW, dtype=jnp.int32)
    orders = jnp.arange(MODES, dtype=jnp.int32)
    phase_angle = 2.0 * math.pi / SW * (columns[:, None] * orders[None, :] % SW).astype(jnp.float32)
    return jnp.concatenate([jnp.cos(phase_angle), -jnp.sin(phase_angle)], axis=1).astype(
        jnp.bfloat16
    )


def inverse_table():
    columns = jnp.arange(SW, dtype=jnp.int32)
    orders = jnp.arange(MODES, dtype=jnp.int32)
    phase_angle = 2.0 * math.pi / SW * (orders[:, None] * columns[None, :] % SW).astype(jnp.float32)
    weights = jnp.where(orders == 0, 1.0, 2.0).astype(jnp.float32)[:, None]
    return jnp.concatenate(
        [weights * jnp.cos(phase_angle), -weights * jnp.sin(phase_angle)], axis=0
    )


def row_tables(row_ids, total_rows):
    orders = jnp.arange(2 * MODES, dtype=jnp.int32)
    wave_numbers = jnp.where(orders < MODES, orders, total_rows - 2 * MODES + orders)
    phase_angle = (
        2.0
        * math.pi
        / total_rows
        * (wave_numbers[:, None] * row_ids[None, :] % total_rows).astype(jnp.float32)
    )
    return (jnp.cos(phase_angle), jnp.sin(phase_angle))


def rows_forward(part_real, part_imag, cosine_table, sine_table):
    highest = lax.Precision.HIGHEST
    real_part = jnp.einsum("jy,yhl->hjl", cosine_table, part_real, precision=highest) + jnp.einsum(
        "jy,yhl->hjl", sine_table, part_imag, precision=highest
    )
    imag_part = jnp.einsum("jy,yhl->hjl", cosine_table, part_imag, precision=highest) - jnp.einsum(
        "jy,yhl->hjl", sine_table, part_real, precision=highest
    )
    return (real_part, imag_part)


def rows_inverse(mixed_real, mixed_imag, cosine_table, sine_table):
    highest = lax.Precision.HIGHEST
    rows_real = jnp.einsum("jy,ojl->yol", cosine_table, mixed_real, precision=highest) - jnp.einsum(
        "jy,ojl->yol", sine_table, mixed_imag, precision=highest
    )
    rows_imag = jnp.einsum("jy,ojl->yol", sine_table, mixed_real, precision=highest) + jnp.einsum(
        "jy,ojl->yol", cosine_table, mixed_imag, precision=highest
    )
    return jnp.concatenate([rows_real, rows_imag], axis=2)


def mix_modes(spectral, mode_real, mode_imag):
    real_weight, imag_weight = spectral[0], spectral[1]
    mode_real = mode_real[:, None]
    mode_imag = mode_imag[:, None]
    mixed_real = jnp.sum(real_weight * mode_real - imag_weight * mode_imag, axis=0)
    mixed_imag = jnp.sum(real_weight * mode_imag + imag_weight * mode_real, axis=0)
    return (mixed_real, mixed_imag)


def gelu_slope(pre_act):
    normal_cdf = 0.5 * (1.0 + lax.erf(pre_act * (1.0 / math.sqrt(2.0))))
    density = jnp.exp(-0.5 * pre_act * pre_act) * (1.0 / math.sqrt(2.0 * math.pi))
    return normal_cdf + pre_act * density


def weight_grads(back_real, back_imag, mode_real, mode_imag):
    highest = lax.Precision.HIGHEST
    grad_real = jnp.einsum("ojl,hjl->hojl", back_real, mode_real, precision=highest) + jnp.einsum(
        "ojl,hjl->hojl", back_imag, mode_imag, precision=highest
    )
    grad_imag = jnp.einsum("ojl,hjl->hojl", back_imag, mode_real, precision=highest) - jnp.einsum(
        "ojl,hjl->hojl", back_real, mode_imag, precision=highest
    )
    return jnp.stack([grad_real, grad_imag])


def lift_rows(sample, lift_weight, lift_bias):
    lifted = jnp.einsum("ycx,ch->yhx", sample, lift_weight, preferred_element_type=jnp.float32)
    return (lifted + lift_bias[None, :, None]).astype(jnp.bfloat16)


def gather_along(block, axis):
    count = lax.axis_size(axis)
    index = lax.axis_index(axis)
    gathered = jnp.zeros((count,) + block.shape, block.dtype)
    for shift in range(count):
        if shift == 0:
            piece = block
        else:
            piece = lax.ppermute(block, axis, [(i, (i + shift) % count) for i in range(count)])
        gathered = lax.dynamic_update_index_in_dim(gathered, piece, (index - shift) % count, 0)
    return gathered


def gather_rows(block, axes):
    for axis in reversed(axes):
        block = gather_along(block, axis)
    return block.reshape((-1,) + block.shape[len(axes):])


def packed_ppermute(parts, axis, perm):
    flat = jnp.concatenate([part.reshape(-1) for part in parts])
    flat = lax.ppermute(flat, axis, perm)
    result = []
    offset = 0
    for part in parts:
        result.append(flat[offset : offset + part.size].reshape(part.shape))
        offset += part.size
    return tuple(result)


def pair_sum(values, axis):
    if lax.axis_size(axis) != 2:
        return lax.psum(values, axis)
    other = packed_ppermute(values, axis, [(0, 1), (1, 0)])
    return tuple(mine + theirs for mine, theirs in zip(values, other))


def group_grads(back_real, back_imag, mode_real, mode_imag, axis):
    count = lax.axis_size(axis)
    index = lax.axis_index(axis)
    block = mode_real.shape[1] // count
    total = None
    for shift in range(count):
        target = (index + shift) % count
        piece = tuple(
            lax.dynamic_slice_in_dim(part, target * block, block, 1)
            for part in (back_real, back_imag, mode_real, mode_imag)
        )
        if shift:
            piece = packed_ppermute(piece, axis, [(i, (i + shift) % count) for i in range(count)])
        term = weight_grads(*piece)
        total = term if total is None else total + term
    return total


def body(
    field,
    counts,
    kappa_rows,
    kappa_cols,
    drift_rows,
    drift_cols,
    assign,
    buffer,
    lift_weight,
    lift_bias,
    point_weight,
    point_bias,
    spectral_weight,
    cotangent,
):
    above_row, below_row = halo_rows(field, ("grp", "mem", "row"))
    row_sums = solve_rows(
        field,
        above_row,
        below_row,
        counts[0],
        kappa_rows,
        drift_rows,
        kappa_cols,
        drift_cols,
    )
    coarse_rows = (row_sums.reshape(C, SW, FACTOR).sum(axis=2) * (1.0 / (FACTOR * FACTOR)))[None]
    coarse_low = coarse_rows.astype(jnp.bfloat16)
    member = lax.axis_index("mem")
    member_rows = buffer.shape[1]
    total_rows = member_rows * lax.axis_size("mem")
    row_ids = member * member_rows + jnp.arange(member_rows, dtype=jnp.int32)
    owners = lax.dynamic_slice_in_dim(assign, member * member_rows, member_rows, 0)
    chosen = (owners == lax.axis_index("grp"))[:, None, None]
    forward_table = column_table()
    every_row = gather_rows(coarse_low[0], ("grp", "mem", "row"))
    fresh_rows = lax.dynamic_slice_in_dim(every_row, member * member_rows, member_rows, 0)
    sample = jnp.where(chosen, fresh_rows, buffer[0])
    hidden = lift_rows(sample, lift_weight, lift_bias)
    column_part = jnp.einsum(
        "yhx,xk->yhk", hidden, forward_table, preferred_element_type=jnp.float32
    )
    norm_scale = 1.0 / math.sqrt(total_rows * SW)
    cosine_table, sine_table = row_tables(row_ids, total_rows)
    part_real, part_imag = rows_forward(
        column_part[:, :, :MODES], column_part[:, :, MODES:], cosine_table, sine_table
    )
    mode_real, mode_imag = pair_sum((part_real * norm_scale, part_imag * norm_scale), "mem")
    mixed_real, mixed_imag = mix_modes(spectral_weight.astype(jnp.float32), mode_real, mode_imag)
    spatial = (
        jnp.einsum(
            "yok,kx->yox",
            rows_inverse(mixed_real, mixed_imag, cosine_table, sine_table),
            inverse_table(),
            precision=lax.Precision.HIGHEST,
        )
        * norm_scale
    )
    pre_act = (
        spatial
        + jnp.einsum("yhx,ho->yox", hidden, point_weight, preferred_element_type=jnp.float32)
        + point_bias[None, :, None]
    )
    layer_rows = jax.nn.gelu(pre_act, approximate=False).astype(jnp.bfloat16)[None]
    back_signal = (cotangent[0].astype(jnp.float32) * gelu_slope(pre_act)).astype(jnp.bfloat16)
    back_part = jnp.einsum(
        "yox,xk->yok", back_signal, forward_table, preferred_element_type=jnp.float32
    )
    back_real, back_imag = rows_forward(
        back_part[:, :, :MODES], back_part[:, :, MODES:], cosine_table, sine_table
    )
    weights_mode = jnp.where(jnp.arange(MODES) == 0, 1.0, 2.0).astype(jnp.float32) * norm_scale
    back_real, back_imag = pair_sum((back_real * weights_mode, back_imag * weights_mode), "mem")
    block_size = HID // lax.axis_size("mem")
    block_real = lax.dynamic_slice_in_dim(mode_real, member * block_size, block_size, 0)
    block_imag = lax.dynamic_slice_in_dim(mode_imag, member * block_size, block_size, 0)
    summed = group_grads(back_real, back_imag, block_real, block_imag, "grp")
    return (coarse_rows, layer_rows, summed / lax.axis_size("grp"))


def solution(mesh):
    in_specs = (
        P(None, ("grp", "mem", "row"), None),
        P(("grp", "mem", "row")),
        P(("grp", "mem", "row")),
        P(),
        P(None, ("grp", "mem", "row")),
        P(),
        P(),
        P("grp", "mem", None, None),
        P(),
        P(),
        P(None, "row"),
        P("row"),
        P(None, None, "row", None, None),
        P("grp", "mem", "row", None),
    )
    out_specs = (
        P(("grp", "mem", "row"), None, None),
        P("grp", "mem", "row", None),
        P(None, "mem", "row", "grp", None),
    )
    return jax.shard_map(body, mesh=mesh, in_specs=in_specs, out_specs=out_specs, check_vma=False)
```

```python
import math

import jax
import jax.numpy as jnp
from jax import lax
from jax.experimental import pallas as pl
from jax.experimental.pallas import tpu as pltpu
from jax.sharding import PartitionSpec as P

C = 4
SW = 1024
FACTOR = 16
HID = 32
MODES = 16


window_time = 0.24


def with_halo(block, sides, width):
    for axis, dim in sides:
        count = lax.axis_size(axis)
        forward = [(i, i + 1) for i in range(count - 1)]
        forward.append((count - 1, 0))
        backward = [(target, source) for source, target in forward]
        low = lax.ppermute(
            lax.slice_in_dim(block, block.shape[dim] - width, None, axis=dim), axis, forward
        )
        high = lax.ppermute(lax.slice_in_dim(block, 0, width, axis=dim), axis, backward)
        block = jnp.concatenate([low, block, high], axis=dim)
    return block


def halo_rows(block, axis):
    count = lax.axis_size(axis)
    forward = [(i, (i + 1) % count) for i in range(count)]
    backward = [((i + 1) % count, i) for i in range(count)]
    above = lax.ppermute(block[:, -1:], axis, forward)
    below = lax.ppermute(block[:, :1], axis, backward)
    return above, below


def slab_solve(
    slab_rows, above_row, below_row, substeps, kappa_row, drift_row, kappa_col, drift_col
):
    diffusion = kappa_row[:, None] * kappa_col[None, :]
    drift_along = drift_row[0][:, None] * drift_col[0][None, :]
    drift_across = drift_row[1][:, None] * drift_col[1][None, :]
    step_size = window_time / substeps.astype(jnp.float32)

    def advance(number, current):
        stacked = jnp.concatenate([above_row, current, below_row], axis=1)
        upper_rows = stacked[:, :-2]
        lower_rows = stacked[:, 2:]
        right_cells = jnp.roll(current, -1, axis=2)
        left_cells = jnp.roll(current, 1, axis=2)
        change = diffusion * (right_cells + left_cells + upper_rows + lower_rows - 4.0 * current)
        change = (
            change
            - 0.5 * drift_along * (right_cells - left_cells)
            - 0.5 * drift_across * (lower_rows - upper_rows)
        )
        return current + step_size * change

    return lax.fori_loop(jnp.zeros((), jnp.int32), substeps, advance, slab_rows)


CHUNK = 256
UNROLL = 2


def solve_kernel(
    step_ref, count_ref, field_ref, above_ref, below_ref, coef_ref, out_ref, first_ref, second_ref
):
    tracers, rows, width = field_ref.shape
    chunks = width // CHUNK

    def chunk_at(index):
        return pl.ds(pl.multiple_of(index * CHUNK, CHUNK), CHUNK)

    def prepare(index, carry):
        cols = chunk_at(index)
        for tracer in range(tracers):
            first_ref[tracer, :, cols] = field_ref[tracer, :, cols].astype(jnp.float32)
        return carry

    lax.fori_loop(0, chunks, prepare, 0)
    step = step_ref[0]
    row_ids = lax.broadcasted_iota(jnp.int32, (rows, CHUNK), 0)

    def sweep(source_ref, target_ref):
        def update(column, inner):
            cols = chunk_at(column)
            before = pl.ds(pl.multiple_of(((column * CHUNK - 128) % width), 128), 128)
            after = pl.ds(pl.multiple_of((((column + 1) * CHUNK) % width), 128), 128)
            diffusion = coef_ref[0, :, cols]
            along = coef_ref[1, :, cols]
            across = coef_ref[2, :, cols]
            for tracer in range(tracers):
                current = source_ref[tracer, :, cols]
                extended = jnp.concatenate(
                    [source_ref[tracer, :, before], current, source_ref[tracer, :, after]], axis=1
                )
                span = CHUNK + 256
                right_cells = pltpu.roll(extended, span - 1, 1)[:, 128 : 128 + CHUNK]
                left_cells = pltpu.roll(extended, 1, 1)[:, 128 : 128 + CHUNK]
                upper_rows = jnp.where(
                    row_ids == 0, above_ref[tracer, :, cols], pltpu.roll(current, 1, 0)
                )
                lower_rows = jnp.where(
                    row_ids == rows - 1, below_ref[tracer, :, cols], pltpu.roll(current, rows - 1, 0)
                )
                change = diffusion * (
                    right_cells + left_cells + upper_rows + lower_rows - 4.0 * current
                )
                change = (
                    change
                    - along * (right_cells - left_cells)
                    - across * (lower_rows - upper_rows)
                )
                target_ref[tracer, :, cols] = current + step * change
            return inner

        lax.fori_loop(0, chunks, update, 0, unroll=UNROLL)

    def two_steps(number, carry):
        sweep(first_ref, second_ref)
        sweep(second_ref, first_ref)
        return carry

    total = count_ref[0]
    lax.fori_loop(0, total // 2, two_steps, 0)

    def collect(final_ref):
        def store(index, carry):
            tracer = index // chunks
            cols = chunk_at(index % chunks)
            out_ref[tracer, :, cols] = jnp.sum(final_ref[tracer, :, cols], axis=0, keepdims=True)
            return carry

        lax.fori_loop(0, tracers * chunks, store, 0)

    @pl.when(total % 2 == 1)
    def _():
        sweep(first_ref, second_ref)
        collect(second_ref)

    @pl.when(total % 2 == 0)
    def _():
        collect(first_ref)


def solve_rows(field, above_row, below_row, substeps, kappa_row, drift_row, kappa_col, drift_col):
    tracers, rows, width = field.shape
    step = (window_time / substeps.astype(jnp.float32)).reshape(1)
    kappa_col = kappa_col.astype(jnp.float32)
    drift_col = drift_col.astype(jnp.float32)
    coefficients = jnp.stack(
        [
            kappa_row[:, None] * kappa_col[None, :],
            0.5 * (drift_row[0][:, None] * drift_col[0][None, :]),
            0.5 * (drift_row[1][:, None] * drift_col[1][None, :]),
        ]
    )
    smem = pl.BlockSpec(memory_space=pltpu.SMEM)
    vmem = pl.BlockSpec(memory_space=pltpu.VMEM)
    return pl.pallas_call(
        solve_kernel,
        out_shape=jax.ShapeDtypeStruct((tracers, 1, width), jnp.float32),
        in_specs=[smem, smem] + [vmem] * 4,
        out_specs=vmem,
        scratch_shapes=[
            pltpu.VMEM((tracers, rows, width), jnp.float32),
            pltpu.VMEM((tracers, rows, width), jnp.float32),
        ],
        compiler_params=pltpu.CompilerParams(vmem_limit_bytes=56 * 1024 * 1024),
    )(
        step,
        substeps.reshape(1),
        field,
        above_row.astype(jnp.float32),
        below_row.astype(jnp.float32),
        coefficients,
    )


def coarsen(stepped):
    return stepped.reshape(C, FACTOR, SW, FACTOR).mean(axis=(1, 3))


def column_table():
    columns = jnp.arange(SW, dtype=jnp.int32)
    orders = jnp.arange(MODES, dtype=jnp.int32)
    phase_angle = 2.0 * math.pi / SW * (columns[:, None] * orders[None, :] % SW).astype(jnp.float32)
    return jnp.concatenate([jnp.cos(phase_angle), -jnp.sin(phase_angle)], axis=1).astype(
        jnp.bfloat16
    )


def inverse_table():
    columns = jnp.arange(SW, dtype=jnp.int32)
    orders = jnp.arange(MODES, dtype=jnp.int32)
    phase_angle = 2.0 * math.pi / SW * (orders[:, None] * columns[None, :] % SW).astype(jnp.float32)
    weights = jnp.where(orders == 0, 1.0, 2.0).astype(jnp.float32)[:, None]
    return jnp.concatenate(
        [weights * jnp.cos(phase_angle), -weights * jnp.sin(phase_angle)], axis=0
    )


def row_tables(row_ids, total_rows):
    orders = jnp.arange(2 * MODES, dtype=jnp.int32)
    wave_numbers = jnp.where(orders < MODES, orders, total_rows - 2 * MODES + orders)
    phase_angle = (
        2.0
        * math.pi
        / total_rows
        * (wave_numbers[:, None] * row_ids[None, :] % total_rows).astype(jnp.float32)
    )
    return (jnp.cos(phase_angle), jnp.sin(phase_angle))


def rows_forward(part_real, part_imag, cosine_table, sine_table):
    highest = lax.Precision.HIGHEST
    real_part = jnp.einsum("jy,yhl->hjl", cosine_table, part_real, precision=highest) + jnp.einsum(
        "jy,yhl->hjl", sine_table, part_imag, precision=highest
    )
    imag_part = jnp.einsum("jy,yhl->hjl", cosine_table, part_imag, precision=highest) - jnp.einsum(
        "jy,yhl->hjl", sine_table, part_real, precision=highest
    )
    return (real_part, imag_part)


def rows_inverse(mixed_real, mixed_imag, cosine_table, sine_table):
    highest = lax.Precision.HIGHEST
    rows_real = jnp.einsum("jy,ojl->yol", cosine_table, mixed_real, precision=highest) - jnp.einsum(
        "jy,ojl->yol", sine_table, mixed_imag, precision=highest
    )
    rows_imag = jnp.einsum("jy,ojl->yol", sine_table, mixed_real, precision=highest) + jnp.einsum(
        "jy,ojl->yol", cosine_table, mixed_imag, precision=highest
    )
    return jnp.concatenate([rows_real, rows_imag], axis=2)


def mix_modes(spectral, mode_real, mode_imag):
    real_weight, imag_weight = spectral[0], spectral[1]
    mode_real = mode_real[:, None]
    mode_imag = mode_imag[:, None]
    mixed_real = jnp.sum(real_weight * mode_real - imag_weight * mode_imag, axis=0)
    mixed_imag = jnp.sum(real_weight * mode_imag + imag_weight * mode_real, axis=0)
    return (mixed_real, mixed_imag)


def gelu_slope(pre_act):
    normal_cdf = 0.5 * (1.0 + lax.erf(pre_act * (1.0 / math.sqrt(2.0))))
    density = jnp.exp(-0.5 * pre_act * pre_act) * (1.0 / math.sqrt(2.0 * math.pi))
    return normal_cdf + pre_act * density


def weight_grads(back_real, back_imag, mode_real, mode_imag):
    highest = lax.Precision.HIGHEST
    grad_real = jnp.einsum("ojl,hjl->hojl", back_real, mode_real, precision=highest) + jnp.einsum(
        "ojl,hjl->hojl", back_imag, mode_imag, precision=highest
    )
    grad_imag = jnp.einsum("ojl,hjl->hojl", back_imag, mode_real, precision=highest) - jnp.einsum(
        "ojl,hjl->hojl", back_real, mode_imag, precision=highest
    )
    return jnp.stack([grad_real, grad_imag])


def lift_rows(sample, lift_weight, lift_bias):
    lifted = jnp.einsum("ycx,ch->yhx", sample, lift_weight, preferred_element_type=jnp.float32)
    return (lifted + lift_bias[None, :, None]).astype(jnp.bfloat16)


def gather_along(block, axis):
    count = lax.axis_size(axis)
    index = lax.axis_index(axis)
    gathered = jnp.zeros((count,) + block.shape, block.dtype)
    for shift in range(count):
        if shift == 0:
            piece = block
        else:
            piece = lax.ppermute(block, axis, [(i, (i + shift) % count) for i in range(count)])
        gathered = lax.dynamic_update_index_in_dim(gathered, piece, (index - shift) % count, 0)
    return gathered


def gather_rows(block, axes):
    for axis in reversed(axes):
        block = gather_along(block, axis)
    return block.reshape((-1,) + block.shape[len(axes):])


def packed_ppermute(parts, axis, perm):
    flat = jnp.concatenate([part.reshape(-1) for part in parts])
    flat = lax.ppermute(flat, axis, perm)
    result = []
    offset = 0
    for part in parts:
        result.append(flat[offset : offset + part.size].reshape(part.shape))
        offset += part.size
    return tuple(result)


def pair_sum(values, axis):
    if lax.axis_size(axis) != 2:
        return lax.psum(values, axis)
    other = packed_ppermute(values, axis, [(0, 1), (1, 0)])
    return tuple(mine + theirs for mine, theirs in zip(values, other))


def group_grads(back_real, back_imag, mode_real, mode_imag, axis):
    count = lax.axis_size(axis)
    index = lax.axis_index(axis)
    block = mode_real.shape[1] // count
    total = None
    for shift in range(count):
        target = (index + shift) % count
        piece = tuple(
            lax.dynamic_slice_in_dim(part, target * block, block, 1)
            for part in (back_real, back_imag, mode_real, mode_imag)
        )
        if shift:
            piece = packed_ppermute(piece, axis, [(i, (i + shift) % count) for i in range(count)])
        term = weight_grads(*piece)
        total = term if total is None else total + term
    return total


def body(
    field,
    counts,
    kappa_rows,
    kappa_cols,
    drift_rows,
    drift_cols,
    assign,
    buffer,
    lift_weight,
    lift_bias,
    point_weight,
    point_bias,
    spectral_weight,
    cotangent,
):
    above_row, below_row = halo_rows(field, ("grp", "mem", "row"))
    row_sums = solve_rows(
        field,
        above_row,
        below_row,
        counts[0],
        kappa_rows,
        drift_rows,
        kappa_cols,
        drift_cols,
    )
    coarse_rows = (row_sums.reshape(C, SW, FACTOR).sum(axis=2) * (1.0 / (FACTOR * FACTOR)))[None]
    coarse_low = coarse_rows.astype(jnp.bfloat16)
    member = lax.axis_index("mem")
    member_rows = buffer.shape[1]
    total_rows = member_rows * lax.axis_size("mem")
    row_ids = member * member_rows + jnp.arange(member_rows, dtype=jnp.int32)
    owners = lax.dynamic_slice_in_dim(assign, member * member_rows, member_rows, 0)
    chosen = (owners == lax.axis_index("grp"))[:, None, None]
    forward_table = column_table()
    every_row = gather_rows(coarse_low[0], ("grp", "mem", "row"))
    fresh_rows = lax.dynamic_slice_in_dim(every_row, member * member_rows, member_rows, 0)
    sample = jnp.where(chosen, fresh_rows, buffer[0])
    hidden = lift_rows(sample, lift_weight, lift_bias)
    column_part = jnp.einsum(
        "yhx,xk->yhk", hidden, forward_table, preferred_element_type=jnp.float32
    )
    norm_scale = 1.0 / math.sqrt(total_rows * SW)
    cosine_table, sine_table = row_tables(row_ids, total_rows)
    part_real, part_imag = rows_forward(
        column_part[:, :, :MODES], column_part[:, :, MODES:], cosine_table, sine_table
    )
    mode_real, mode_imag = pair_sum((part_real * norm_scale, part_imag * norm_scale), "mem")
    mixed_real, mixed_imag = mix_modes(spectral_weight.astype(jnp.float32), mode_real, mode_imag)
    spatial = (
        jnp.einsum(
            "yok,kx->yox",
            rows_inverse(mixed_real, mixed_imag, cosine_table, sine_table),
            inverse_table(),
            precision=lax.Precision.HIGHEST,
        )
        * norm_scale
    )
    pre_act = (
        spatial
        + jnp.einsum("yhx,ho->yox", hidden, point_weight, preferred_element_type=jnp.float32)
        + point_bias[None, :, None]
    )
    layer_rows = jax.nn.gelu(pre_act, approximate=False).astype(jnp.bfloat16)[None]
    back_signal = (cotangent[0].astype(jnp.float32) * gelu_slope(pre_act)).astype(jnp.bfloat16)
    back_part = jnp.einsum(
        "yox,xk->yok", back_signal, forward_table, preferred_element_type=jnp.float32
    )
    back_real, back_imag = rows_forward(
        back_part[:, :, :MODES], back_part[:, :, MODES:], cosine_table, sine_table
    )
    weights_mode = jnp.where(jnp.arange(MODES) == 0, 1.0, 2.0).astype(jnp.float32) * norm_scale
    back_real, back_imag = pair_sum((back_real * weights_mode, back_imag * weights_mode), "mem")
    block_size = HID // lax.axis_size("mem")
    block_real = lax.dynamic_slice_in_dim(mode_real, member * block_size, block_size, 0)
    block_imag = lax.dynamic_slice_in_dim(mode_imag, member * block_size, block_size, 0)
    summed = group_grads(back_real, back_imag, block_real, block_imag, "grp")
    return (coarse_rows, layer_rows, summed / lax.axis_size("grp"))


def solution(mesh):
    in_specs = (
        P(None, ("grp", "mem", "row"), None),
        P(("grp", "mem", "row")),
        P(("grp", "mem", "row")),
        P(),
        P(None, ("grp", "mem", "row")),
        P(),
        P(),
        P("grp", "mem", None, None),
        P(),
        P(),
        P(None, "row"),
        P("row"),
        P(None, None, "row", None, None),
        P("grp", "mem", "row", None),
    )
    out_specs = (
        P(("grp", "mem", "row"), None, None),
        P("grp", "mem", "row", None),
        P(None, "mem", "row", "grp", None),
    )
    return jax.shard_map(body, mesh=mesh, in_specs=in_specs, out_specs=out_specs, check_vma=False)
```

```python
import math

import jax
import jax.numpy as jnp
from jax import lax
from jax.experimental import pallas as pl
from jax.experimental.pallas import tpu as pltpu
from jax.sharding import PartitionSpec as P

C = 4
SW = 1024
FACTOR = 16
HID = 32
MODES = 16


window_time = 0.24


def with_halo(block, sides, width):
    for axis, dim in sides:
        count = lax.axis_size(axis)
        forward = [(i, i + 1) for i in range(count - 1)]
        forward.append((count - 1, 0))
        backward = [(target, source) for source, target in forward]
        low = lax.ppermute(
            lax.slice_in_dim(block, block.shape[dim] - width, None, axis=dim), axis, forward
        )
        high = lax.ppermute(lax.slice_in_dim(block, 0, width, axis=dim), axis, backward)
        block = jnp.concatenate([low, block, high], axis=dim)
    return block


def halo_rows(block, axis):
    count = lax.axis_size(axis)
    forward = [(i, (i + 1) % count) for i in range(count)]
    backward = [((i + 1) % count, i) for i in range(count)]
    above = lax.ppermute(block[:, -1:], axis, forward)
    below = lax.ppermute(block[:, :1], axis, backward)
    return above, below


def slab_solve(
    slab_rows, above_row, below_row, substeps, kappa_row, drift_row, kappa_col, drift_col
):
    diffusion = kappa_row[:, None] * kappa_col[None, :]
    drift_along = drift_row[0][:, None] * drift_col[0][None, :]
    drift_across = drift_row[1][:, None] * drift_col[1][None, :]
    step_size = window_time / substeps.astype(jnp.float32)

    def advance(number, current):
        stacked = jnp.concatenate([above_row, current, below_row], axis=1)
        upper_rows = stacked[:, :-2]
        lower_rows = stacked[:, 2:]
        right_cells = jnp.roll(current, -1, axis=2)
        left_cells = jnp.roll(current, 1, axis=2)
        change = diffusion * (right_cells + left_cells + upper_rows + lower_rows - 4.0 * current)
        change = (
            change
            - 0.5 * drift_along * (right_cells - left_cells)
            - 0.5 * drift_across * (lower_rows - upper_rows)
        )
        return current + step_size * change

    return lax.fori_loop(jnp.zeros((), jnp.int32), substeps, advance, slab_rows)


CHUNK = 512
UNROLL = 4


def solve_kernel(
    step_ref, count_ref, field_ref, above_ref, below_ref, coef_ref, out_ref, first_ref, second_ref
):
    tracers, rows, width = field_ref.shape
    chunks = width // CHUNK

    def chunk_at(index):
        return pl.ds(pl.multiple_of(index * CHUNK, CHUNK), CHUNK)

    def prepare(index, carry):
        cols = chunk_at(index)
        for tracer in range(tracers):
            first_ref[tracer, :, cols] = field_ref[tracer, :, cols].astype(jnp.float32)
        return carry

    lax.fori_loop(0, chunks, prepare, 0)
    step = step_ref[0]
    row_ids = lax.broadcasted_iota(jnp.int32, (rows, CHUNK), 0)

    def sweep(source_ref, target_ref):
        def update(index, inner):
            tracer = index // chunks
            column = index % chunks
            cols = chunk_at(column)
            before = pl.ds(pl.multiple_of(((column * CHUNK - 128) % width), 128), 128)
            after = pl.ds(pl.multiple_of((((column + 1) * CHUNK) % width), 128), 128)
            current = source_ref[tracer, :, cols]
            extended = jnp.concatenate(
                [source_ref[tracer, :, before], current, source_ref[tracer, :, after]], axis=1
            )
            span = CHUNK + 256
            right_cells = pltpu.roll(extended, span - 1, 1)[:, 128 : 128 + CHUNK]
            left_cells = pltpu.roll(extended, 1, 1)[:, 128 : 128 + CHUNK]
            upper_rows = jnp.where(
                row_ids == 0,
                above_ref[tracer, :, cols].astype(jnp.float32),
                pltpu.roll(current, 1, 0),
            )
            lower_rows = jnp.where(
                row_ids == rows - 1,
                below_ref[tracer, :, cols].astype(jnp.float32),
                pltpu.roll(current, rows - 1, 0),
            )
            change = coef_ref[0, :, cols] * (
                right_cells + left_cells + upper_rows + lower_rows - 4.0 * current
            )
            change = (
                change
                - coef_ref[1, :, cols] * (right_cells - left_cells)
                - coef_ref[2, :, cols] * (lower_rows - upper_rows)
            )
            target_ref[tracer, :, cols] = current + step * change
            return inner

        lax.fori_loop(0, tracers * chunks, update, 0, unroll=UNROLL)

    def two_steps(number, carry):
        sweep(first_ref, second_ref)
        sweep(second_ref, first_ref)
        return carry

    total = count_ref[0]
    lax.fori_loop(0, total // 2, two_steps, 0)

    def collect(final_ref):
        def store(index, carry):
            tracer = index // chunks
            cols = chunk_at(index % chunks)
            out_ref[tracer, :, cols] = jnp.sum(final_ref[tracer, :, cols], axis=0, keepdims=True)
            return carry

        lax.fori_loop(0, tracers * chunks, store, 0)

    @pl.when(total % 2 == 1)
    def _():
        sweep(first_ref, second_ref)
        collect(second_ref)

    @pl.when(total % 2 == 0)
    def _():
        collect(first_ref)


def solve_rows(field, above_row, below_row, substeps, kappa_row, drift_row, kappa_col, drift_col):
    tracers, rows, width = field.shape
    step = (window_time / substeps.astype(jnp.float32)).reshape(1)
    kappa_col = kappa_col.astype(jnp.float32)
    drift_col = drift_col.astype(jnp.float32)
    coefficients = jnp.stack(
        [
            kappa_row[:, None] * kappa_col[None, :],
            0.5 * (drift_row[0][:, None] * drift_col[0][None, :]),
            0.5 * (drift_row[1][:, None] * drift_col[1][None, :]),
        ]
    )
    smem = pl.BlockSpec(memory_space=pltpu.SMEM)
    vmem = pl.BlockSpec(memory_space=pltpu.VMEM)
    return pl.pallas_call(
        solve_kernel,
        out_shape=jax.ShapeDtypeStruct((tracers, 1, width), jnp.float32),
        in_specs=[smem, smem] + [vmem] * 4,
        out_specs=vmem,
        scratch_shapes=[
            pltpu.VMEM((tracers, rows, width), jnp.float32),
            pltpu.VMEM((tracers, rows, width), jnp.float32),
        ],
        compiler_params=pltpu.CompilerParams(vmem_limit_bytes=56 * 1024 * 1024),
    )(
        step,
        substeps.reshape(1),
        field,
        above_row,
        below_row,
        coefficients,
    )


def coarsen(stepped):
    return stepped.reshape(C, FACTOR, SW, FACTOR).mean(axis=(1, 3))


def column_table():
    columns = jnp.arange(SW, dtype=jnp.int32)
    orders = jnp.arange(MODES, dtype=jnp.int32)
    phase_angle = 2.0 * math.pi / SW * (columns[:, None] * orders[None, :] % SW).astype(jnp.float32)
    return jnp.concatenate([jnp.cos(phase_angle), -jnp.sin(phase_angle)], axis=1).astype(
        jnp.bfloat16
    )


def inverse_table():
    columns = jnp.arange(SW, dtype=jnp.int32)
    orders = jnp.arange(MODES, dtype=jnp.int32)
    phase_angle = 2.0 * math.pi / SW * (orders[:, None] * columns[None, :] % SW).astype(jnp.float32)
    weights = jnp.where(orders == 0, 1.0, 2.0).astype(jnp.float32)[:, None]
    return jnp.concatenate(
        [weights * jnp.cos(phase_angle), -weights * jnp.sin(phase_angle)], axis=0
    )


def row_tables(row_ids, total_rows):
    orders = jnp.arange(2 * MODES, dtype=jnp.int32)
    wave_numbers = jnp.where(orders < MODES, orders, total_rows - 2 * MODES + orders)
    phase_angle = (
        2.0
        * math.pi
        / total_rows
        * (wave_numbers[:, None] * row_ids[None, :] % total_rows).astype(jnp.float32)
    )
    return (jnp.cos(phase_angle), jnp.sin(phase_angle))


def rows_forward(part_real, part_imag, cosine_table, sine_table):
    highest = lax.Precision.HIGHEST
    real_part = jnp.einsum("jy,yhl->hjl", cosine_table, part_real, precision=highest) + jnp.einsum(
        "jy,yhl->hjl", sine_table, part_imag, precision=highest
    )
    imag_part = jnp.einsum("jy,yhl->hjl", cosine_table, part_imag, precision=highest) - jnp.einsum(
        "jy,yhl->hjl", sine_table, part_real, precision=highest
    )
    return (real_part, imag_part)


def rows_inverse(mixed_real, mixed_imag, cosine_table, sine_table):
    highest = lax.Precision.HIGHEST
    rows_real = jnp.einsum("jy,ojl->yol", cosine_table, mixed_real, precision=highest) - jnp.einsum(
        "jy,ojl->yol", sine_table, mixed_imag, precision=highest
    )
    rows_imag = jnp.einsum("jy,ojl->yol", sine_table, mixed_real, precision=highest) + jnp.einsum(
        "jy,ojl->yol", cosine_table, mixed_imag, precision=highest
    )
    return jnp.concatenate([rows_real, rows_imag], axis=2)


def mix_modes(spectral, mode_real, mode_imag):
    real_weight, imag_weight = spectral[0], spectral[1]
    mode_real = mode_real[:, None]
    mode_imag = mode_imag[:, None]
    mixed_real = jnp.sum(real_weight * mode_real - imag_weight * mode_imag, axis=0)
    mixed_imag = jnp.sum(real_weight * mode_imag + imag_weight * mode_real, axis=0)
    return (mixed_real, mixed_imag)


def gelu_slope(pre_act):
    normal_cdf = 0.5 * (1.0 + lax.erf(pre_act * (1.0 / math.sqrt(2.0))))
    density = jnp.exp(-0.5 * pre_act * pre_act) * (1.0 / math.sqrt(2.0 * math.pi))
    return normal_cdf + pre_act * density


def weight_grads(back_real, back_imag, mode_real, mode_imag):
    highest = lax.Precision.HIGHEST
    grad_real = jnp.einsum("ojl,hjl->hojl", back_real, mode_real, precision=highest) + jnp.einsum(
        "ojl,hjl->hojl", back_imag, mode_imag, precision=highest
    )
    grad_imag = jnp.einsum("ojl,hjl->hojl", back_imag, mode_real, precision=highest) - jnp.einsum(
        "ojl,hjl->hojl", back_real, mode_imag, precision=highest
    )
    return jnp.stack([grad_real, grad_imag])


def lift_rows(sample, lift_weight, lift_bias):
    lifted = jnp.einsum("ycx,ch->yhx", sample, lift_weight, preferred_element_type=jnp.float32)
    return (lifted + lift_bias[None, :, None]).astype(jnp.bfloat16)


def gather_along(block, axis):
    count = lax.axis_size(axis)
    index = lax.axis_index(axis)
    gathered = jnp.zeros((count,) + block.shape, block.dtype)
    for shift in range(count):
        if shift == 0:
            piece = block
        else:
            piece = lax.ppermute(block, axis, [(i, (i + shift) % count) for i in range(count)])
        gathered = lax.dynamic_update_index_in_dim(gathered, piece, (index - shift) % count, 0)
    return gathered


def gather_rows(block, axes):
    for axis in reversed(axes):
        block = gather_along(block, axis)
    return block.reshape((-1,) + block.shape[len(axes):])


def packed_ppermute(parts, axis, perm):
    flat = jnp.concatenate([part.reshape(-1) for part in parts])
    flat = lax.ppermute(flat, axis, perm)
    result = []
    offset = 0
    for part in parts:
        result.append(flat[offset : offset + part.size].reshape(part.shape))
        offset += part.size
    return tuple(result)


def pair_sum(values, axis):
    if lax.axis_size(axis) != 2:
        return lax.psum(values, axis)
    other = packed_ppermute(values, axis, [(0, 1), (1, 0)])
    return tuple(mine + theirs for mine, theirs in zip(values, other))


def group_grads(back_real, back_imag, mode_real, mode_imag, axis):
    count = lax.axis_size(axis)
    index = lax.axis_index(axis)
    block = mode_real.shape[1] // count
    total = None
    for shift in range(count):
        target = (index + shift) % count
        piece = tuple(
            lax.dynamic_slice_in_dim(part, target * block, block, 1)
            for part in (back_real, back_imag, mode_real, mode_imag)
        )
        if shift:
            piece = packed_ppermute(piece, axis, [(i, (i + shift) % count) for i in range(count)])
        term = weight_grads(*piece)
        total = term if total is None else total + term
    return total


def body(
    field,
    counts,
    kappa_rows,
    kappa_cols,
    drift_rows,
    drift_cols,
    assign,
    buffer,
    lift_weight,
    lift_bias,
    point_weight,
    point_bias,
    spectral_weight,
    cotangent,
):
    above_row, below_row = halo_rows(field, ("grp", "mem", "row"))
    row_sums = solve_rows(
        field,
        above_row,
        below_row,
        counts[0],
        kappa_rows,
        drift_rows,
        kappa_cols,
        drift_cols,
    )
    coarse_rows = (row_sums.reshape(C, SW, FACTOR).sum(axis=2) * (1.0 / (FACTOR * FACTOR)))[None]
    coarse_low = coarse_rows.astype(jnp.bfloat16)
    member = lax.axis_index("mem")
    member_rows = buffer.shape[1]
    total_rows = member_rows * lax.axis_size("mem")
    row_ids = member * member_rows + jnp.arange(member_rows, dtype=jnp.int32)
    owners = lax.dynamic_slice_in_dim(assign, member * member_rows, member_rows, 0)
    chosen = (owners == lax.axis_index("grp"))[:, None, None]
    forward_table = column_table()
    every_row = gather_rows(coarse_low[0], ("grp", "mem", "row"))
    fresh_rows = lax.dynamic_slice_in_dim(every_row, member * member_rows, member_rows, 0)
    sample = jnp.where(chosen, fresh_rows, buffer[0])
    hidden = lift_rows(sample, lift_weight, lift_bias)
    column_part = jnp.einsum(
        "yhx,xk->yhk", hidden, forward_table, preferred_element_type=jnp.float32
    )
    norm_scale = 1.0 / math.sqrt(total_rows * SW)
    cosine_table, sine_table = row_tables(row_ids, total_rows)
    part_real, part_imag = rows_forward(
        column_part[:, :, :MODES], column_part[:, :, MODES:], cosine_table, sine_table
    )
    mode_real, mode_imag = pair_sum((part_real * norm_scale, part_imag * norm_scale), "mem")
    mixed_real, mixed_imag = mix_modes(spectral_weight, mode_real, mode_imag)
    spatial = (
        jnp.einsum(
            "yok,kx->yox",
            rows_inverse(mixed_real, mixed_imag, cosine_table, sine_table),
            inverse_table(),
            precision=lax.Precision.HIGHEST,
        )
        * norm_scale
    )
    pre_act = (
        spatial
        + jnp.einsum("yhx,ho->yox", hidden, point_weight, preferred_element_type=jnp.float32)
        + point_bias[None, :, None]
    )
    layer_rows = jax.nn.gelu(pre_act, approximate=False).astype(jnp.bfloat16)[None]
    back_signal = (cotangent[0].astype(jnp.float32) * gelu_slope(pre_act)).astype(jnp.bfloat16)
    back_part = jnp.einsum(
        "yox,xk->yok", back_signal, forward_table, preferred_element_type=jnp.float32
    )
    back_real, back_imag = rows_forward(
        back_part[:, :, :MODES], back_part[:, :, MODES:], cosine_table, sine_table
    )
    weights_mode = jnp.where(jnp.arange(MODES) == 0, 1.0, 2.0).astype(jnp.float32) * norm_scale
    back_real, back_imag = pair_sum((back_real * weights_mode, back_imag * weights_mode), "mem")
    block_size = HID // lax.axis_size("mem")
    block_real = lax.dynamic_slice_in_dim(mode_real, member * block_size, block_size, 0)
    block_imag = lax.dynamic_slice_in_dim(mode_imag, member * block_size, block_size, 0)
    summed = group_grads(back_real, back_imag, block_real, block_imag, "grp")
    return (coarse_rows, layer_rows, summed / lax.axis_size("grp"))


def solution(mesh):
    in_specs = (
        P(None, ("grp", "mem", "row"), None),
        P(("grp", "mem", "row")),
        P(("grp", "mem", "row")),
        P(),
        P(None, ("grp", "mem", "row")),
        P(),
        P(),
        P("grp", "mem", None, None),
        P(),
        P(),
        P(None, "row"),
        P("row"),
        P(None, None, "row", None, None),
        P("grp", "mem", "row", None),
    )
    out_specs = (
        P(("grp", "mem", "row"), None, None),
        P("grp", "mem", "row", None),
        P(None, "mem", "row", "grp", None),
    )
    return jax.shard_map(body, mesh=mesh, in_specs=in_specs, out_specs=out_specs, check_vma=False)
```

```python
import math

import jax
import jax.numpy as jnp
from jax import lax
from jax.experimental import pallas as pl
from jax.experimental.pallas import tpu as pltpu
from jax.sharding import PartitionSpec as P

C = 4
SW = 1024
FACTOR = 16
HID = 32
MODES = 16


window_time = 0.24


def with_halo(block, sides, width):
    for axis, dim in sides:
        count = lax.axis_size(axis)
        forward = [(i, i + 1) for i in range(count - 1)]
        forward.append((count - 1, 0))
        backward = [(target, source) for source, target in forward]
        low = lax.ppermute(
            lax.slice_in_dim(block, block.shape[dim] - width, None, axis=dim), axis, forward
        )
        high = lax.ppermute(lax.slice_in_dim(block, 0, width, axis=dim), axis, backward)
        block = jnp.concatenate([low, block, high], axis=dim)
    return block


def halo_rows(block, axis):
    count = lax.axis_size(axis)
    forward = [(i, (i + 1) % count) for i in range(count)]
    backward = [((i + 1) % count, i) for i in range(count)]
    above = lax.ppermute(block[:, -1:], axis, forward)
    below = lax.ppermute(block[:, :1], axis, backward)
    return above, below


def slab_solve(
    slab_rows, above_row, below_row, substeps, kappa_row, drift_row, kappa_col, drift_col
):
    diffusion = kappa_row[:, None] * kappa_col[None, :]
    drift_along = drift_row[0][:, None] * drift_col[0][None, :]
    drift_across = drift_row[1][:, None] * drift_col[1][None, :]
    step_size = window_time / substeps.astype(jnp.float32)

    def advance(number, current):
        stacked = jnp.concatenate([above_row, current, below_row], axis=1)
        upper_rows = stacked[:, :-2]
        lower_rows = stacked[:, 2:]
        right_cells = jnp.roll(current, -1, axis=2)
        left_cells = jnp.roll(current, 1, axis=2)
        change = diffusion * (right_cells + left_cells + upper_rows + lower_rows - 4.0 * current)
        change = (
            change
            - 0.5 * drift_along * (right_cells - left_cells)
            - 0.5 * drift_across * (lower_rows - upper_rows)
        )
        return current + step_size * change

    return lax.fori_loop(jnp.zeros((), jnp.int32), substeps, advance, slab_rows)


CHUNK = 512
UNROLL = 4


def solve_kernel(
    step_ref, count_ref, field_ref, above_ref, below_ref, coef_ref, out_ref, first_ref, second_ref
):
    tracers, rows, width = field_ref.shape
    chunks = width // CHUNK

    def chunk_at(index):
        return pl.ds(pl.multiple_of(index * CHUNK, CHUNK), CHUNK)

    def prepare(index, carry):
        cols = chunk_at(index)
        for tracer in range(tracers):
            first_ref[tracer, :, cols] = field_ref[tracer, :, cols].astype(jnp.float32)
        return carry

    lax.fori_loop(0, chunks, prepare, 0)
    step = step_ref[0]
    row_ids = lax.broadcasted_iota(jnp.int32, (rows, CHUNK), 0)

    def sweep(source_ref, target_ref):
        def update(index, inner):
            tracer = index // chunks
            column = index % chunks
            cols = chunk_at(column)
            before = pl.ds(pl.multiple_of(((column * CHUNK - 128) % width), 128), 128)
            after = pl.ds(pl.multiple_of((((column + 1) * CHUNK) % width), 128), 128)
            current = source_ref[tracer, :, cols]
            extended = jnp.concatenate(
                [source_ref[tracer, :, before], current, source_ref[tracer, :, after]], axis=1
            )
            span = CHUNK + 256
            right_cells = pltpu.roll(extended, span - 1, 1)[:, 128 : 128 + CHUNK]
            left_cells = pltpu.roll(extended, 1, 1)[:, 128 : 128 + CHUNK]
            upper_rows = jnp.where(
                row_ids == 0,
                above_ref[tracer, :, cols].astype(jnp.float32),
                pltpu.roll(current, 1, 0),
            )
            lower_rows = jnp.where(
                row_ids == rows - 1,
                below_ref[tracer, :, cols].astype(jnp.float32),
                pltpu.roll(current, rows - 1, 0),
            )
            change = coef_ref[0, :, cols] * (
                right_cells + left_cells + upper_rows + lower_rows - 4.0 * current
            )
            change = (
                change
                - coef_ref[1, :, cols] * (right_cells - left_cells)
                - coef_ref[2, :, cols] * (lower_rows - upper_rows)
            )
            target_ref[tracer, :, cols] = current + step * change
            return inner

        lax.fori_loop(0, tracers * chunks, update, 0, unroll=UNROLL)

    def two_steps(number, carry):
        sweep(first_ref, second_ref)
        sweep(second_ref, first_ref)
        return carry

    total = count_ref[0]
    lax.fori_loop(0, total // 2, two_steps, 0)

    def collect(final_ref):
        def store(index, carry):
            tracer = index // chunks
            cols = chunk_at(index % chunks)
            out_ref[tracer, :, cols] = jnp.sum(final_ref[tracer, :, cols], axis=0, keepdims=True)
            return carry

        lax.fori_loop(0, tracers * chunks, store, 0)

    @pl.when(total % 2 == 1)
    def _():
        sweep(first_ref, second_ref)
        collect(second_ref)

    @pl.when(total % 2 == 0)
    def _():
        collect(first_ref)


def solve_rows(field, above_row, below_row, substeps, kappa_row, drift_row, kappa_col, drift_col):
    tracers, rows, width = field.shape
    step = (window_time / substeps.astype(jnp.float32)).reshape(1)
    kappa_col = kappa_col.astype(jnp.float32)
    drift_col = drift_col.astype(jnp.float32)
    coefficients = jnp.stack(
        [
            kappa_row[:, None] * kappa_col[None, :],
            0.5 * (drift_row[0][:, None] * drift_col[0][None, :]),
            0.5 * (drift_row[1][:, None] * drift_col[1][None, :]),
        ]
    )
    smem = pl.BlockSpec(memory_space=pltpu.SMEM)
    vmem = pl.BlockSpec(memory_space=pltpu.VMEM)
    return pl.pallas_call(
        solve_kernel,
        out_shape=jax.ShapeDtypeStruct((tracers, 1, width), jnp.float32),
        in_specs=[smem, smem] + [vmem] * 4,
        out_specs=vmem,
        scratch_shapes=[
            pltpu.VMEM((tracers, rows, width), jnp.float32),
            pltpu.VMEM((tracers, rows, width), jnp.float32),
        ],
        compiler_params=pltpu.CompilerParams(vmem_limit_bytes=56 * 1024 * 1024),
    )(
        step,
        substeps.reshape(1),
        field,
        above_row,
        below_row,
        coefficients,
    )


def coarsen(stepped):
    return stepped.reshape(C, FACTOR, SW, FACTOR).mean(axis=(1, 3))


def column_table():
    columns = jnp.arange(SW, dtype=jnp.int32)
    orders = jnp.arange(MODES, dtype=jnp.int32)
    phase_angle = 2.0 * math.pi / SW * (columns[:, None] * orders[None, :] % SW).astype(jnp.float32)
    return jnp.concatenate([jnp.cos(phase_angle), -jnp.sin(phase_angle)], axis=1).astype(
        jnp.bfloat16
    )


def inverse_table():
    columns = jnp.arange(SW, dtype=jnp.int32)
    orders = jnp.arange(MODES, dtype=jnp.int32)
    phase_angle = 2.0 * math.pi / SW * (orders[:, None] * columns[None, :] % SW).astype(jnp.float32)
    weights = jnp.where(orders == 0, 1.0, 2.0).astype(jnp.float32)[:, None]
    return jnp.concatenate(
        [weights * jnp.cos(phase_angle), -weights * jnp.sin(phase_angle)], axis=0
    )


def row_tables(row_ids, total_rows):
    orders = jnp.arange(2 * MODES, dtype=jnp.int32)
    wave_numbers = jnp.where(orders < MODES, orders, total_rows - 2 * MODES + orders)
    phase_angle = (
        2.0
        * math.pi
        / total_rows
        * (wave_numbers[:, None] * row_ids[None, :] % total_rows).astype(jnp.float32)
    )
    return (jnp.cos(phase_angle), jnp.sin(phase_angle))


def rows_forward(part_real, part_imag, cosine_table, sine_table):
    highest = lax.Precision.HIGHEST
    real_part = jnp.einsum("jy,yhl->hjl", cosine_table, part_real, precision=highest) + jnp.einsum(
        "jy,yhl->hjl", sine_table, part_imag, precision=highest
    )
    imag_part = jnp.einsum("jy,yhl->hjl", cosine_table, part_imag, precision=highest) - jnp.einsum(
        "jy,yhl->hjl", sine_table, part_real, precision=highest
    )
    return (real_part, imag_part)


def rows_inverse(mixed_real, mixed_imag, cosine_table, sine_table):
    highest = lax.Precision.HIGHEST
    rows_real = jnp.einsum("jy,ojl->yol", cosine_table, mixed_real, precision=highest) - jnp.einsum(
        "jy,ojl->yol", sine_table, mixed_imag, precision=highest
    )
    rows_imag = jnp.einsum("jy,ojl->yol", sine_table, mixed_real, precision=highest) + jnp.einsum(
        "jy,ojl->yol", cosine_table, mixed_imag, precision=highest
    )
    return jnp.concatenate([rows_real, rows_imag], axis=2)


def mix_modes(spectral, mode_real, mode_imag):
    real_weight, imag_weight = spectral[0], spectral[1]
    mode_real = mode_real[:, None]
    mode_imag = mode_imag[:, None]
    mixed_real = jnp.sum(real_weight * mode_real - imag_weight * mode_imag, axis=0)
    mixed_imag = jnp.sum(real_weight * mode_imag + imag_weight * mode_real, axis=0)
    return (mixed_real, mixed_imag)


def gelu_slope(pre_act):
    normal_cdf = 0.5 * (1.0 + lax.erf(pre_act * (1.0 / math.sqrt(2.0))))
    density = jnp.exp(-0.5 * pre_act * pre_act) * (1.0 / math.sqrt(2.0 * math.pi))
    return normal_cdf + pre_act * density


def weight_grads(back_real, back_imag, mode_real, mode_imag):
    highest = lax.Precision.HIGHEST
    grad_real = jnp.einsum("ojl,hjl->hojl", back_real, mode_real, precision=highest) + jnp.einsum(
        "ojl,hjl->hojl", back_imag, mode_imag, precision=highest
    )
    grad_imag = jnp.einsum("ojl,hjl->hojl", back_imag, mode_real, precision=highest) - jnp.einsum(
        "ojl,hjl->hojl", back_real, mode_imag, precision=highest
    )
    return jnp.stack([grad_real, grad_imag])


def lift_rows(sample, lift_weight, lift_bias):
    lifted = jnp.einsum("ycx,ch->yhx", sample, lift_weight, preferred_element_type=jnp.float32)
    return (lifted + lift_bias[None, :, None]).astype(jnp.bfloat16)


def gather_along(block, axis):
    count = lax.axis_size(axis)
    index = lax.axis_index(axis)
    gathered = jnp.zeros((count,) + block.shape, block.dtype)
    for shift in range(count):
        if shift == 0:
            piece = block
        else:
            piece = lax.ppermute(block, axis, [(i, (i + shift) % count) for i in range(count)])
        gathered = lax.dynamic_update_index_in_dim(gathered, piece, (index - shift) % count, 0)
    return gathered


def gather_rows(block, axes):
    for axis in reversed(axes):
        block = gather_along(block, axis)
    return block.reshape((-1,) + block.shape[len(axes):])


def packed_ppermute(parts, axis, perm):
    packed = lax.ppermute(jnp.concatenate(parts, axis=0), axis, perm)
    result = []
    offset = 0
    for part in parts:
        result.append(lax.slice_in_dim(packed, offset, offset + part.shape[0], axis=0))
        offset += part.shape[0]
    return tuple(result)


def pair_sum(values, axis):
    if lax.axis_size(axis) != 2:
        return lax.psum(values, axis)
    other = packed_ppermute(values, axis, [(0, 1), (1, 0)])
    return tuple(mine + theirs for mine, theirs in zip(values, other))


def group_grads(back_real, back_imag, mode_real, mode_imag, axis):
    count = lax.axis_size(axis)
    index = lax.axis_index(axis)
    block = mode_real.shape[1] // count
    total = None
    for shift in range(count):
        target = (index + shift) % count
        piece = tuple(
            lax.dynamic_slice_in_dim(part, target * block, block, 1)
            for part in (back_real, back_imag, mode_real, mode_imag)
        )
        if shift:
            piece = packed_ppermute(piece, axis, [(i, (i + shift) % count) for i in range(count)])
        term = weight_grads(*piece)
        total = term if total is None else total + term
    return total


def body(
    field,
    counts,
    kappa_rows,
    kappa_cols,
    drift_rows,
    drift_cols,
    assign,
    buffer,
    lift_weight,
    lift_bias,
    point_weight,
    point_bias,
    spectral_weight,
    cotangent,
):
    above_row, below_row = halo_rows(field, ("grp", "mem", "row"))
    row_sums = solve_rows(
        field,
        above_row,
        below_row,
        counts[0],
        kappa_rows,
        drift_rows,
        kappa_cols,
        drift_cols,
    )
    coarse_rows = (row_sums.reshape(C, SW, FACTOR).sum(axis=2) * (1.0 / (FACTOR * FACTOR)))[None]
    coarse_low = coarse_rows.astype(jnp.bfloat16)
    member = lax.axis_index("mem")
    member_rows = buffer.shape[1]
    total_rows = member_rows * lax.axis_size("mem")
    row_ids = member * member_rows + jnp.arange(member_rows, dtype=jnp.int32)
    owners = lax.dynamic_slice_in_dim(assign, member * member_rows, member_rows, 0)
    chosen = (owners == lax.axis_index("grp"))[:, None, None]
    forward_table = column_table()
    every_row = gather_rows(coarse_low[0], ("grp", "mem", "row"))
    fresh_rows = lax.dynamic_slice_in_dim(every_row, member * member_rows, member_rows, 0)
    sample = jnp.where(chosen, fresh_rows, buffer[0])
    hidden = lift_rows(sample, lift_weight, lift_bias)
    column_part = jnp.einsum(
        "yhx,xk->yhk", hidden, forward_table, preferred_element_type=jnp.float32
    )
    norm_scale = 1.0 / math.sqrt(total_rows * SW)
    cosine_table, sine_table = row_tables(row_ids, total_rows)
    part_real, part_imag = rows_forward(
        column_part[:, :, :MODES], column_part[:, :, MODES:], cosine_table, sine_table
    )
    mode_real, mode_imag = pair_sum((part_real * norm_scale, part_imag * norm_scale), "mem")
    mixed_real, mixed_imag = mix_modes(spectral_weight, mode_real, mode_imag)
    spatial = (
        jnp.einsum(
            "yok,kx->yox",
            rows_inverse(mixed_real, mixed_imag, cosine_table, sine_table),
            inverse_table(),
            precision=lax.Precision.HIGHEST,
        )
        * norm_scale
    )
    pre_act = (
        spatial
        + jnp.einsum("yhx,ho->yox", hidden, point_weight, preferred_element_type=jnp.float32)
        + point_bias[None, :, None]
    )
    layer_rows = jax.nn.gelu(pre_act, approximate=False).astype(jnp.bfloat16)[None]
    back_signal = (cotangent[0].astype(jnp.float32) * gelu_slope(pre_act)).astype(jnp.bfloat16)
    back_part = jnp.einsum(
        "yox,xk->yok", back_signal, forward_table, preferred_element_type=jnp.float32
    )
    back_real, back_imag = rows_forward(
        back_part[:, :, :MODES], back_part[:, :, MODES:], cosine_table, sine_table
    )
    weights_mode = jnp.where(jnp.arange(MODES) == 0, 1.0, 2.0).astype(jnp.float32) * norm_scale
    back_real, back_imag = pair_sum((back_real * weights_mode, back_imag * weights_mode), "mem")
    block_size = HID // lax.axis_size("mem")
    block_real = lax.dynamic_slice_in_dim(mode_real, member * block_size, block_size, 0)
    block_imag = lax.dynamic_slice_in_dim(mode_imag, member * block_size, block_size, 0)
    summed = group_grads(back_real, back_imag, block_real, block_imag, "grp")
    return (coarse_rows, layer_rows, summed / lax.axis_size("grp"))


def solution(mesh):
    in_specs = (
        P(None, ("grp", "mem", "row"), None),
        P(("grp", "mem", "row")),
        P(("grp", "mem", "row")),
        P(),
        P(None, ("grp", "mem", "row")),
        P(),
        P(),
        P("grp", "mem", None, None),
        P(),
        P(),
        P(None, "row"),
        P("row"),
        P(None, None, "row", None, None),
        P("grp", "mem", "row", None),
    )
    out_specs = (
        P(("grp", "mem", "row"), None, None),
        P("grp", "mem", "row", None),
        P(None, "mem", "row", "grp", None),
    )
    return jax.shard_map(body, mesh=mesh, in_specs=in_specs, out_specs=out_specs, check_vma=False)
```

```python
import math

import jax
import jax.numpy as jnp
from jax import lax
from jax.experimental import pallas as pl
from jax.experimental.pallas import tpu as pltpu
from jax.sharding import PartitionSpec as P

C = 4
SW = 1024
FACTOR = 16
HID = 32
MODES = 16


window_time = 0.24


def with_halo(block, sides, width):
    for axis, dim in sides:
        count = lax.axis_size(axis)
        forward = [(i, i + 1) for i in range(count - 1)]
        forward.append((count - 1, 0))
        backward = [(target, source) for source, target in forward]
        low = lax.ppermute(
            lax.slice_in_dim(block, block.shape[dim] - width, None, axis=dim), axis, forward
        )
        high = lax.ppermute(lax.slice_in_dim(block, 0, width, axis=dim), axis, backward)
        block = jnp.concatenate([low, block, high], axis=dim)
    return block


def halo_rows(block, axis):
    count = lax.axis_size(axis)
    forward = [(i, (i + 1) % count) for i in range(count)]
    backward = [((i + 1) % count, i) for i in range(count)]
    above = lax.ppermute(block[:, -1:], axis, forward)
    below = lax.ppermute(block[:, :1], axis, backward)
    return above, below


def slab_solve(
    slab_rows, above_row, below_row, substeps, kappa_row, drift_row, kappa_col, drift_col
):
    diffusion = kappa_row[:, None] * kappa_col[None, :]
    drift_along = drift_row[0][:, None] * drift_col[0][None, :]
    drift_across = drift_row[1][:, None] * drift_col[1][None, :]
    step_size = window_time / substeps.astype(jnp.float32)

    def advance(number, current):
        stacked = jnp.concatenate([above_row, current, below_row], axis=1)
        upper_rows = stacked[:, :-2]
        lower_rows = stacked[:, 2:]
        right_cells = jnp.roll(current, -1, axis=2)
        left_cells = jnp.roll(current, 1, axis=2)
        change = diffusion * (right_cells + left_cells + upper_rows + lower_rows - 4.0 * current)
        change = (
            change
            - 0.5 * drift_along * (right_cells - left_cells)
            - 0.5 * drift_across * (lower_rows - upper_rows)
        )
        return current + step_size * change

    return lax.fori_loop(jnp.zeros((), jnp.int32), substeps, advance, slab_rows)


CHUNK = 1024
UNROLL = 8


def solve_kernel(
    step_ref, count_ref, field_ref, above_ref, below_ref, coef_ref, out_ref, first_ref, second_ref
):
    tracers, rows, width = field_ref.shape
    chunks = width // CHUNK

    def chunk_at(index):
        return pl.ds(pl.multiple_of(index * CHUNK, CHUNK), CHUNK)

    def prepare(index, carry):
        cols = chunk_at(index)
        for tracer in range(tracers):
            first_ref[tracer, :, cols] = field_ref[tracer, :, cols].astype(jnp.float32)
        return carry

    lax.fori_loop(0, chunks, prepare, 0)
    step = step_ref[0]
    row_ids = lax.broadcasted_iota(jnp.int32, (rows, CHUNK), 0)

    def sweep(source_ref, target_ref):
        def update(index, inner):
            tracer = index // chunks
            column = index % chunks
            cols = chunk_at(column)
            before = pl.ds(pl.multiple_of(((column * CHUNK - 128) % width), 128), 128)
            after = pl.ds(pl.multiple_of((((column + 1) * CHUNK) % width), 128), 128)
            current = source_ref[tracer, :, cols]
            extended = jnp.concatenate(
                [source_ref[tracer, :, before], current, source_ref[tracer, :, after]], axis=1
            )
            span = CHUNK + 256
            right_cells = pltpu.roll(extended, span - 1, 1)[:, 128 : 128 + CHUNK]
            left_cells = pltpu.roll(extended, 1, 1)[:, 128 : 128 + CHUNK]
            upper_rows = jnp.where(
                row_ids == 0,
                above_ref[tracer, :, cols].astype(jnp.float32),
                pltpu.roll(current, 1, 0),
            )
            lower_rows = jnp.where(
                row_ids == rows - 1,
                below_ref[tracer, :, cols].astype(jnp.float32),
                pltpu.roll(current, rows - 1, 0),
            )
            change = coef_ref[0, :, cols] * (
                right_cells + left_cells + upper_rows + lower_rows - 4.0 * current
            )
            change = (
                change
                - coef_ref[1, :, cols] * (right_cells - left_cells)
                - coef_ref[2, :, cols] * (lower_rows - upper_rows)
            )
            target_ref[tracer, :, cols] = current + step * change
            return inner

        lax.fori_loop(0, tracers * chunks, update, 0, unroll=UNROLL)

    def two_steps(number, carry):
        sweep(first_ref, second_ref)
        sweep(second_ref, first_ref)
        return carry

    total = count_ref[0]
    lax.fori_loop(0, total // 2, two_steps, 0)

    def collect(final_ref):
        def store(index, carry):
            tracer = index // chunks
            cols = chunk_at(index % chunks)
            out_ref[tracer, :, cols] = jnp.sum(final_ref[tracer, :, cols], axis=0, keepdims=True)
            return carry

        lax.fori_loop(0, tracers * chunks, store, 0)

    @pl.when(total % 2 == 1)
    def _():
        sweep(first_ref, second_ref)
        collect(second_ref)

    @pl.when(total % 2 == 0)
    def _():
        collect(first_ref)


def solve_rows(field, above_row, below_row, substeps, kappa_row, drift_row, kappa_col, drift_col):
    tracers, rows, width = field.shape
    step = (window_time / substeps.astype(jnp.float32)).reshape(1)
    kappa_col = kappa_col.astype(jnp.float32)
    drift_col = drift_col.astype(jnp.float32)
    coefficients = jnp.stack(
        [
            kappa_row[:, None] * kappa_col[None, :],
            0.5 * (drift_row[0][:, None] * drift_col[0][None, :]),
            0.5 * (drift_row[1][:, None] * drift_col[1][None, :]),
        ]
    )
    smem = pl.BlockSpec(memory_space=pltpu.SMEM)
    vmem = pl.BlockSpec(memory_space=pltpu.VMEM)
    return pl.pallas_call(
        solve_kernel,
        out_shape=jax.ShapeDtypeStruct((tracers, 1, width), jnp.float32),
        in_specs=[smem, smem] + [vmem] * 4,
        out_specs=vmem,
        scratch_shapes=[
            pltpu.VMEM((tracers, rows, width), jnp.float32),
            pltpu.VMEM((tracers, rows, width), jnp.float32),
        ],
        compiler_params=pltpu.CompilerParams(vmem_limit_bytes=56 * 1024 * 1024),
    )(
        step,
        substeps.reshape(1),
        field,
        above_row,
        below_row,
        coefficients,
    )


def coarsen(stepped):
    return stepped.reshape(C, FACTOR, SW, FACTOR).mean(axis=(1, 3))


def column_table():
    columns = jnp.arange(SW, dtype=jnp.int32)
    orders = jnp.arange(MODES, dtype=jnp.int32)
    phase_angle = 2.0 * math.pi / SW * (columns[:, None] * orders[None, :] % SW).astype(jnp.float32)
    return jnp.concatenate([jnp.cos(phase_angle), -jnp.sin(phase_angle)], axis=1).astype(
        jnp.bfloat16
    )


def inverse_table():
    columns = jnp.arange(SW, dtype=jnp.int32)
    orders = jnp.arange(MODES, dtype=jnp.int32)
    phase_angle = 2.0 * math.pi / SW * (orders[:, None] * columns[None, :] % SW).astype(jnp.float32)
    weights = jnp.where(orders == 0, 1.0, 2.0).astype(jnp.float32)[:, None]
    return jnp.concatenate(
        [weights * jnp.cos(phase_angle), -weights * jnp.sin(phase_angle)], axis=0
    )


def row_tables(row_ids, total_rows):
    orders = jnp.arange(2 * MODES, dtype=jnp.int32)
    wave_numbers = jnp.where(orders < MODES, orders, total_rows - 2 * MODES + orders)
    phase_angle = (
        2.0
        * math.pi
        / total_rows
        * (wave_numbers[:, None] * row_ids[None, :] % total_rows).astype(jnp.float32)
    )
    return (jnp.cos(phase_angle), jnp.sin(phase_angle))


def rows_forward(part_real, part_imag, cosine_table, sine_table):
    highest = lax.Precision.HIGHEST
    real_part = jnp.einsum("jy,yhl->hjl", cosine_table, part_real, precision=highest) + jnp.einsum(
        "jy,yhl->hjl", sine_table, part_imag, precision=highest
    )
    imag_part = jnp.einsum("jy,yhl->hjl", cosine_table, part_imag, precision=highest) - jnp.einsum(
        "jy,yhl->hjl", sine_table, part_real, precision=highest
    )
    return (real_part, imag_part)


def rows_inverse(mixed_real, mixed_imag, cosine_table, sine_table):
    highest = lax.Precision.HIGHEST
    rows_real = jnp.einsum("jy,ojl->yol", cosine_table, mixed_real, precision=highest) - jnp.einsum(
        "jy,ojl->yol", sine_table, mixed_imag, precision=highest
    )
    rows_imag = jnp.einsum("jy,ojl->yol", sine_table, mixed_real, precision=highest) + jnp.einsum(
        "jy,ojl->yol", cosine_table, mixed_imag, precision=highest
    )
    return jnp.concatenate([rows_real, rows_imag], axis=2)


def mix_modes(spectral, mode_real, mode_imag):
    real_weight, imag_weight = spectral[0], spectral[1]
    mode_real = mode_real[:, None]
    mode_imag = mode_imag[:, None]
    mixed_real = jnp.sum(real_weight * mode_real - imag_weight * mode_imag, axis=0)
    mixed_imag = jnp.sum(real_weight * mode_imag + imag_weight * mode_real, axis=0)
    return (mixed_real, mixed_imag)


def gelu_slope(pre_act):
    normal_cdf = 0.5 * (1.0 + lax.erf(pre_act * (1.0 / math.sqrt(2.0))))
    density = jnp.exp(-0.5 * pre_act * pre_act) * (1.0 / math.sqrt(2.0 * math.pi))
    return normal_cdf + pre_act * density


def weight_grads(back_real, back_imag, mode_real, mode_imag):
    highest = lax.Precision.HIGHEST
    grad_real = jnp.einsum("ojl,hjl->hojl", back_real, mode_real, precision=highest) + jnp.einsum(
        "ojl,hjl->hojl", back_imag, mode_imag, precision=highest
    )
    grad_imag = jnp.einsum("ojl,hjl->hojl", back_imag, mode_real, precision=highest) - jnp.einsum(
        "ojl,hjl->hojl", back_real, mode_imag, precision=highest
    )
    return jnp.stack([grad_real, grad_imag])


def lift_rows(sample, lift_weight, lift_bias):
    lifted = jnp.einsum("ycx,ch->yhx", sample, lift_weight, preferred_element_type=jnp.float32)
    return (lifted + lift_bias[None, :, None]).astype(jnp.bfloat16)


def gather_along(block, axis):
    count = lax.axis_size(axis)
    index = lax.axis_index(axis)
    gathered = jnp.zeros((count,) + block.shape, block.dtype)
    for shift in range(count):
        if shift == 0:
            piece = block
        else:
            piece = lax.ppermute(block, axis, [(i, (i + shift) % count) for i in range(count)])
        gathered = lax.dynamic_update_index_in_dim(gathered, piece, (index - shift) % count, 0)
    return gathered


def gather_rows(block, axes):
    for axis in reversed(axes):
        block = gather_along(block, axis)
    return block.reshape((-1,) + block.shape[len(axes):])


def packed_ppermute(parts, axis, perm):
    packed = lax.ppermute(jnp.concatenate(parts, axis=0), axis, perm)
    result = []
    offset = 0
    for part in parts:
        result.append(lax.slice_in_dim(packed, offset, offset + part.shape[0], axis=0))
        offset += part.shape[0]
    return tuple(result)


def pair_sum(values, axis):
    if lax.axis_size(axis) != 2:
        return lax.psum(values, axis)
    other = packed_ppermute(values, axis, [(0, 1), (1, 0)])
    return tuple(mine + theirs for mine, theirs in zip(values, other))


def group_grads(back_real, back_imag, mode_real, mode_imag, axis):
    count = lax.axis_size(axis)
    index = lax.axis_index(axis)
    block = mode_real.shape[1] // count
    total = None
    for shift in range(count):
        target = (index + shift) % count
        piece = tuple(
            lax.dynamic_slice_in_dim(part, target * block, block, 1)
            for part in (back_real, back_imag, mode_real, mode_imag)
        )
        if shift:
            piece = packed_ppermute(piece, axis, [(i, (i + shift) % count) for i in range(count)])
        term = weight_grads(*piece)
        total = term if total is None else total + term
    return total


def body(
    field,
    counts,
    kappa_rows,
    kappa_cols,
    drift_rows,
    drift_cols,
    assign,
    buffer,
    lift_weight,
    lift_bias,
    point_weight,
    point_bias,
    spectral_weight,
    cotangent,
):
    above_row, below_row = halo_rows(field, ("grp", "mem", "row"))
    row_sums = solve_rows(
        field,
        above_row,
        below_row,
        counts[0],
        kappa_rows,
        drift_rows,
        kappa_cols,
        drift_cols,
    )
    coarse_rows = (row_sums.reshape(C, SW, FACTOR).sum(axis=2) * (1.0 / (FACTOR * FACTOR)))[None]
    coarse_low = coarse_rows.astype(jnp.bfloat16)
    member = lax.axis_index("mem")
    member_rows = buffer.shape[1]
    total_rows = member_rows * lax.axis_size("mem")
    row_ids = member * member_rows + jnp.arange(member_rows, dtype=jnp.int32)
    owners = lax.dynamic_slice_in_dim(assign, member * member_rows, member_rows, 0)
    chosen = (owners == lax.axis_index("grp"))[:, None, None]
    forward_table = column_table()
    every_row = gather_rows(coarse_low[0], ("grp", "mem", "row"))
    fresh_rows = lax.dynamic_slice_in_dim(every_row, member * member_rows, member_rows, 0)
    sample = jnp.where(chosen, fresh_rows, buffer[0])
    hidden = lift_rows(sample, lift_weight, lift_bias)
    column_part = jnp.einsum(
        "yhx,xk->yhk", hidden, forward_table, preferred_element_type=jnp.float32
    )
    norm_scale = 1.0 / math.sqrt(total_rows * SW)
    cosine_table, sine_table = row_tables(row_ids, total_rows)
    part_real, part_imag = rows_forward(
        column_part[:, :, :MODES], column_part[:, :, MODES:], cosine_table, sine_table
    )
    mode_real, mode_imag = pair_sum((part_real * norm_scale, part_imag * norm_scale), "mem")
    mixed_real, mixed_imag = mix_modes(spectral_weight, mode_real, mode_imag)
    spatial = (
        jnp.einsum(
            "yok,kx->yox",
            rows_inverse(mixed_real, mixed_imag, cosine_table, sine_table),
            inverse_table(),
            precision=lax.Precision.HIGHEST,
        )
        * norm_scale
    )
    pre_act = (
        spatial
        + jnp.einsum("yhx,ho->yox", hidden, point_weight, preferred_element_type=jnp.float32)
        + point_bias[None, :, None]
    )
    layer_rows = jax.nn.gelu(pre_act, approximate=False).astype(jnp.bfloat16)[None]
    back_signal = (cotangent[0].astype(jnp.float32) * gelu_slope(pre_act)).astype(jnp.bfloat16)
    back_part = jnp.einsum(
        "yox,xk->yok", back_signal, forward_table, preferred_element_type=jnp.float32
    )
    back_real, back_imag = rows_forward(
        back_part[:, :, :MODES], back_part[:, :, MODES:], cosine_table, sine_table
    )
    weights_mode = jnp.where(jnp.arange(MODES) == 0, 1.0, 2.0).astype(jnp.float32) * norm_scale
    back_real, back_imag = pair_sum((back_real * weights_mode, back_imag * weights_mode), "mem")
    block_size = HID // lax.axis_size("mem")
    block_real = lax.dynamic_slice_in_dim(mode_real, member * block_size, block_size, 0)
    block_imag = lax.dynamic_slice_in_dim(mode_imag, member * block_size, block_size, 0)
    summed = group_grads(back_real, back_imag, block_real, block_imag, "grp")
    return (coarse_rows, layer_rows, summed / lax.axis_size("grp"))


def solution(mesh):
    in_specs = (
        P(None, ("grp", "mem", "row"), None),
        P(("grp", "mem", "row")),
        P(("grp", "mem", "row")),
        P(),
        P(None, ("grp", "mem", "row")),
        P(),
        P(),
        P("grp", "mem", None, None),
        P(),
        P(),
        P(None, "row"),
        P("row"),
        P(None, None, "row", None, None),
        P("grp", "mem", "row", None),
    )
    out_specs = (
        P(("grp", "mem", "row"), None, None),
        P("grp", "mem", "row", None),
        P(None, "mem", "row", "grp", None),
    )
    return jax.shard_map(body, mesh=mesh, in_specs=in_specs, out_specs=out_specs, check_vma=False)
```

```python
import math

import jax
import jax.numpy as jnp
from jax import lax
from jax.experimental import pallas as pl
from jax.experimental.pallas import tpu as pltpu
from jax.sharding import PartitionSpec as P

C = 4
SW = 1024
FACTOR = 16
HID = 32
MODES = 16


window_time = 0.24


def with_halo(block, sides, width):
    for axis, dim in sides:
        count = lax.axis_size(axis)
        forward = [(i, i + 1) for i in range(count - 1)]
        forward.append((count - 1, 0))
        backward = [(target, source) for source, target in forward]
        low = lax.ppermute(
            lax.slice_in_dim(block, block.shape[dim] - width, None, axis=dim), axis, forward
        )
        high = lax.ppermute(lax.slice_in_dim(block, 0, width, axis=dim), axis, backward)
        block = jnp.concatenate([low, block, high], axis=dim)
    return block


def halo_rows(block, axis):
    count = lax.axis_size(axis)
    forward = [(i, (i + 1) % count) for i in range(count)]
    backward = [((i + 1) % count, i) for i in range(count)]
    above = lax.ppermute(block[:, -1:], axis, forward)
    below = lax.ppermute(block[:, :1], axis, backward)
    return above, below


def slab_solve(
    slab_rows, above_row, below_row, substeps, kappa_row, drift_row, kappa_col, drift_col
):
    diffusion = kappa_row[:, None] * kappa_col[None, :]
    drift_along = drift_row[0][:, None] * drift_col[0][None, :]
    drift_across = drift_row[1][:, None] * drift_col[1][None, :]
    step_size = window_time / substeps.astype(jnp.float32)

    def advance(number, current):
        stacked = jnp.concatenate([above_row, current, below_row], axis=1)
        upper_rows = stacked[:, :-2]
        lower_rows = stacked[:, 2:]
        right_cells = jnp.roll(current, -1, axis=2)
        left_cells = jnp.roll(current, 1, axis=2)
        change = diffusion * (right_cells + left_cells + upper_rows + lower_rows - 4.0 * current)
        change = (
            change
            - 0.5 * drift_along * (right_cells - left_cells)
            - 0.5 * drift_across * (lower_rows - upper_rows)
        )
        return current + step_size * change

    return lax.fori_loop(jnp.zeros((), jnp.int32), substeps, advance, slab_rows)


CHUNK = 2048
UNROLL = 4


def solve_kernel(
    step_ref, count_ref, field_ref, above_ref, below_ref, coef_ref, out_ref, first_ref, second_ref
):
    tracers, rows, width = field_ref.shape
    chunks = width // CHUNK

    def chunk_at(index):
        return pl.ds(pl.multiple_of(index * CHUNK, CHUNK), CHUNK)

    def prepare(index, carry):
        cols = chunk_at(index)
        for tracer in range(tracers):
            first_ref[tracer, :, cols] = field_ref[tracer, :, cols].astype(jnp.float32)
        return carry

    lax.fori_loop(0, chunks, prepare, 0)
    step = step_ref[0]
    row_ids = lax.broadcasted_iota(jnp.int32, (rows, CHUNK), 0)

    def sweep(source_ref, target_ref):
        def update(column, inner):
            cols = chunk_at(column)
            before = pl.ds(pl.multiple_of(((column * CHUNK - 128) % width), 128), 128)
            after = pl.ds(pl.multiple_of((((column + 1) * CHUNK) % width), 128), 128)
            diffusion = coef_ref[0, :, cols]
            along = coef_ref[1, :, cols]
            across = coef_ref[2, :, cols]
            for tracer in range(tracers):
                current = source_ref[tracer, :, cols]
                extended = jnp.concatenate(
                    [source_ref[tracer, :, before], current, source_ref[tracer, :, after]], axis=1
                )
                span = CHUNK + 256
                right_cells = pltpu.roll(extended, span - 1, 1)[:, 128 : 128 + CHUNK]
                left_cells = pltpu.roll(extended, 1, 1)[:, 128 : 128 + CHUNK]
                upper_rows = jnp.where(
                    row_ids == 0, above_ref[tracer, :, cols].astype(jnp.float32), pltpu.roll(current, 1, 0)
                )
                lower_rows = jnp.where(
                    row_ids == rows - 1, below_ref[tracer, :, cols].astype(jnp.float32), pltpu.roll(current, rows - 1, 0)
                )
                change = diffusion * (
                    right_cells + left_cells + upper_rows + lower_rows - 4.0 * current
                )
                change = (
                    change
                    - along * (right_cells - left_cells)
                    - across * (lower_rows - upper_rows)
                )
                target_ref[tracer, :, cols] = current + step * change
            return inner

        lax.fori_loop(0, chunks, update, 0, unroll=UNROLL)

    def two_steps(number, carry):
        sweep(first_ref, second_ref)
        sweep(second_ref, first_ref)
        return carry

    total = count_ref[0]
    lax.fori_loop(0, total // 2, two_steps, 0)

    def collect(final_ref):
        def store(index, carry):
            tracer = index // chunks
            cols = chunk_at(index % chunks)
            out_ref[tracer, :, cols] = jnp.sum(final_ref[tracer, :, cols], axis=0, keepdims=True)
            return carry

        lax.fori_loop(0, tracers * chunks, store, 0)

    @pl.when(total % 2 == 1)
    def _():
        sweep(first_ref, second_ref)
        collect(second_ref)

    @pl.when(total % 2 == 0)
    def _():
        collect(first_ref)


def solve_rows(field, above_row, below_row, substeps, kappa_row, drift_row, kappa_col, drift_col):
    tracers, rows, width = field.shape
    step = (window_time / substeps.astype(jnp.float32)).reshape(1)
    kappa_col = kappa_col.astype(jnp.float32)
    drift_col = drift_col.astype(jnp.float32)
    coefficients = jnp.stack(
        [
            kappa_row[:, None] * kappa_col[None, :],
            0.5 * (drift_row[0][:, None] * drift_col[0][None, :]),
            0.5 * (drift_row[1][:, None] * drift_col[1][None, :]),
        ]
    )
    smem = pl.BlockSpec(memory_space=pltpu.SMEM)
    vmem = pl.BlockSpec(memory_space=pltpu.VMEM)
    return pl.pallas_call(
        solve_kernel,
        out_shape=jax.ShapeDtypeStruct((tracers, 1, width), jnp.float32),
        in_specs=[smem, smem] + [vmem] * 4,
        out_specs=vmem,
        scratch_shapes=[
            pltpu.VMEM((tracers, rows, width), jnp.float32),
            pltpu.VMEM((tracers, rows, width), jnp.float32),
        ],
        compiler_params=pltpu.CompilerParams(vmem_limit_bytes=56 * 1024 * 1024),
    )(
        step,
        substeps.reshape(1),
        field,
        above_row,
        below_row,
        coefficients,
    )


def coarsen(stepped):
    return stepped.reshape(C, FACTOR, SW, FACTOR).mean(axis=(1, 3))


def column_table():
    columns = jnp.arange(SW, dtype=jnp.int32)
    orders = jnp.arange(MODES, dtype=jnp.int32)
    phase_angle = 2.0 * math.pi / SW * (columns[:, None] * orders[None, :] % SW).astype(jnp.float32)
    return jnp.concatenate([jnp.cos(phase_angle), -jnp.sin(phase_angle)], axis=1).astype(
        jnp.bfloat16
    )


def inverse_table():
    columns = jnp.arange(SW, dtype=jnp.int32)
    orders = jnp.arange(MODES, dtype=jnp.int32)
    phase_angle = 2.0 * math.pi / SW * (orders[:, None] * columns[None, :] % SW).astype(jnp.float32)
    weights = jnp.where(orders == 0, 1.0, 2.0).astype(jnp.float32)[:, None]
    return jnp.concatenate(
        [weights * jnp.cos(phase_angle), -weights * jnp.sin(phase_angle)], axis=0
    )


def row_tables(row_ids, total_rows):
    orders = jnp.arange(2 * MODES, dtype=jnp.int32)
    wave_numbers = jnp.where(orders < MODES, orders, total_rows - 2 * MODES + orders)
    phase_angle = (
        2.0
        * math.pi
        / total_rows
        * (wave_numbers[:, None] * row_ids[None, :] % total_rows).astype(jnp.float32)
    )
    return (jnp.cos(phase_angle), jnp.sin(phase_angle))


def rows_forward(part_real, part_imag, cosine_table, sine_table):
    highest = lax.Precision.HIGHEST
    real_part = jnp.einsum("jy,yhl->hjl", cosine_table, part_real, precision=highest) + jnp.einsum(
        "jy,yhl->hjl", sine_table, part_imag, precision=highest
    )
    imag_part = jnp.einsum("jy,yhl->hjl", cosine_table, part_imag, precision=highest) - jnp.einsum(
        "jy,yhl->hjl", sine_table, part_real, precision=highest
    )
    return (real_part, imag_part)


def rows_inverse(mixed_real, mixed_imag, cosine_table, sine_table):
    highest = lax.Precision.HIGHEST
    rows_real = jnp.einsum("jy,ojl->yol", cosine_table, mixed_real, precision=highest) - jnp.einsum(
        "jy,ojl->yol", sine_table, mixed_imag, precision=highest
    )
    rows_imag = jnp.einsum("jy,ojl->yol", sine_table, mixed_real, precision=highest) + jnp.einsum(
        "jy,ojl->yol", cosine_table, mixed_imag, precision=highest
    )
    return jnp.concatenate([rows_real, rows_imag], axis=2)


def mix_modes(spectral, mode_real, mode_imag):
    real_weight, imag_weight = spectral[0], spectral[1]
    mode_real = mode_real[:, None]
    mode_imag = mode_imag[:, None]
    mixed_real = jnp.sum(real_weight * mode_real - imag_weight * mode_imag, axis=0)
    mixed_imag = jnp.sum(real_weight * mode_imag + imag_weight * mode_real, axis=0)
    return (mixed_real, mixed_imag)


def gelu_slope(pre_act):
    normal_cdf = 0.5 * (1.0 + lax.erf(pre_act * (1.0 / math.sqrt(2.0))))
    density = jnp.exp(-0.5 * pre_act * pre_act) * (1.0 / math.sqrt(2.0 * math.pi))
    return normal_cdf + pre_act * density


def weight_grads(back_real, back_imag, mode_real, mode_imag):
    highest = lax.Precision.HIGHEST
    grad_real = jnp.einsum("ojl,hjl->hojl", back_real, mode_real, precision=highest) + jnp.einsum(
        "ojl,hjl->hojl", back_imag, mode_imag, precision=highest
    )
    grad_imag = jnp.einsum("ojl,hjl->hojl", back_imag, mode_real, precision=highest) - jnp.einsum(
        "ojl,hjl->hojl", back_real, mode_imag, precision=highest
    )
    return jnp.stack([grad_real, grad_imag])


def lift_rows(sample, lift_weight, lift_bias):
    lifted = jnp.einsum("ycx,ch->yhx", sample, lift_weight, preferred_element_type=jnp.float32)
    return (lifted + lift_bias[None, :, None]).astype(jnp.bfloat16)


def gather_along(block, axis):
    count = lax.axis_size(axis)
    index = lax.axis_index(axis)
    gathered = jnp.zeros((count,) + block.shape, block.dtype)
    for shift in range(count):
        if shift == 0:
            piece = block
        else:
            piece = lax.ppermute(block, axis, [(i, (i + shift) % count) for i in range(count)])
        gathered = lax.dynamic_update_index_in_dim(gathered, piece, (index - shift) % count, 0)
    return gathered


def gather_rows(block, axes):
    for axis in reversed(axes):
        block = gather_along(block, axis)
    return block.reshape((-1,) + block.shape[len(axes):])


def packed_ppermute(parts, axis, perm):
    packed = lax.ppermute(jnp.concatenate(parts, axis=0), axis, perm)
    result = []
    offset = 0
    for part in parts:
        result.append(lax.slice_in_dim(packed, offset, offset + part.shape[0], axis=0))
        offset += part.shape[0]
    return tuple(result)


def pair_sum(values, axis):
    if lax.axis_size(axis) != 2:
        return lax.psum(values, axis)
    other = packed_ppermute(values, axis, [(0, 1), (1, 0)])
    return tuple(mine + theirs for mine, theirs in zip(values, other))


def group_grads(back_real, back_imag, mode_real, mode_imag, axis):
    count = lax.axis_size(axis)
    index = lax.axis_index(axis)
    block = mode_real.shape[1] // count
    total = None
    for shift in range(count):
        target = (index + shift) % count
        piece = tuple(
            lax.dynamic_slice_in_dim(part, target * block, block, 1)
            for part in (back_real, back_imag, mode_real, mode_imag)
        )
        if shift:
            piece = packed_ppermute(piece, axis, [(i, (i + shift) % count) for i in range(count)])
        term = weight_grads(*piece)
        total = term if total is None else total + term
    return total


def body(
    field,
    counts,
    kappa_rows,
    kappa_cols,
    drift_rows,
    drift_cols,
    assign,
    buffer,
    lift_weight,
    lift_bias,
    point_weight,
    point_bias,
    spectral_weight,
    cotangent,
):
    above_row, below_row = halo_rows(field, ("grp", "mem", "row"))
    row_sums = solve_rows(
        field,
        above_row,
        below_row,
        counts[0],
        kappa_rows,
        drift_rows,
        kappa_cols,
        drift_cols,
    )
    coarse_rows = (row_sums.reshape(C, SW, FACTOR).sum(axis=2) * (1.0 / (FACTOR * FACTOR)))[None]
    coarse_low = coarse_rows.astype(jnp.bfloat16)
    member = lax.axis_index("mem")
    member_rows = buffer.shape[1]
    total_rows = member_rows * lax.axis_size("mem")
    row_ids = member * member_rows + jnp.arange(member_rows, dtype=jnp.int32)
    owners = lax.dynamic_slice_in_dim(assign, member * member_rows, member_rows, 0)
    chosen = (owners == lax.axis_index("grp"))[:, None, None]
    forward_table = column_table()
    every_row = gather_rows(coarse_low[0], ("grp", "mem", "row"))
    fresh_rows = lax.dynamic_slice_in_dim(every_row, member * member_rows, member_rows, 0)
    sample = jnp.where(chosen, fresh_rows, buffer[0])
    hidden = lift_rows(sample, lift_weight, lift_bias)
    column_part = jnp.einsum(
        "yhx,xk->yhk", hidden, forward_table, preferred_element_type=jnp.float32
    )
    norm_scale = 1.0 / math.sqrt(total_rows * SW)
    cosine_table, sine_table = row_tables(row_ids, total_rows)
    part_real, part_imag = rows_forward(
        column_part[:, :, :MODES], column_part[:, :, MODES:], cosine_table, sine_table
    )
    mode_real, mode_imag = pair_sum((part_real * norm_scale, part_imag * norm_scale), "mem")
    mixed_real, mixed_imag = mix_modes(spectral_weight, mode_real, mode_imag)
    spatial = (
        jnp.einsum(
            "yok,kx->yox",
            rows_inverse(mixed_real, mixed_imag, cosine_table, sine_table),
            inverse_table(),
            precision=lax.Precision.HIGHEST,
        )
        * norm_scale
    )
    pre_act = (
        spatial
        + jnp.einsum("yhx,ho->yox", hidden, point_weight, preferred_element_type=jnp.float32)
        + point_bias[None, :, None]
    )
    layer_rows = jax.nn.gelu(pre_act, approximate=False).astype(jnp.bfloat16)[None]
    back_signal = (cotangent[0].astype(jnp.float32) * gelu_slope(pre_act)).astype(jnp.bfloat16)
    back_part = jnp.einsum(
        "yox,xk->yok", back_signal, forward_table, preferred_element_type=jnp.float32
    )
    back_real, back_imag = rows_forward(
        back_part[:, :, :MODES], back_part[:, :, MODES:], cosine_table, sine_table
    )
    weights_mode = jnp.where(jnp.arange(MODES) == 0, 1.0, 2.0).astype(jnp.float32) * norm_scale
    back_real, back_imag = pair_sum((back_real * weights_mode, back_imag * weights_mode), "mem")
    block_size = HID // lax.axis_size("mem")
    block_real = lax.dynamic_slice_in_dim(mode_real, member * block_size, block_size, 0)
    block_imag = lax.dynamic_slice_in_dim(mode_imag, member * block_size, block_size, 0)
    summed = group_grads(back_real, back_imag, block_real, block_imag, "grp")
    return (coarse_rows, layer_rows, summed / lax.axis_size("grp"))


def solution(mesh):
    in_specs = (
        P(None, ("grp", "mem", "row"), None),
        P(("grp", "mem", "row")),
        P(("grp", "mem", "row")),
        P(),
        P(None, ("grp", "mem", "row")),
        P(),
        P(),
        P("grp", "mem", None, None),
        P(),
        P(),
        P(None, "row"),
        P("row"),
        P(None, None, "row", None, None),
        P("grp", "mem", "row", None),
    )
    out_specs = (
        P(("grp", "mem", "row"), None, None),
        P("grp", "mem", "row", None),
        P(None, "mem", "row", "grp", None),
    )
    return jax.shard_map(body, mesh=mesh, in_specs=in_specs, out_specs=out_specs, check_vma=False)
```

```python
import math

import jax
import jax.numpy as jnp
from jax import lax
from jax.experimental import pallas as pl
from jax.experimental.pallas import tpu as pltpu
from jax.sharding import PartitionSpec as P

C = 4
SW = 1024
FACTOR = 16
HID = 32
MODES = 16


window_time = 0.24


def with_halo(block, sides, width):
    for axis, dim in sides:
        count = lax.axis_size(axis)
        forward = [(i, i + 1) for i in range(count - 1)]
        forward.append((count - 1, 0))
        backward = [(target, source) for source, target in forward]
        low = lax.ppermute(
            lax.slice_in_dim(block, block.shape[dim] - width, None, axis=dim), axis, forward
        )
        high = lax.ppermute(lax.slice_in_dim(block, 0, width, axis=dim), axis, backward)
        block = jnp.concatenate([low, block, high], axis=dim)
    return block


def halo_rows(block, axis):
    count = lax.axis_size(axis)
    forward = [(i, (i + 1) % count) for i in range(count)]
    backward = [((i + 1) % count, i) for i in range(count)]
    above = lax.ppermute(block[:, -1:], axis, forward)
    below = lax.ppermute(block[:, :1], axis, backward)
    return above, below


def slab_solve(
    slab_rows, above_row, below_row, substeps, kappa_row, drift_row, kappa_col, drift_col
):
    diffusion = kappa_row[:, None] * kappa_col[None, :]
    drift_along = drift_row[0][:, None] * drift_col[0][None, :]
    drift_across = drift_row[1][:, None] * drift_col[1][None, :]
    step_size = window_time / substeps.astype(jnp.float32)

    def advance(number, current):
        stacked = jnp.concatenate([above_row, current, below_row], axis=1)
        upper_rows = stacked[:, :-2]
        lower_rows = stacked[:, 2:]
        right_cells = jnp.roll(current, -1, axis=2)
        left_cells = jnp.roll(current, 1, axis=2)
        change = diffusion * (right_cells + left_cells + upper_rows + lower_rows - 4.0 * current)
        change = (
            change
            - 0.5 * drift_along * (right_cells - left_cells)
            - 0.5 * drift_across * (lower_rows - upper_rows)
        )
        return current + step_size * change

    return lax.fori_loop(jnp.zeros((), jnp.int32), substeps, advance, slab_rows)


CHUNK = 2048
UNROLL = 8


def solve_kernel(
    step_ref, count_ref, field_ref, above_ref, below_ref, coef_ref, out_ref, first_ref, second_ref
):
    tracers, rows, width = field_ref.shape
    chunks = width // CHUNK

    def chunk_at(index):
        return pl.ds(pl.multiple_of(index * CHUNK, CHUNK), CHUNK)

    def prepare(index, carry):
        cols = chunk_at(index)
        for tracer in range(tracers):
            first_ref[tracer, :, cols] = field_ref[tracer, :, cols].astype(jnp.float32)
        return carry

    lax.fori_loop(0, chunks, prepare, 0, unroll=UNROLL)
    row_ids = lax.broadcasted_iota(jnp.int32, (rows, CHUNK), 0)

    def sweep(source_ref, target_ref):
        def update(column, inner):
            cols = chunk_at(column)
            before = pl.ds(pl.multiple_of(((column * CHUNK - 128) % width), 128), 128)
            after = pl.ds(pl.multiple_of((((column + 1) * CHUNK) % width), 128), 128)
            diffusion = coef_ref[0, :, cols]
            along = coef_ref[1, :, cols]
            across = coef_ref[2, :, cols]
            for tracer in range(tracers):
                current = source_ref[tracer, :, cols]
                extended = jnp.concatenate(
                    [source_ref[tracer, :, before], current, source_ref[tracer, :, after]], axis=1
                )
                span = CHUNK + 256
                right_cells = pltpu.roll(extended, span - 1, 1)[:, 128 : 128 + CHUNK]
                left_cells = pltpu.roll(extended, 1, 1)[:, 128 : 128 + CHUNK]
                upper_rows = jnp.where(
                    row_ids == 0, above_ref[tracer, :, cols].astype(jnp.float32), pltpu.roll(current, 1, 0)
                )
                lower_rows = jnp.where(
                    row_ids == rows - 1, below_ref[tracer, :, cols].astype(jnp.float32), pltpu.roll(current, rows - 1, 0)
                )
                change = diffusion * (
                    right_cells + left_cells + upper_rows + lower_rows - 4.0 * current
                )
                change = (
                    change
                    - along * (right_cells - left_cells)
                    - across * (lower_rows - upper_rows)
                )
                target_ref[tracer, :, cols] = current + change
            return inner

        lax.fori_loop(0, chunks, update, 0, unroll=UNROLL)

    def two_steps(number, carry):
        sweep(first_ref, second_ref)
        sweep(second_ref, first_ref)
        return carry

    total = count_ref[0]
    lax.fori_loop(0, total // 2, two_steps, 0)

    def collect(final_ref):
        def store(index, carry):
            tracer = index // chunks
            cols = chunk_at(index % chunks)
            out_ref[tracer, :, cols] = jnp.sum(final_ref[tracer, :, cols], axis=0, keepdims=True)
            return carry

        lax.fori_loop(0, tracers * chunks, store, 0, unroll=UNROLL)

    @pl.when(total % 2 == 1)
    def _():
        sweep(first_ref, second_ref)
        collect(second_ref)

    @pl.when(total % 2 == 0)
    def _():
        collect(first_ref)


def solve_rows(field, above_row, below_row, substeps, kappa_row, drift_row, kappa_col, drift_col):
    tracers, rows, width = field.shape
    step = (window_time / substeps.astype(jnp.float32)).reshape(1)
    kappa_col = kappa_col.astype(jnp.float32)
    drift_col = drift_col.astype(jnp.float32)
    coefficients = step * jnp.stack(
        [
            kappa_row[:, None] * kappa_col[None, :],
            0.5 * (drift_row[0][:, None] * drift_col[0][None, :]),
            0.5 * (drift_row[1][:, None] * drift_col[1][None, :]),
        ]
    )
    smem = pl.BlockSpec(memory_space=pltpu.SMEM)
    vmem = pl.BlockSpec(memory_space=pltpu.VMEM)
    return pl.pallas_call(
        solve_kernel,
        out_shape=jax.ShapeDtypeStruct((tracers, 1, width), jnp.float32),
        in_specs=[smem, smem] + [vmem] * 4,
        out_specs=vmem,
        scratch_shapes=[
            pltpu.VMEM((tracers, rows, width), jnp.float32),
            pltpu.VMEM((tracers, rows, width), jnp.float32),
        ],
        compiler_params=pltpu.CompilerParams(vmem_limit_bytes=56 * 1024 * 1024),
    )(
        step,
        substeps.reshape(1),
        field,
        above_row,
        below_row,
        coefficients,
    )


def coarsen(stepped):
    return stepped.reshape(C, FACTOR, SW, FACTOR).mean(axis=(1, 3))


def column_table():
    columns = jnp.arange(SW, dtype=jnp.int32)
    orders = jnp.arange(MODES, dtype=jnp.int32)
    phase_angle = 2.0 * math.pi / SW * (columns[:, None] * orders[None, :] % SW).astype(jnp.float32)
    return jnp.concatenate([jnp.cos(phase_angle), -jnp.sin(phase_angle)], axis=1).astype(
        jnp.bfloat16
    )


def inverse_table():
    columns = jnp.arange(SW, dtype=jnp.int32)
    orders = jnp.arange(MODES, dtype=jnp.int32)
    phase_angle = 2.0 * math.pi / SW * (orders[:, None] * columns[None, :] % SW).astype(jnp.float32)
    weights = jnp.where(orders == 0, 1.0, 2.0).astype(jnp.float32)[:, None]
    return jnp.concatenate(
        [weights * jnp.cos(phase_angle), -weights * jnp.sin(phase_angle)], axis=0
    )


def row_tables(row_ids, total_rows):
    orders = jnp.arange(2 * MODES, dtype=jnp.int32)
    wave_numbers = jnp.where(orders < MODES, orders, total_rows - 2 * MODES + orders)
    phase_angle = (
        2.0
        * math.pi
        / total_rows
        * (wave_numbers[:, None] * row_ids[None, :] % total_rows).astype(jnp.float32)
    )
    return (jnp.cos(phase_angle), jnp.sin(phase_angle))


def rows_forward(part_real, part_imag, cosine_table, sine_table):
    highest = lax.Precision.HIGHEST
    real_part = jnp.einsum("jy,yhl->hjl", cosine_table, part_real, precision=highest) + jnp.einsum(
        "jy,yhl->hjl", sine_table, part_imag, precision=highest
    )
    imag_part = jnp.einsum("jy,yhl->hjl", cosine_table, part_imag, precision=highest) - jnp.einsum(
        "jy,yhl->hjl", sine_table, part_real, precision=highest
    )
    return (real_part, imag_part)


def rows_inverse(mixed_real, mixed_imag, cosine_table, sine_table):
    highest = lax.Precision.HIGHEST
    rows_real = jnp.einsum("jy,ojl->yol", cosine_table, mixed_real, precision=highest) - jnp.einsum(
        "jy,ojl->yol", sine_table, mixed_imag, precision=highest
    )
    rows_imag = jnp.einsum("jy,ojl->yol", sine_table, mixed_real, precision=highest) + jnp.einsum(
        "jy,ojl->yol", cosine_table, mixed_imag, precision=highest
    )
    return jnp.concatenate([rows_real, rows_imag], axis=2)


def mix_modes(spectral, mode_real, mode_imag):
    real_weight, imag_weight = spectral[0], spectral[1]
    mode_real = mode_real[:, None]
    mode_imag = mode_imag[:, None]
    mixed_real = jnp.sum(real_weight * mode_real - imag_weight * mode_imag, axis=0)
    mixed_imag = jnp.sum(real_weight * mode_imag + imag_weight * mode_real, axis=0)
    return (mixed_real, mixed_imag)


def gelu_slope(pre_act):
    normal_cdf = 0.5 * (1.0 + lax.erf(pre_act * (1.0 / math.sqrt(2.0))))
    density = jnp.exp(-0.5 * pre_act * pre_act) * (1.0 / math.sqrt(2.0 * math.pi))
    return normal_cdf + pre_act * density


def weight_grads(back_real, back_imag, mode_real, mode_imag):
    highest = lax.Precision.HIGHEST
    grad_real = jnp.einsum("ojl,hjl->hojl", back_real, mode_real, precision=highest) + jnp.einsum(
        "ojl,hjl->hojl", back_imag, mode_imag, precision=highest
    )
    grad_imag = jnp.einsum("ojl,hjl->hojl", back_imag, mode_real, precision=highest) - jnp.einsum(
        "ojl,hjl->hojl", back_real, mode_imag, precision=highest
    )
    return jnp.stack([grad_real, grad_imag])


def lift_rows(sample, lift_weight, lift_bias):
    lifted = jnp.einsum("ycx,ch->yhx", sample, lift_weight, preferred_element_type=jnp.float32)
    return (lifted + lift_bias[None, :, None]).astype(jnp.bfloat16)


def gather_along(block, axis):
    count = lax.axis_size(axis)
    index = lax.axis_index(axis)
    gathered = jnp.zeros((count,) + block.shape, block.dtype)
    for shift in range(count):
        if shift == 0:
            piece = block
        else:
            piece = lax.ppermute(block, axis, [(i, (i + shift) % count) for i in range(count)])
        gathered = lax.dynamic_update_index_in_dim(gathered, piece, (index - shift) % count, 0)
    return gathered


def gather_rows(block, axes):
    for axis in reversed(axes):
        block = gather_along(block, axis)
    return block.reshape((-1,) + block.shape[len(axes):])


def packed_ppermute(parts, axis, perm):
    packed = lax.ppermute(jnp.concatenate(parts, axis=0), axis, perm)
    result = []
    offset = 0
    for part in parts:
        result.append(lax.slice_in_dim(packed, offset, offset + part.shape[0], axis=0))
        offset += part.shape[0]
    return tuple(result)


def pair_sum(values, axis):
    if lax.axis_size(axis) != 2:
        return lax.psum(values, axis)
    other = packed_ppermute(values, axis, [(0, 1), (1, 0)])
    return tuple(mine + theirs for mine, theirs in zip(values, other))


def group_grads(back_real, back_imag, mode_real, mode_imag, axis):
    count = lax.axis_size(axis)
    index = lax.axis_index(axis)
    block = mode_real.shape[1] // count
    total = None
    for shift in range(count):
        target = (index + shift) % count
        piece = tuple(
            lax.dynamic_slice_in_dim(part, target * block, block, 1)
            for part in (back_real, back_imag, mode_real, mode_imag)
        )
        if shift:
            piece = packed_ppermute(piece, axis, [(i, (i + shift) % count) for i in range(count)])
        term = weight_grads(*piece)
        total = term if total is None else total + term
    return total


def body(
    field,
    counts,
    kappa_rows,
    kappa_cols,
    drift_rows,
    drift_cols,
    assign,
    buffer,
    lift_weight,
    lift_bias,
    point_weight,
    point_bias,
    spectral_weight,
    cotangent,
):
    above_row, below_row = halo_rows(field, ("grp", "mem", "row"))
    row_sums = solve_rows(
        field,
        above_row,
        below_row,
        counts[0],
        kappa_rows,
        drift_rows,
        kappa_cols,
        drift_cols,
    )
    coarse_rows = (row_sums.reshape(C, SW, FACTOR).sum(axis=2) * (1.0 / (FACTOR * FACTOR)))[None]
    coarse_low = coarse_rows.astype(jnp.bfloat16)
    member = lax.axis_index("mem")
    member_rows = buffer.shape[1]
    total_rows = member_rows * lax.axis_size("mem")
    row_ids = member * member_rows + jnp.arange(member_rows, dtype=jnp.int32)
    owners = lax.dynamic_slice_in_dim(assign, member * member_rows, member_rows, 0)
    chosen = (owners == lax.axis_index("grp"))[:, None, None]
    forward_table = column_table()
    every_row = gather_rows(coarse_low[0], ("grp", "mem", "row"))
    fresh_rows = lax.dynamic_slice_in_dim(every_row, member * member_rows, member_rows, 0)
    sample = jnp.where(chosen, fresh_rows, buffer[0])
    hidden = lift_rows(sample, lift_weight, lift_bias)
    column_part = jnp.einsum(
        "yhx,xk->yhk", hidden, forward_table, preferred_element_type=jnp.float32
    )
    norm_scale = 1.0 / math.sqrt(total_rows * SW)
    cosine_table, sine_table = row_tables(row_ids, total_rows)
    part_real, part_imag = rows_forward(
        column_part[:, :, :MODES], column_part[:, :, MODES:], cosine_table, sine_table
    )
    mode_real, mode_imag = pair_sum((part_real * norm_scale, part_imag * norm_scale), "mem")
    mixed_real, mixed_imag = mix_modes(spectral_weight, mode_real, mode_imag)
    spatial = (
        jnp.einsum(
            "yok,kx->yox",
            rows_inverse(mixed_real, mixed_imag, cosine_table, sine_table),
            inverse_table(),
            precision=lax.Precision.HIGHEST,
        )
        * norm_scale
    )
    pre_act = (
        spatial
        + jnp.einsum("yhx,ho->yox", hidden, point_weight, preferred_element_type=jnp.float32)
        + point_bias[None, :, None]
    )
    layer_rows = jax.nn.gelu(pre_act, approximate=False).astype(jnp.bfloat16)[None]
    back_signal = (cotangent[0].astype(jnp.float32) * gelu_slope(pre_act)).astype(jnp.bfloat16)
    back_part = jnp.einsum(
        "yox,xk->yok", back_signal, forward_table, preferred_element_type=jnp.float32
    )
    back_real, back_imag = rows_forward(
        back_part[:, :, :MODES], back_part[:, :, MODES:], cosine_table, sine_table
    )
    weights_mode = jnp.where(jnp.arange(MODES) == 0, 1.0, 2.0).astype(jnp.float32) * norm_scale
    back_real, back_imag = pair_sum((back_real * weights_mode, back_imag * weights_mode), "mem")
    block_size = HID // lax.axis_size("mem")
    block_real = lax.dynamic_slice_in_dim(mode_real, member * block_size, block_size, 0)
    block_imag = lax.dynamic_slice_in_dim(mode_imag, member * block_size, block_size, 0)
    summed = group_grads(back_real, back_imag, block_real, block_imag, "grp")
    return (coarse_rows, layer_rows, summed / lax.axis_size("grp"))


def solution(mesh):
    in_specs = (
        P(None, ("grp", "mem", "row"), None),
        P(("grp", "mem", "row")),
        P(("grp", "mem", "row")),
        P(),
        P(None, ("grp", "mem", "row")),
        P(),
        P(),
        P("grp", "mem", None, None),
        P(),
        P(),
        P(None, "row"),
        P("row"),
        P(None, None, "row", None, None),
        P("grp", "mem", "row", None),
    )
    out_specs = (
        P(("grp", "mem", "row"), None, None),
        P("grp", "mem", "row", None),
        P(None, "mem", "row", "grp", None),
    )
    return jax.shard_map(body, mesh=mesh, in_specs=in_specs, out_specs=out_specs, check_vma=False)
```

```python
import math

import jax
import jax.numpy as jnp
from jax import lax
from jax.experimental import pallas as pl
from jax.experimental.pallas import tpu as pltpu
from jax.sharding import PartitionSpec as P

C = 4
SW = 1024
FACTOR = 16
HID = 32
MODES = 16


window_time = 0.24


def with_halo(block, sides, width):
    for axis, dim in sides:
        count = lax.axis_size(axis)
        forward = [(i, i + 1) for i in range(count - 1)]
        forward.append((count - 1, 0))
        backward = [(target, source) for source, target in forward]
        low = lax.ppermute(
            lax.slice_in_dim(block, block.shape[dim] - width, None, axis=dim), axis, forward
        )
        high = lax.ppermute(lax.slice_in_dim(block, 0, width, axis=dim), axis, backward)
        block = jnp.concatenate([low, block, high], axis=dim)
    return block


def halo_rows(block, axis):
    count = lax.axis_size(axis)
    forward = [(i, (i + 1) % count) for i in range(count)]
    backward = [((i + 1) % count, i) for i in range(count)]
    above = lax.ppermute(block[:, -1:], axis, forward)
    below = lax.ppermute(block[:, :1], axis, backward)
    return above, below


def slab_solve(
    slab_rows, above_row, below_row, substeps, kappa_row, drift_row, kappa_col, drift_col
):
    diffusion = kappa_row[:, None] * kappa_col[None, :]
    drift_along = drift_row[0][:, None] * drift_col[0][None, :]
    drift_across = drift_row[1][:, None] * drift_col[1][None, :]
    step_size = window_time / substeps.astype(jnp.float32)

    def advance(number, current):
        stacked = jnp.concatenate([above_row, current, below_row], axis=1)
        upper_rows = stacked[:, :-2]
        lower_rows = stacked[:, 2:]
        right_cells = jnp.roll(current, -1, axis=2)
        left_cells = jnp.roll(current, 1, axis=2)
        change = diffusion * (right_cells + left_cells + upper_rows + lower_rows - 4.0 * current)
        change = (
            change
            - 0.5 * drift_along * (right_cells - left_cells)
            - 0.5 * drift_across * (lower_rows - upper_rows)
        )
        return current + step_size * change

    return lax.fori_loop(jnp.zeros((), jnp.int32), substeps, advance, slab_rows)


CHUNK = 2048
UNROLL = 8


def solve_kernel(
    step_ref, count_ref, field_ref, above_ref, below_ref, coef_ref, out_ref, first_ref, second_ref
):
    tracers, rows, width = field_ref.shape
    chunks = width // CHUNK

    def chunk_at(index):
        return pl.ds(pl.multiple_of(index * CHUNK, CHUNK), CHUNK)

    def prepare(index, carry):
        cols = chunk_at(index)
        for tracer in range(tracers):
            first_ref[tracer, :, cols] = field_ref[tracer, :, cols].astype(jnp.float32)
        return carry

    lax.fori_loop(0, chunks, prepare, 0, unroll=UNROLL)
    row_ids = lax.broadcasted_iota(jnp.int32, (rows, CHUNK), 0)

    def sweep(source_ref, target_ref):
        def update(column, inner):
            cols = chunk_at(column)
            before = pl.ds(pl.multiple_of(((column * CHUNK - 128) % width), 128), 128)
            after = pl.ds(pl.multiple_of((((column + 1) * CHUNK) % width), 128), 128)
            diffusion = coef_ref[0, :, cols]
            along = coef_ref[1, :, cols]
            across = coef_ref[2, :, cols]
            for tracer in range(tracers):
                current = source_ref[tracer, :, cols]
                extended = jnp.concatenate(
                    [source_ref[tracer, :, before], current, source_ref[tracer, :, after]], axis=1
                )
                span = CHUNK + 256
                right_cells = pltpu.roll(extended, span - 1, 1)[:, 128 : 128 + CHUNK]
                left_cells = pltpu.roll(extended, 1, 1)[:, 128 : 128 + CHUNK]
                upper_rows = jnp.where(
                    row_ids == 0, above_ref[tracer, :, cols].astype(jnp.float32), pltpu.roll(current, 1, 0)
                )
                lower_rows = jnp.where(
                    row_ids == rows - 1, below_ref[tracer, :, cols].astype(jnp.float32), pltpu.roll(current, rows - 1, 0)
                )
                change = diffusion * (
                    right_cells + left_cells + upper_rows + lower_rows - 4.0 * current
                )
                change = (
                    change
                    - along * (right_cells - left_cells)
                    - across * (lower_rows - upper_rows)
                )
                target_ref[tracer, :, cols] = current + change
            return inner

        lax.fori_loop(0, chunks, update, 0, unroll=UNROLL)

    def two_steps(number, carry):
        sweep(first_ref, second_ref)
        sweep(second_ref, first_ref)
        return carry

    total = count_ref[0]
    lax.fori_loop(0, total // 2, two_steps, 0)

    def collect(final_ref):
        def store(index, carry):
            cols = chunk_at(index)
            for tracer in range(tracers):
                out_ref[tracer : tracer + 1, cols] = jnp.sum(
                    final_ref[tracer, :, cols], axis=0, keepdims=True
                )
            return carry

        lax.fori_loop(0, chunks, store, 0, unroll=UNROLL)

    @pl.when(total % 2 == 1)
    def _():
        sweep(first_ref, second_ref)
        collect(second_ref)

    @pl.when(total % 2 == 0)
    def _():
        collect(first_ref)


def solve_rows(field, above_row, below_row, substeps, kappa_row, drift_row, kappa_col, drift_col):
    tracers, rows, width = field.shape
    step = (window_time / substeps.astype(jnp.float32)).reshape(1)
    kappa_col = kappa_col.astype(jnp.float32)
    drift_col = drift_col.astype(jnp.float32)
    coefficients = step * jnp.stack(
        [
            kappa_row[:, None] * kappa_col[None, :],
            0.5 * (drift_row[0][:, None] * drift_col[0][None, :]),
            0.5 * (drift_row[1][:, None] * drift_col[1][None, :]),
        ]
    )
    smem = pl.BlockSpec(memory_space=pltpu.SMEM)
    vmem = pl.BlockSpec(memory_space=pltpu.VMEM)
    return pl.pallas_call(
        solve_kernel,
        out_shape=jax.ShapeDtypeStruct((tracers, width), jnp.float32),
        in_specs=[smem, smem] + [vmem] * 4,
        out_specs=vmem,
        scratch_shapes=[
            pltpu.VMEM((tracers, rows, width), jnp.float32),
            pltpu.VMEM((tracers, rows, width), jnp.float32),
        ],
        compiler_params=pltpu.CompilerParams(vmem_limit_bytes=56 * 1024 * 1024),
    )(
        step,
        substeps.reshape(1),
        field,
        above_row,
        below_row,
        coefficients,
    )


def coarsen(stepped):
    return stepped.reshape(C, FACTOR, SW, FACTOR).mean(axis=(1, 3))


def column_table():
    columns = jnp.arange(SW, dtype=jnp.int32)
    orders = jnp.arange(MODES, dtype=jnp.int32)
    phase_angle = 2.0 * math.pi / SW * (columns[:, None] * orders[None, :] % SW).astype(jnp.float32)
    return jnp.concatenate([jnp.cos(phase_angle), -jnp.sin(phase_angle)], axis=1).astype(
        jnp.bfloat16
    )


def inverse_table():
    columns = jnp.arange(SW, dtype=jnp.int32)
    orders = jnp.arange(MODES, dtype=jnp.int32)
    phase_angle = 2.0 * math.pi / SW * (orders[:, None] * columns[None, :] % SW).astype(jnp.float32)
    weights = jnp.where(orders == 0, 1.0, 2.0).astype(jnp.float32)[:, None]
    return jnp.concatenate(
        [weights * jnp.cos(phase_angle), -weights * jnp.sin(phase_angle)], axis=0
    )


def row_tables(row_ids, total_rows):
    orders = jnp.arange(2 * MODES, dtype=jnp.int32)
    wave_numbers = jnp.where(orders < MODES, orders, total_rows - 2 * MODES + orders)
    phase_angle = (
        2.0
        * math.pi
        / total_rows
        * (wave_numbers[:, None] * row_ids[None, :] % total_rows).astype(jnp.float32)
    )
    return (jnp.cos(phase_angle), jnp.sin(phase_angle))


def rows_forward(part_real, part_imag, cosine_table, sine_table):
    highest = lax.Precision.HIGHEST
    real_part = jnp.einsum("jy,yhl->hjl", cosine_table, part_real, precision=highest) + jnp.einsum(
        "jy,yhl->hjl", sine_table, part_imag, precision=highest
    )
    imag_part = jnp.einsum("jy,yhl->hjl", cosine_table, part_imag, precision=highest) - jnp.einsum(
        "jy,yhl->hjl", sine_table, part_real, precision=highest
    )
    return (real_part, imag_part)


def rows_inverse(mixed_real, mixed_imag, cosine_table, sine_table):
    highest = lax.Precision.HIGHEST
    rows_real = jnp.einsum("jy,ojl->yol", cosine_table, mixed_real, precision=highest) - jnp.einsum(
        "jy,ojl->yol", sine_table, mixed_imag, precision=highest
    )
    rows_imag = jnp.einsum("jy,ojl->yol", sine_table, mixed_real, precision=highest) + jnp.einsum(
        "jy,ojl->yol", cosine_table, mixed_imag, precision=highest
    )
    return jnp.concatenate([rows_real, rows_imag], axis=2)


def mix_modes(spectral, mode_real, mode_imag):
    real_weight, imag_weight = spectral[0], spectral[1]
    mode_real = mode_real[:, None]
    mode_imag = mode_imag[:, None]
    mixed_real = jnp.sum(real_weight * mode_real - imag_weight * mode_imag, axis=0)
    mixed_imag = jnp.sum(real_weight * mode_imag + imag_weight * mode_real, axis=0)
    return (mixed_real, mixed_imag)


def gelu_slope(pre_act):
    normal_cdf = 0.5 * (1.0 + lax.erf(pre_act * (1.0 / math.sqrt(2.0))))
    density = jnp.exp(-0.5 * pre_act * pre_act) * (1.0 / math.sqrt(2.0 * math.pi))
    return normal_cdf + pre_act * density


def weight_grads(back_real, back_imag, mode_real, mode_imag):
    highest = lax.Precision.HIGHEST
    grad_real = jnp.einsum("ojl,hjl->hojl", back_real, mode_real, precision=highest) + jnp.einsum(
        "ojl,hjl->hojl", back_imag, mode_imag, precision=highest
    )
    grad_imag = jnp.einsum("ojl,hjl->hojl", back_imag, mode_real, precision=highest) - jnp.einsum(
        "ojl,hjl->hojl", back_real, mode_imag, precision=highest
    )
    return jnp.stack([grad_real, grad_imag])


def lift_rows(sample, lift_weight, lift_bias):
    lifted = jnp.einsum("ycx,ch->yhx", sample, lift_weight, preferred_element_type=jnp.float32)
    return (lifted + lift_bias[None, :, None]).astype(jnp.bfloat16)


def gather_along(block, axis):
    count = lax.axis_size(axis)
    index = lax.axis_index(axis)
    gathered = jnp.zeros((count,) + block.shape, block.dtype)
    for shift in range(count):
        if shift == 0:
            piece = block
        else:
            piece = lax.ppermute(block, axis, [(i, (i + shift) % count) for i in range(count)])
        gathered = lax.dynamic_update_index_in_dim(gathered, piece, (index - shift) % count, 0)
    return gathered


def gather_rows(block, axes):
    for axis in reversed(axes):
        block = gather_along(block, axis)
    return block.reshape((-1,) + block.shape[len(axes):])


def packed_ppermute(parts, axis, perm):
    packed = lax.ppermute(jnp.concatenate(parts, axis=0), axis, perm)
    result = []
    offset = 0
    for part in parts:
        result.append(lax.slice_in_dim(packed, offset, offset + part.shape[0], axis=0))
        offset += part.shape[0]
    return tuple(result)


def pair_sum(values, axis):
    if lax.axis_size(axis) != 2:
        return lax.psum(values, axis)
    other = packed_ppermute(values, axis, [(0, 1), (1, 0)])
    return tuple(mine + theirs for mine, theirs in zip(values, other))


def group_grads(back_real, back_imag, mode_real, mode_imag, axis):
    count = lax.axis_size(axis)
    index = lax.axis_index(axis)
    block = mode_real.shape[1] // count
    total = None
    for shift in range(count):
        target = (index + shift) % count
        piece = tuple(
            lax.dynamic_slice_in_dim(part, target * block, block, 1)
            for part in (back_real, back_imag, mode_real, mode_imag)
        )
        if shift:
            piece = packed_ppermute(piece, axis, [(i, (i + shift) % count) for i in range(count)])
        term = weight_grads(*piece)
        total = term if total is None else total + term
    return total


def body(
    field,
    counts,
    kappa_rows,
    kappa_cols,
    drift_rows,
    drift_cols,
    assign,
    buffer,
    lift_weight,
    lift_bias,
    point_weight,
    point_bias,
    spectral_weight,
    cotangent,
):
    above_row, below_row = halo_rows(field, ("grp", "mem", "row"))
    row_sums = solve_rows(
        field,
        above_row,
        below_row,
        counts[0],
        kappa_rows,
        drift_rows,
        kappa_cols,
        drift_cols,
    )
    coarse_rows = (row_sums.reshape(C, SW, FACTOR).sum(axis=2) * (1.0 / (FACTOR * FACTOR)))[None]
    coarse_low = coarse_rows.astype(jnp.bfloat16)
    member = lax.axis_index("mem")
    member_rows = buffer.shape[1]
    total_rows = member_rows * lax.axis_size("mem")
    row_ids = member * member_rows + jnp.arange(member_rows, dtype=jnp.int32)
    owners = lax.dynamic_slice_in_dim(assign, member * member_rows, member_rows, 0)
    chosen = (owners == lax.axis_index("grp"))[:, None, None]
    forward_table = column_table()
    every_row = gather_rows(coarse_low[0], ("grp", "mem", "row"))
    fresh_rows = lax.dynamic_slice_in_dim(every_row, member * member_rows, member_rows, 0)
    sample = jnp.where(chosen, fresh_rows, buffer[0])
    hidden = lift_rows(sample, lift_weight, lift_bias)
    column_part = jnp.einsum(
        "yhx,xk->yhk", hidden, forward_table, preferred_element_type=jnp.float32
    )
    norm_scale = 1.0 / math.sqrt(total_rows * SW)
    cosine_table, sine_table = row_tables(row_ids, total_rows)
    part_real, part_imag = rows_forward(
        column_part[:, :, :MODES], column_part[:, :, MODES:], cosine_table, sine_table
    )
    mode_real, mode_imag = pair_sum((part_real * norm_scale, part_imag * norm_scale), "mem")
    mixed_real, mixed_imag = mix_modes(spectral_weight, mode_real, mode_imag)
    spatial = (
        jnp.einsum(
            "yok,kx->yox",
            rows_inverse(mixed_real, mixed_imag, cosine_table, sine_table),
            inverse_table(),
            precision=lax.Precision.HIGHEST,
        )
        * norm_scale
    )
    pre_act = (
        spatial
        + jnp.einsum("yhx,ho->yox", hidden, point_weight, preferred_element_type=jnp.float32)
        + point_bias[None, :, None]
    )
    layer_rows = jax.nn.gelu(pre_act, approximate=False).astype(jnp.bfloat16)[None]
    back_signal = (cotangent[0].astype(jnp.float32) * gelu_slope(pre_act)).astype(jnp.bfloat16)
    back_part = jnp.einsum(
        "yox,xk->yok", back_signal, forward_table, preferred_element_type=jnp.float32
    )
    back_real, back_imag = rows_forward(
        back_part[:, :, :MODES], back_part[:, :, MODES:], cosine_table, sine_table
    )
    weights_mode = jnp.where(jnp.arange(MODES) == 0, 1.0, 2.0).astype(jnp.float32) * norm_scale
    back_real, back_imag = pair_sum((back_real * weights_mode, back_imag * weights_mode), "mem")
    block_size = HID // lax.axis_size("mem")
    block_real = lax.dynamic_slice_in_dim(mode_real, member * block_size, block_size, 0)
    block_imag = lax.dynamic_slice_in_dim(mode_imag, member * block_size, block_size, 0)
    summed = group_grads(back_real, back_imag, block_real, block_imag, "grp")
    return (coarse_rows, layer_rows, summed / lax.axis_size("grp"))


def solution(mesh):
    in_specs = (
        P(None, ("grp", "mem", "row"), None),
        P(("grp", "mem", "row")),
        P(("grp", "mem", "row")),
        P(),
        P(None, ("grp", "mem", "row")),
        P(),
        P(),
        P("grp", "mem", None, None),
        P(),
        P(),
        P(None, "row"),
        P("row"),
        P(None, None, "row", None, None),
        P("grp", "mem", "row", None),
    )
    out_specs = (
        P(("grp", "mem", "row"), None, None),
        P("grp", "mem", "row", None),
        P(None, "mem", "row", "grp", None),
    )
    return jax.shard_map(body, mesh=mesh, in_specs=in_specs, out_specs=out_specs, check_vma=False)
```

```python
import math

import jax
import jax.numpy as jnp
from jax import lax
from jax.experimental import pallas as pl
from jax.experimental.pallas import tpu as pltpu
from jax.sharding import PartitionSpec as P

C = 4
SW = 1024
FACTOR = 16
HID = 32
MODES = 16


window_time = 0.24


def with_halo(block, sides, width):
    for axis, dim in sides:
        count = lax.axis_size(axis)
        forward = [(i, i + 1) for i in range(count - 1)]
        forward.append((count - 1, 0))
        backward = [(target, source) for source, target in forward]
        low = lax.ppermute(
            lax.slice_in_dim(block, block.shape[dim] - width, None, axis=dim), axis, forward
        )
        high = lax.ppermute(lax.slice_in_dim(block, 0, width, axis=dim), axis, backward)
        block = jnp.concatenate([low, block, high], axis=dim)
    return block


def halo_rows(block, axis):
    count = lax.axis_size(axis)
    forward = [(i, (i + 1) % count) for i in range(count)]
    backward = [((i + 1) % count, i) for i in range(count)]
    above = lax.ppermute(block[:, -1:], axis, forward)
    below = lax.ppermute(block[:, :1], axis, backward)
    return above, below


def slab_solve(
    slab_rows, above_row, below_row, substeps, kappa_row, drift_row, kappa_col, drift_col
):
    diffusion = kappa_row[:, None] * kappa_col[None, :]
    drift_along = drift_row[0][:, None] * drift_col[0][None, :]
    drift_across = drift_row[1][:, None] * drift_col[1][None, :]
    step_size = window_time / substeps.astype(jnp.float32)

    def advance(number, current):
        stacked = jnp.concatenate([above_row, current, below_row], axis=1)
        upper_rows = stacked[:, :-2]
        lower_rows = stacked[:, 2:]
        right_cells = jnp.roll(current, -1, axis=2)
        left_cells = jnp.roll(current, 1, axis=2)
        change = diffusion * (right_cells + left_cells + upper_rows + lower_rows - 4.0 * current)
        change = (
            change
            - 0.5 * drift_along * (right_cells - left_cells)
            - 0.5 * drift_across * (lower_rows - upper_rows)
        )
        return current + step_size * change

    return lax.fori_loop(jnp.zeros((), jnp.int32), substeps, advance, slab_rows)


CHUNK = 2048
UNROLL = 8


def solve_kernel(
    step_ref, count_ref, field_ref, above_ref, below_ref, coef_ref, out_ref, first_ref, second_ref
):
    tracers, rows, width = field_ref.shape
    chunks = width // CHUNK

    def chunk_at(index):
        return pl.ds(pl.multiple_of(index * CHUNK, CHUNK), CHUNK)

    row_ids = lax.broadcasted_iota(jnp.int32, (rows, CHUNK), 0)

    def sweep(source_ref, target_ref):
        def update(column, inner):
            cols = chunk_at(column)
            before = pl.ds(pl.multiple_of(((column * CHUNK - 128) % width), 128), 128)
            after = pl.ds(pl.multiple_of((((column + 1) * CHUNK) % width), 128), 128)
            diffusion = coef_ref[0, :, cols]
            along = coef_ref[1, :, cols]
            across = coef_ref[2, :, cols]
            for tracer in range(tracers):
                current = source_ref[tracer, :, cols].astype(jnp.float32)
                extended = jnp.concatenate(
                    [
                        source_ref[tracer, :, before].astype(jnp.float32),
                        current,
                        source_ref[tracer, :, after].astype(jnp.float32),
                    ],
                    axis=1,
                )
                span = CHUNK + 256
                right_cells = pltpu.roll(extended, span - 1, 1)[:, 128 : 128 + CHUNK]
                left_cells = pltpu.roll(extended, 1, 1)[:, 128 : 128 + CHUNK]
                upper_rows = jnp.where(
                    row_ids == 0, above_ref[tracer, :, cols].astype(jnp.float32), pltpu.roll(current, 1, 0)
                )
                lower_rows = jnp.where(
                    row_ids == rows - 1, below_ref[tracer, :, cols].astype(jnp.float32), pltpu.roll(current, rows - 1, 0)
                )
                change = diffusion * (
                    right_cells + left_cells + upper_rows + lower_rows - 4.0 * current
                )
                change = (
                    change
                    - along * (right_cells - left_cells)
                    - across * (lower_rows - upper_rows)
                )
                target_ref[tracer, :, cols] = current + change
            return inner

        lax.fori_loop(0, chunks, update, 0, unroll=UNROLL)

    def two_steps(number, carry):
        sweep(second_ref, first_ref)
        sweep(first_ref, second_ref)
        return carry

    total = count_ref[0]
    sweep(field_ref, second_ref)
    lax.fori_loop(0, (total - 1) // 2, two_steps, 0)

    def collect(final_ref):
        def store(index, carry):
            cols = chunk_at(index)
            for tracer in range(tracers):
                out_ref[tracer : tracer + 1, cols] = jnp.sum(
                    final_ref[tracer, :, cols], axis=0, keepdims=True
                )
            return carry

        lax.fori_loop(0, chunks, store, 0, unroll=UNROLL)

    @pl.when(total % 2 == 0)
    def _():
        sweep(second_ref, first_ref)
        collect(first_ref)

    @pl.when(total % 2 == 1)
    def _():
        collect(second_ref)


def solve_rows(field, above_row, below_row, substeps, kappa_row, drift_row, kappa_col, drift_col):
    tracers, rows, width = field.shape
    step = (window_time / substeps.astype(jnp.float32)).reshape(1)
    kappa_col = kappa_col.astype(jnp.float32)
    drift_col = drift_col.astype(jnp.float32)
    coefficients = step * jnp.stack(
        [
            kappa_row[:, None] * kappa_col[None, :],
            0.5 * (drift_row[0][:, None] * drift_col[0][None, :]),
            0.5 * (drift_row[1][:, None] * drift_col[1][None, :]),
        ]
    )
    smem = pl.BlockSpec(memory_space=pltpu.SMEM)
    vmem = pl.BlockSpec(memory_space=pltpu.VMEM)
    return pl.pallas_call(
        solve_kernel,
        out_shape=jax.ShapeDtypeStruct((tracers, width), jnp.float32),
        in_specs=[smem, smem] + [vmem] * 4,
        out_specs=vmem,
        scratch_shapes=[
            pltpu.VMEM((tracers, rows, width), jnp.float32),
            pltpu.VMEM((tracers, rows, width), jnp.float32),
        ],
        compiler_params=pltpu.CompilerParams(vmem_limit_bytes=56 * 1024 * 1024),
    )(
        step,
        substeps.reshape(1),
        field,
        above_row,
        below_row,
        coefficients,
    )


def coarsen(stepped):
    return stepped.reshape(C, FACTOR, SW, FACTOR).mean(axis=(1, 3))


def column_table():
    columns = jnp.arange(SW, dtype=jnp.int32)
    orders = jnp.arange(MODES, dtype=jnp.int32)
    phase_angle = 2.0 * math.pi / SW * (columns[:, None] * orders[None, :] % SW).astype(jnp.float32)
    return jnp.concatenate([jnp.cos(phase_angle), -jnp.sin(phase_angle)], axis=1).astype(
        jnp.bfloat16
    )


def inverse_table():
    columns = jnp.arange(SW, dtype=jnp.int32)
    orders = jnp.arange(MODES, dtype=jnp.int32)
    phase_angle = 2.0 * math.pi / SW * (orders[:, None] * columns[None, :] % SW).astype(jnp.float32)
    weights = jnp.where(orders == 0, 1.0, 2.0).astype(jnp.float32)[:, None]
    return jnp.concatenate(
        [weights * jnp.cos(phase_angle), -weights * jnp.sin(phase_angle)], axis=0
    )


def row_tables(row_ids, total_rows):
    orders = jnp.arange(2 * MODES, dtype=jnp.int32)
    wave_numbers = jnp.where(orders < MODES, orders, total_rows - 2 * MODES + orders)
    phase_angle = (
        2.0
        * math.pi
        / total_rows
        * (wave_numbers[:, None] * row_ids[None, :] % total_rows).astype(jnp.float32)
    )
    return (jnp.cos(phase_angle), jnp.sin(phase_angle))


def rows_forward(part_real, part_imag, cosine_table, sine_table):
    highest = lax.Precision.HIGHEST
    real_part = jnp.einsum("jy,yhl->hjl", cosine_table, part_real, precision=highest) + jnp.einsum(
        "jy,yhl->hjl", sine_table, part_imag, precision=highest
    )
    imag_part = jnp.einsum("jy,yhl->hjl", cosine_table, part_imag, precision=highest) - jnp.einsum(
        "jy,yhl->hjl", sine_table, part_real, precision=highest
    )
    return (real_part, imag_part)


def rows_inverse(mixed_real, mixed_imag, cosine_table, sine_table):
    highest = lax.Precision.HIGHEST
    rows_real = jnp.einsum("jy,ojl->yol", cosine_table, mixed_real, precision=highest) - jnp.einsum(
        "jy,ojl->yol", sine_table, mixed_imag, precision=highest
    )
    rows_imag = jnp.einsum("jy,ojl->yol", sine_table, mixed_real, precision=highest) + jnp.einsum(
        "jy,ojl->yol", cosine_table, mixed_imag, precision=highest
    )
    return jnp.concatenate([rows_real, rows_imag], axis=2)


def mix_modes(spectral, mode_real, mode_imag):
    real_weight, imag_weight = spectral[0], spectral[1]
    mode_real = mode_real[:, None]
    mode_imag = mode_imag[:, None]
    mixed_real = jnp.sum(real_weight * mode_real - imag_weight * mode_imag, axis=0)
    mixed_imag = jnp.sum(real_weight * mode_imag + imag_weight * mode_real, axis=0)
    return (mixed_real, mixed_imag)


def gelu_slope(pre_act):
    normal_cdf = 0.5 * (1.0 + lax.erf(pre_act * (1.0 / math.sqrt(2.0))))
    density = jnp.exp(-0.5 * pre_act * pre_act) * (1.0 / math.sqrt(2.0 * math.pi))
    return normal_cdf + pre_act * density


def weight_grads(back_real, back_imag, mode_real, mode_imag):
    highest = lax.Precision.HIGHEST
    grad_real = jnp.einsum("ojl,hjl->hojl", back_real, mode_real, precision=highest) + jnp.einsum(
        "ojl,hjl->hojl", back_imag, mode_imag, precision=highest
    )
    grad_imag = jnp.einsum("ojl,hjl->hojl", back_imag, mode_real, precision=highest) - jnp.einsum(
        "ojl,hjl->hojl", back_real, mode_imag, precision=highest
    )
    return jnp.stack([grad_real, grad_imag])


def lift_rows(sample, lift_weight, lift_bias):
    lifted = jnp.einsum("ycx,ch->yhx", sample, lift_weight, preferred_element_type=jnp.float32)
    return (lifted + lift_bias[None, :, None]).astype(jnp.bfloat16)


def gather_along(block, axis):
    count = lax.axis_size(axis)
    index = lax.axis_index(axis)
    gathered = jnp.zeros((count,) + block.shape, block.dtype)
    for shift in range(count):
        if shift == 0:
            piece = block
        else:
            piece = lax.ppermute(block, axis, [(i, (i + shift) % count) for i in range(count)])
        gathered = lax.dynamic_update_index_in_dim(gathered, piece, (index - shift) % count, 0)
    return gathered


def gather_rows(block, axes):
    for axis in reversed(axes):
        block = gather_along(block, axis)
    return block.reshape((-1,) + block.shape[len(axes):])


def packed_ppermute(parts, axis, perm):
    packed = lax.ppermute(jnp.concatenate(parts, axis=0), axis, perm)
    result = []
    offset = 0
    for part in parts:
        result.append(lax.slice_in_dim(packed, offset, offset + part.shape[0], axis=0))
        offset += part.shape[0]
    return tuple(result)


def pair_sum(values, axis):
    if lax.axis_size(axis) != 2:
        return lax.psum(values, axis)
    other = packed_ppermute(values, axis, [(0, 1), (1, 0)])
    return tuple(mine + theirs for mine, theirs in zip(values, other))


def group_grads(back_real, back_imag, mode_real, mode_imag, axis):
    count = lax.axis_size(axis)
    index = lax.axis_index(axis)
    block = mode_real.shape[1] // count
    total = None
    for shift in range(count):
        target = (index + shift) % count
        piece = tuple(
            lax.dynamic_slice_in_dim(part, target * block, block, 1)
            for part in (back_real, back_imag, mode_real, mode_imag)
        )
        if shift:
            piece = packed_ppermute(piece, axis, [(i, (i + shift) % count) for i in range(count)])
        term = weight_grads(*piece)
        total = term if total is None else total + term
    return total


def body(
    field,
    counts,
    kappa_rows,
    kappa_cols,
    drift_rows,
    drift_cols,
    assign,
    buffer,
    lift_weight,
    lift_bias,
    point_weight,
    point_bias,
    spectral_weight,
    cotangent,
):
    above_row, below_row = halo_rows(field, ("grp", "mem", "row"))
    row_sums = solve_rows(
        field,
        above_row,
        below_row,
        counts[0],
        kappa_rows,
        drift_rows,
        kappa_cols,
        drift_cols,
    )
    coarse_rows = (row_sums.reshape(C, SW, FACTOR).sum(axis=2) * (1.0 / (FACTOR * FACTOR)))[None]
    coarse_low = coarse_rows.astype(jnp.bfloat16)
    member = lax.axis_index("mem")
    member_rows = buffer.shape[1]
    total_rows = member_rows * lax.axis_size("mem")
    row_ids = member * member_rows + jnp.arange(member_rows, dtype=jnp.int32)
    owners = lax.dynamic_slice_in_dim(assign, member * member_rows, member_rows, 0)
    chosen = (owners == lax.axis_index("grp"))[:, None, None]
    forward_table = column_table()
    every_row = gather_rows(coarse_low[0], ("grp", "mem", "row"))
    fresh_rows = lax.dynamic_slice_in_dim(every_row, member * member_rows, member_rows, 0)
    sample = jnp.where(chosen, fresh_rows, buffer[0])
    hidden = lift_rows(sample, lift_weight, lift_bias)
    column_part = jnp.einsum(
        "yhx,xk->yhk", hidden, forward_table, preferred_element_type=jnp.float32
    )
    norm_scale = 1.0 / math.sqrt(total_rows * SW)
    cosine_table, sine_table = row_tables(row_ids, total_rows)
    part_real, part_imag = rows_forward(
        column_part[:, :, :MODES], column_part[:, :, MODES:], cosine_table, sine_table
    )
    mode_real, mode_imag = pair_sum((part_real * norm_scale, part_imag * norm_scale), "mem")
    mixed_real, mixed_imag = mix_modes(spectral_weight, mode_real, mode_imag)
    spatial = (
        jnp.einsum(
            "yok,kx->yox",
            rows_inverse(mixed_real, mixed_imag, cosine_table, sine_table),
            inverse_table(),
            precision=lax.Precision.HIGHEST,
        )
        * norm_scale
    )
    pre_act = (
        spatial
        + jnp.einsum("yhx,ho->yox", hidden, point_weight, preferred_element_type=jnp.float32)
        + point_bias[None, :, None]
    )
    layer_rows = jax.nn.gelu(pre_act, approximate=False).astype(jnp.bfloat16)[None]
    back_signal = (cotangent[0].astype(jnp.float32) * gelu_slope(pre_act)).astype(jnp.bfloat16)
    back_part = jnp.einsum(
        "yox,xk->yok", back_signal, forward_table, preferred_element_type=jnp.float32
    )
    back_real, back_imag = rows_forward(
        back_part[:, :, :MODES], back_part[:, :, MODES:], cosine_table, sine_table
    )
    weights_mode = jnp.where(jnp.arange(MODES) == 0, 1.0, 2.0).astype(jnp.float32) * norm_scale
    back_real, back_imag = pair_sum((back_real * weights_mode, back_imag * weights_mode), "mem")
    block_size = HID // lax.axis_size("mem")
    block_real = lax.dynamic_slice_in_dim(mode_real, member * block_size, block_size, 0)
    block_imag = lax.dynamic_slice_in_dim(mode_imag, member * block_size, block_size, 0)
    summed = group_grads(back_real, back_imag, block_real, block_imag, "grp")
    return (coarse_rows, layer_rows, summed / lax.axis_size("grp"))


def solution(mesh):
    in_specs = (
        P(None, ("grp", "mem", "row"), None),
        P(("grp", "mem", "row")),
        P(("grp", "mem", "row")),
        P(),
        P(None, ("grp", "mem", "row")),
        P(),
        P(),
        P("grp", "mem", None, None),
        P(),
        P(),
        P(None, "row"),
        P("row"),
        P(None, None, "row", None, None),
        P("grp", "mem", "row", None),
    )
    out_specs = (
        P(("grp", "mem", "row"), None, None),
        P("grp", "mem", "row", None),
        P(None, "mem", "row", "grp", None),
    )
    return jax.shard_map(body, mesh=mesh, in_specs=in_specs, out_specs=out_specs, check_vma=False)
```

```python
import math

import jax
import jax.numpy as jnp
from jax import lax
from jax.experimental import pallas as pl
from jax.experimental.pallas import tpu as pltpu
from jax.sharding import PartitionSpec as P

C = 4
SW = 1024
FACTOR = 16
HID = 32
MODES = 16


window_time = 0.24


def with_halo(block, sides, width):
    for axis, dim in sides:
        count = lax.axis_size(axis)
        forward = [(i, i + 1) for i in range(count - 1)]
        forward.append((count - 1, 0))
        backward = [(target, source) for source, target in forward]
        low = lax.ppermute(
            lax.slice_in_dim(block, block.shape[dim] - width, None, axis=dim), axis, forward
        )
        high = lax.ppermute(lax.slice_in_dim(block, 0, width, axis=dim), axis, backward)
        block = jnp.concatenate([low, block, high], axis=dim)
    return block


def halo_rows(block, axis):
    count = lax.axis_size(axis)
    forward = [(i, (i + 1) % count) for i in range(count)]
    backward = [((i + 1) % count, i) for i in range(count)]
    above = lax.ppermute(block[:, -1:], axis, forward)
    below = lax.ppermute(block[:, :1], axis, backward)
    return above, below


def slab_solve(
    slab_rows, above_row, below_row, substeps, kappa_row, drift_row, kappa_col, drift_col
):
    diffusion = kappa_row[:, None] * kappa_col[None, :]
    drift_along = drift_row[0][:, None] * drift_col[0][None, :]
    drift_across = drift_row[1][:, None] * drift_col[1][None, :]
    step_size = window_time / substeps.astype(jnp.float32)

    def advance(number, current):
        stacked = jnp.concatenate([above_row, current, below_row], axis=1)
        upper_rows = stacked[:, :-2]
        lower_rows = stacked[:, 2:]
        right_cells = jnp.roll(current, -1, axis=2)
        left_cells = jnp.roll(current, 1, axis=2)
        change = diffusion * (right_cells + left_cells + upper_rows + lower_rows - 4.0 * current)
        change = (
            change
            - 0.5 * drift_along * (right_cells - left_cells)
            - 0.5 * drift_across * (lower_rows - upper_rows)
        )
        return current + step_size * change

    return lax.fori_loop(jnp.zeros((), jnp.int32), substeps, advance, slab_rows)


CHUNK = 2048
UNROLL = 8


def solve_kernel(
    step_ref, count_ref, field_ref, above_ref, below_ref, coef_ref, out_ref, first_ref, second_ref
):
    tracers, rows, width = field_ref.shape
    chunks = width // CHUNK

    def chunk_at(index):
        return pl.ds(pl.multiple_of(index * CHUNK, CHUNK), CHUNK)

    def prepare(index, carry):
        cols = chunk_at(index)
        for tracer in range(tracers):
            first_ref[tracer, :, cols] = field_ref[tracer, :, cols].astype(jnp.float32)
        return carry

    lax.fori_loop(0, chunks, prepare, 0, unroll=UNROLL)
    row_ids = lax.broadcasted_iota(jnp.int32, (rows, CHUNK), 0)

    def sweep(source_ref, target_ref):
        def update(column, inner):
            cols = chunk_at(column)
            before = pl.ds(pl.multiple_of(((column * CHUNK - 128) % width), 128), 128)
            after = pl.ds(pl.multiple_of((((column + 1) * CHUNK) % width), 128), 128)
            diffusion = coef_ref[0, :, cols]
            along = coef_ref[1, :, cols]
            across = coef_ref[2, :, cols]
            for tracer in range(tracers):
                current = source_ref[tracer, :, cols]
                extended = jnp.concatenate(
                    [source_ref[tracer, :, before], current, source_ref[tracer, :, after]], axis=1
                )
                span = CHUNK + 256
                right_cells = pltpu.roll(extended, span - 1, 1)[:, 128 : 128 + CHUNK]
                left_cells = pltpu.roll(extended, 1, 1)[:, 128 : 128 + CHUNK]
                upper_rows = jnp.where(
                    row_ids == 0, above_ref[tracer, :, cols].astype(jnp.float32), pltpu.roll(current, 1, 0)
                )
                lower_rows = jnp.where(
                    row_ids == rows - 1, below_ref[tracer, :, cols].astype(jnp.float32), pltpu.roll(current, rows - 1, 0)
                )
                change = diffusion * (
                    right_cells + left_cells + upper_rows + lower_rows - 4.0 * current
                )
                change = (
                    change
                    - along * (right_cells - left_cells)
                    - across * (lower_rows - upper_rows)
                )
                target_ref[tracer, :, cols] = current + change
            return inner

        lax.fori_loop(0, chunks, update, 0, unroll=UNROLL)

    def two_steps(number, carry):
        sweep(first_ref, second_ref)
        sweep(second_ref, first_ref)
        return carry

    total = count_ref[0]
    lax.fori_loop(0, total // 2, two_steps, 0)

    def collect(final_ref):
        def store(index, carry):
            cols = chunk_at(index)
            for tracer in range(tracers):
                out_ref[tracer : tracer + 1, cols] = jnp.sum(
                    final_ref[tracer, :, cols], axis=0, keepdims=True
                )
            return carry

        lax.fori_loop(0, chunks, store, 0, unroll=UNROLL)

    @pl.when(total % 2 == 1)
    def _():
        sweep(first_ref, second_ref)
        collect(second_ref)

    @pl.when(total % 2 == 0)
    def _():
        collect(first_ref)


def solve_rows(field, above_row, below_row, substeps, kappa_row, drift_row, kappa_col, drift_col):
    tracers, rows, width = field.shape
    step = (window_time / substeps.astype(jnp.float32)).reshape(1)
    kappa_col = kappa_col.astype(jnp.float32)
    drift_col = drift_col.astype(jnp.float32)
    coefficients = step * jnp.stack(
        [
            kappa_row[:, None] * kappa_col[None, :],
            0.5 * (drift_row[0][:, None] * drift_col[0][None, :]),
            0.5 * (drift_row[1][:, None] * drift_col[1][None, :]),
        ]
    )
    smem = pl.BlockSpec(memory_space=pltpu.SMEM)
    vmem = pl.BlockSpec(memory_space=pltpu.VMEM)
    return pl.pallas_call(
        solve_kernel,
        out_shape=jax.ShapeDtypeStruct((tracers, width), jnp.float32),
        in_specs=[smem, smem] + [vmem] * 4,
        out_specs=vmem,
        scratch_shapes=[
            pltpu.VMEM((tracers, rows, width), jnp.float32),
            pltpu.VMEM((tracers, rows, width), jnp.float32),
        ],
        compiler_params=pltpu.CompilerParams(vmem_limit_bytes=56 * 1024 * 1024),
    )(
        step,
        substeps.reshape(1),
        field,
        above_row,
        below_row,
        coefficients,
    )


def coarsen(stepped):
    return stepped.reshape(C, FACTOR, SW, FACTOR).mean(axis=(1, 3))


def column_table():
    columns = jnp.arange(SW, dtype=jnp.int32)
    orders = jnp.arange(MODES, dtype=jnp.int32)
    phase_angle = 2.0 * math.pi / SW * (columns[:, None] * orders[None, :] % SW).astype(jnp.float32)
    return jnp.concatenate([jnp.cos(phase_angle), -jnp.sin(phase_angle)], axis=1).astype(
        jnp.bfloat16
    )


def inverse_table():
    columns = jnp.arange(SW, dtype=jnp.int32)
    orders = jnp.arange(MODES, dtype=jnp.int32)
    phase_angle = 2.0 * math.pi / SW * (orders[:, None] * columns[None, :] % SW).astype(jnp.float32)
    weights = jnp.where(orders == 0, 1.0, 2.0).astype(jnp.float32)[:, None]
    return jnp.concatenate(
        [weights * jnp.cos(phase_angle), -weights * jnp.sin(phase_angle)], axis=0
    )


def row_tables(row_ids, total_rows):
    orders = jnp.arange(2 * MODES, dtype=jnp.int32)
    wave_numbers = jnp.where(orders < MODES, orders, total_rows - 2 * MODES + orders)
    phase_angle = (
        2.0
        * math.pi
        / total_rows
        * (wave_numbers[:, None] * row_ids[None, :] % total_rows).astype(jnp.float32)
    )
    return (jnp.cos(phase_angle), jnp.sin(phase_angle))


def rows_forward(part_real, part_imag, cosine_table, sine_table):
    highest = lax.Precision.HIGHEST
    real_part = jnp.einsum("jy,yhl->hjl", cosine_table, part_real, precision=highest) + jnp.einsum(
        "jy,yhl->hjl", sine_table, part_imag, precision=highest
    )
    imag_part = jnp.einsum("jy,yhl->hjl", cosine_table, part_imag, precision=highest) - jnp.einsum(
        "jy,yhl->hjl", sine_table, part_real, precision=highest
    )
    return (real_part, imag_part)


def rows_inverse(mixed_real, mixed_imag, cosine_table, sine_table):
    highest = lax.Precision.HIGHEST
    rows_real = jnp.einsum("jy,ojl->yol", cosine_table, mixed_real, precision=highest) - jnp.einsum(
        "jy,ojl->yol", sine_table, mixed_imag, precision=highest
    )
    rows_imag = jnp.einsum("jy,ojl->yol", sine_table, mixed_real, precision=highest) + jnp.einsum(
        "jy,ojl->yol", cosine_table, mixed_imag, precision=highest
    )
    return jnp.concatenate([rows_real, rows_imag], axis=2)


def mix_modes(spectral, mode_real, mode_imag):
    real_weight, imag_weight = spectral[0], spectral[1]
    mode_real = mode_real[:, None]
    mode_imag = mode_imag[:, None]
    mixed_real = jnp.sum(real_weight * mode_real - imag_weight * mode_imag, axis=0)
    mixed_imag = jnp.sum(real_weight * mode_imag + imag_weight * mode_real, axis=0)
    return (mixed_real, mixed_imag)


def gelu_slope(pre_act):
    normal_cdf = 0.5 * (1.0 + lax.erf(pre_act * (1.0 / math.sqrt(2.0))))
    density = jnp.exp(-0.5 * pre_act * pre_act) * (1.0 / math.sqrt(2.0 * math.pi))
    return normal_cdf + pre_act * density


def weight_grads(back_real, back_imag, mode_real, mode_imag):
    highest = lax.Precision.HIGHEST
    grad_real = jnp.einsum("ojl,hjl->hojl", back_real, mode_real, precision=highest) + jnp.einsum(
        "ojl,hjl->hojl", back_imag, mode_imag, precision=highest
    )
    grad_imag = jnp.einsum("ojl,hjl->hojl", back_imag, mode_real, precision=highest) - jnp.einsum(
        "ojl,hjl->hojl", back_real, mode_imag, precision=highest
    )
    return jnp.stack([grad_real, grad_imag])


def lift_rows(sample, lift_weight, lift_bias):
    lifted = jnp.einsum("ycx,ch->yhx", sample, lift_weight, preferred_element_type=jnp.float32)
    return (lifted + lift_bias[None, :, None]).astype(jnp.bfloat16)


def gather_along(block, axis):
    count = lax.axis_size(axis)
    index = lax.axis_index(axis)
    gathered = jnp.zeros((count,) + block.shape, block.dtype)
    for shift in range(count):
        if shift == 0:
            piece = block
        else:
            piece = lax.ppermute(block, axis, [(i, (i + shift) % count) for i in range(count)])
        gathered = lax.dynamic_update_index_in_dim(gathered, piece, (index - shift) % count, 0)
    return gathered


def gather_rows(block, axes):
    for axis in reversed(axes):
        block = gather_along(block, axis)
    return block.reshape((-1,) + block.shape[len(axes):])


def packed_ppermute(parts, axis, perm):
    packed = lax.ppermute(jnp.concatenate(parts, axis=0), axis, perm)
    result = []
    offset = 0
    for part in parts:
        result.append(lax.slice_in_dim(packed, offset, offset + part.shape[0], axis=0))
        offset += part.shape[0]
    return tuple(result)


def pair_sum(values, axis):
    if lax.axis_size(axis) != 2:
        return lax.psum(values, axis)
    other = packed_ppermute(values, axis, [(0, 1), (1, 0)])
    return tuple(mine + theirs for mine, theirs in zip(values, other))


def group_grads(back_real, back_imag, mode_real, mode_imag, axis):
    count = lax.axis_size(axis)
    index = lax.axis_index(axis)
    block = mode_real.shape[1] // count
    total = None
    for shift in range(count):
        target = (index + shift) % count
        piece = tuple(
            lax.dynamic_slice_in_dim(part, target * block, block, 1)
            for part in (back_real, back_imag, mode_real, mode_imag)
        )
        if shift:
            piece = packed_ppermute(piece, axis, [(i, (i + shift) % count) for i in range(count)])
        term = weight_grads(*piece)
        total = term if total is None else total + term
    return total


def body(
    field,
    counts,
    kappa_rows,
    kappa_cols,
    drift_rows,
    drift_cols,
    assign,
    buffer,
    lift_weight,
    lift_bias,
    point_weight,
    point_bias,
    spectral_weight,
    cotangent,
):
    above_row, below_row = halo_rows(field, ("grp", "mem", "row"))
    row_sums = solve_rows(
        field,
        above_row,
        below_row,
        counts[0],
        kappa_rows,
        drift_rows,
        kappa_cols,
        drift_cols,
    )
    lanes = 128
    grouping = (
        jnp.arange(lanes, dtype=jnp.int32)[:, None] // FACTOR
        == jnp.arange(lanes // FACTOR, dtype=jnp.int32)[None, :]
    ).astype(jnp.float32)
    grouped = jnp.dot(
        row_sums.reshape(-1, lanes), grouping, precision=lax.Precision.HIGHEST
    )
    coarse_rows = (grouped.reshape(C, SW) * (1.0 / (FACTOR * FACTOR)))[None]
    coarse_low = coarse_rows.astype(jnp.bfloat16)
    member = lax.axis_index("mem")
    member_rows = buffer.shape[1]
    total_rows = member_rows * lax.axis_size("mem")
    row_ids = member * member_rows + jnp.arange(member_rows, dtype=jnp.int32)
    owners = lax.dynamic_slice_in_dim(assign, member * member_rows, member_rows, 0)
    chosen = (owners == lax.axis_index("grp"))[:, None, None]
    forward_table = column_table()
    every_row = gather_rows(coarse_low[0], ("grp", "mem", "row"))
    fresh_rows = lax.dynamic_slice_in_dim(every_row, member * member_rows, member_rows, 0)
    sample = jnp.where(chosen, fresh_rows, buffer[0])
    hidden = lift_rows(sample, lift_weight, lift_bias)
    column_part = jnp.einsum(
        "yhx,xk->yhk", hidden, forward_table, preferred_element_type=jnp.float32
    )
    norm_scale = 1.0 / math.sqrt(total_rows * SW)
    cosine_table, sine_table = row_tables(row_ids, total_rows)
    part_real, part_imag = rows_forward(
        column_part[:, :, :MODES], column_part[:, :, MODES:], cosine_table, sine_table
    )
    mode_real, mode_imag = pair_sum((part_real * norm_scale, part_imag * norm_scale), "mem")
    mixed_real, mixed_imag = mix_modes(spectral_weight, mode_real, mode_imag)
    spatial = (
        jnp.einsum(
            "yok,kx->yox",
            rows_inverse(mixed_real, mixed_imag, cosine_table, sine_table),
            inverse_table(),
            precision=lax.Precision.HIGHEST,
        )
        * norm_scale
    )
    pre_act = (
        spatial
        + jnp.einsum("yhx,ho->yox", hidden, point_weight, preferred_element_type=jnp.float32)
        + point_bias[None, :, None]
    )
    layer_rows = jax.nn.gelu(pre_act, approximate=False).astype(jnp.bfloat16)[None]
    back_signal = (cotangent[0].astype(jnp.float32) * gelu_slope(pre_act)).astype(jnp.bfloat16)
    back_part = jnp.einsum(
        "yox,xk->yok", back_signal, forward_table, preferred_element_type=jnp.float32
    )
    back_real, back_imag = rows_forward(
        back_part[:, :, :MODES], back_part[:, :, MODES:], cosine_table, sine_table
    )
    weights_mode = jnp.where(jnp.arange(MODES) == 0, 1.0, 2.0).astype(jnp.float32) * norm_scale
    back_real, back_imag = pair_sum((back_real * weights_mode, back_imag * weights_mode), "mem")
    block_size = HID // lax.axis_size("mem")
    block_real = lax.dynamic_slice_in_dim(mode_real, member * block_size, block_size, 0)
    block_imag = lax.dynamic_slice_in_dim(mode_imag, member * block_size, block_size, 0)
    summed = group_grads(back_real, back_imag, block_real, block_imag, "grp")
    return (coarse_rows, layer_rows, summed / lax.axis_size("grp"))


def solution(mesh):
    in_specs = (
        P(None, ("grp", "mem", "row"), None),
        P(("grp", "mem", "row")),
        P(("grp", "mem", "row")),
        P(),
        P(None, ("grp", "mem", "row")),
        P(),
        P(),
        P("grp", "mem", None, None),
        P(),
        P(),
        P(None, "row"),
        P("row"),
        P(None, None, "row", None, None),
        P("grp", "mem", "row", None),
    )
    out_specs = (
        P(("grp", "mem", "row"), None, None),
        P("grp", "mem", "row", None),
        P(None, "mem", "row", "grp", None),
    )
    return jax.shard_map(body, mesh=mesh, in_specs=in_specs, out_specs=out_specs, check_vma=False)
```

```python
import math

import jax
import jax.numpy as jnp
from jax import lax
from jax.experimental import pallas as pl
from jax.experimental.pallas import tpu as pltpu
from jax.sharding import PartitionSpec as P

C = 4
SW = 1024
FACTOR = 16
HID = 32
MODES = 16


window_time = 0.24


def with_halo(block, sides, width):
    for axis, dim in sides:
        count = lax.axis_size(axis)
        forward = [(i, i + 1) for i in range(count - 1)]
        forward.append((count - 1, 0))
        backward = [(target, source) for source, target in forward]
        low = lax.ppermute(
            lax.slice_in_dim(block, block.shape[dim] - width, None, axis=dim), axis, forward
        )
        high = lax.ppermute(lax.slice_in_dim(block, 0, width, axis=dim), axis, backward)
        block = jnp.concatenate([low, block, high], axis=dim)
    return block


def halo_rows(block, axis):
    count = lax.axis_size(axis)
    forward = [(i, (i + 1) % count) for i in range(count)]
    backward = [((i + 1) % count, i) for i in range(count)]
    above = lax.ppermute(block[:, -1], axis, forward)
    below = lax.ppermute(block[:, 0], axis, backward)
    return above, below


def slab_solve(
    slab_rows, above_row, below_row, substeps, kappa_row, drift_row, kappa_col, drift_col
):
    diffusion = kappa_row[:, None] * kappa_col[None, :]
    drift_along = drift_row[0][:, None] * drift_col[0][None, :]
    drift_across = drift_row[1][:, None] * drift_col[1][None, :]
    step_size = window_time / substeps.astype(jnp.float32)

    def advance(number, current):
        stacked = jnp.concatenate([above_row, current, below_row], axis=1)
        upper_rows = stacked[:, :-2]
        lower_rows = stacked[:, 2:]
        right_cells = jnp.roll(current, -1, axis=2)
        left_cells = jnp.roll(current, 1, axis=2)
        change = diffusion * (right_cells + left_cells + upper_rows + lower_rows - 4.0 * current)
        change = (
            change
            - 0.5 * drift_along * (right_cells - left_cells)
            - 0.5 * drift_across * (lower_rows - upper_rows)
        )
        return current + step_size * change

    return lax.fori_loop(jnp.zeros((), jnp.int32), substeps, advance, slab_rows)


CHUNK = 2048
UNROLL = 8


def solve_kernel(
    step_ref, count_ref, field_ref, above_ref, below_ref, coef_ref, out_ref, first_ref, second_ref
):
    tracers, rows, width = field_ref.shape
    chunks = width // CHUNK

    def chunk_at(index):
        return pl.ds(pl.multiple_of(index * CHUNK, CHUNK), CHUNK)

    def prepare(index, carry):
        cols = chunk_at(index)
        for tracer in range(tracers):
            first_ref[tracer, :, cols] = field_ref[tracer, :, cols].astype(jnp.float32)
        return carry

    lax.fori_loop(0, chunks, prepare, 0, unroll=UNROLL)
    row_ids = lax.broadcasted_iota(jnp.int32, (rows, CHUNK), 0)

    def sweep(source_ref, target_ref):
        def update(column, inner):
            cols = chunk_at(column)
            before = pl.ds(pl.multiple_of(((column * CHUNK - 128) % width), 128), 128)
            after = pl.ds(pl.multiple_of((((column + 1) * CHUNK) % width), 128), 128)
            diffusion = coef_ref[0, :, cols]
            along = coef_ref[1, :, cols]
            across = coef_ref[2, :, cols]
            for tracer in range(tracers):
                current = source_ref[tracer, :, cols]
                extended = jnp.concatenate(
                    [source_ref[tracer, :, before], current, source_ref[tracer, :, after]], axis=1
                )
                span = CHUNK + 256
                right_cells = pltpu.roll(extended, span - 1, 1)[:, 128 : 128 + CHUNK]
                left_cells = pltpu.roll(extended, 1, 1)[:, 128 : 128 + CHUNK]
                upper_rows = jnp.where(
                    row_ids == 0, above_ref[tracer : tracer + 1, cols].astype(jnp.float32), pltpu.roll(current, 1, 0)
                )
                lower_rows = jnp.where(
                    row_ids == rows - 1, below_ref[tracer : tracer + 1, cols].astype(jnp.float32), pltpu.roll(current, rows - 1, 0)
                )
                change = diffusion * (
                    right_cells + left_cells + upper_rows + lower_rows - 4.0 * current
                )
                change = (
                    change
                    - along * (right_cells - left_cells)
                    - across * (lower_rows - upper_rows)
                )
                target_ref[tracer, :, cols] = current + change
            return inner

        lax.fori_loop(0, chunks, update, 0, unroll=UNROLL)

    def two_steps(number, carry):
        sweep(first_ref, second_ref)
        sweep(second_ref, first_ref)
        return carry

    total = count_ref[0]
    lax.fori_loop(0, total // 2, two_steps, 0)

    def collect(final_ref):
        def store(index, carry):
            cols = chunk_at(index)
            for tracer in range(tracers):
                out_ref[tracer : tracer + 1, cols] = jnp.sum(
                    final_ref[tracer, :, cols], axis=0, keepdims=True
                )
            return carry

        lax.fori_loop(0, chunks, store, 0, unroll=UNROLL)

    @pl.when(total % 2 == 1)
    def _():
        sweep(first_ref, second_ref)
        collect(second_ref)

    @pl.when(total % 2 == 0)
    def _():
        collect(first_ref)


def solve_rows(field, above_row, below_row, substeps, kappa_row, drift_row, kappa_col, drift_col):
    tracers, rows, width = field.shape
    step = (window_time / substeps.astype(jnp.float32)).reshape(1)
    kappa_col = kappa_col.astype(jnp.float32)
    drift_col = drift_col.astype(jnp.float32)
    coefficients = step * jnp.stack(
        [
            kappa_row[:, None] * kappa_col[None, :],
            0.5 * (drift_row[0][:, None] * drift_col[0][None, :]),
            0.5 * (drift_row[1][:, None] * drift_col[1][None, :]),
        ]
    )
    smem = pl.BlockSpec(memory_space=pltpu.SMEM)
    vmem = pl.BlockSpec(memory_space=pltpu.VMEM)
    return pl.pallas_call(
        solve_kernel,
        out_shape=jax.ShapeDtypeStruct((tracers, width), jnp.float32),
        in_specs=[smem, smem] + [vmem] * 4,
        out_specs=vmem,
        scratch_shapes=[
            pltpu.VMEM((tracers, rows, width), jnp.float32),
            pltpu.VMEM((tracers, rows, width), jnp.float32),
        ],
        compiler_params=pltpu.CompilerParams(vmem_limit_bytes=56 * 1024 * 1024),
    )(
        step,
        substeps.reshape(1),
        field,
        above_row,
        below_row,
        coefficients,
    )


def coarsen(stepped):
    return stepped.reshape(C, FACTOR, SW, FACTOR).mean(axis=(1, 3))


def column_table():
    columns = jnp.arange(SW, dtype=jnp.int32)
    orders = jnp.arange(MODES, dtype=jnp.int32)
    phase_angle = 2.0 * math.pi / SW * (columns[:, None] * orders[None, :] % SW).astype(jnp.float32)
    return jnp.concatenate([jnp.cos(phase_angle), -jnp.sin(phase_angle)], axis=1).astype(
        jnp.bfloat16
    )


def inverse_table():
    columns = jnp.arange(SW, dtype=jnp.int32)
    orders = jnp.arange(MODES, dtype=jnp.int32)
    phase_angle = 2.0 * math.pi / SW * (orders[:, None] * columns[None, :] % SW).astype(jnp.float32)
    weights = jnp.where(orders == 0, 1.0, 2.0).astype(jnp.float32)[:, None]
    return jnp.concatenate(
        [weights * jnp.cos(phase_angle), -weights * jnp.sin(phase_angle)], axis=0
    )


def row_tables(row_ids, total_rows):
    orders = jnp.arange(2 * MODES, dtype=jnp.int32)
    wave_numbers = jnp.where(orders < MODES, orders, total_rows - 2 * MODES + orders)
    phase_angle = (
        2.0
        * math.pi
        / total_rows
        * (wave_numbers[:, None] * row_ids[None, :] % total_rows).astype(jnp.float32)
    )
    return (jnp.cos(phase_angle), jnp.sin(phase_angle))


def rows_forward(part_real, part_imag, cosine_table, sine_table):
    highest = lax.Precision.HIGHEST
    real_part = jnp.einsum("jy,yhl->hjl", cosine_table, part_real, precision=highest) + jnp.einsum(
        "jy,yhl->hjl", sine_table, part_imag, precision=highest
    )
    imag_part = jnp.einsum("jy,yhl->hjl", cosine_table, part_imag, precision=highest) - jnp.einsum(
        "jy,yhl->hjl", sine_table, part_real, precision=highest
    )
    return (real_part, imag_part)


def rows_inverse(mixed_real, mixed_imag, cosine_table, sine_table):
    highest = lax.Precision.HIGHEST
    rows_real = jnp.einsum("jy,ojl->yol", cosine_table, mixed_real, precision=highest) - jnp.einsum(
        "jy,ojl->yol", sine_table, mixed_imag, precision=highest
    )
    rows_imag = jnp.einsum("jy,ojl->yol", sine_table, mixed_real, precision=highest) + jnp.einsum(
        "jy,ojl->yol", cosine_table, mixed_imag, precision=highest
    )
    return jnp.concatenate([rows_real, rows_imag], axis=2)


def mix_modes(spectral, mode_real, mode_imag):
    real_weight, imag_weight = spectral[0], spectral[1]
    mode_real = mode_real[:, None]
    mode_imag = mode_imag[:, None]
    mixed_real = jnp.sum(real_weight * mode_real - imag_weight * mode_imag, axis=0)
    mixed_imag = jnp.sum(real_weight * mode_imag + imag_weight * mode_real, axis=0)
    return (mixed_real, mixed_imag)


def gelu_slope(pre_act):
    normal_cdf = 0.5 * (1.0 + lax.erf(pre_act * (1.0 / math.sqrt(2.0))))
    density = jnp.exp(-0.5 * pre_act * pre_act) * (1.0 / math.sqrt(2.0 * math.pi))
    return normal_cdf + pre_act * density


def weight_grads(back_real, back_imag, mode_real, mode_imag):
    highest = lax.Precision.HIGHEST
    grad_real = jnp.einsum("ojl,hjl->hojl", back_real, mode_real, precision=highest) + jnp.einsum(
        "ojl,hjl->hojl", back_imag, mode_imag, precision=highest
    )
    grad_imag = jnp.einsum("ojl,hjl->hojl", back_imag, mode_real, precision=highest) - jnp.einsum(
        "ojl,hjl->hojl", back_real, mode_imag, precision=highest
    )
    return jnp.stack([grad_real, grad_imag])


def lift_rows(sample, lift_weight, lift_bias):
    lifted = jnp.einsum("ycx,ch->yhx", sample, lift_weight, preferred_element_type=jnp.float32)
    return (lifted + lift_bias[None, :, None]).astype(jnp.bfloat16)


def gather_along(block, axis):
    count = lax.axis_size(axis)
    index = lax.axis_index(axis)
    gathered = jnp.zeros((count,) + block.shape, block.dtype)
    for shift in range(count):
        if shift == 0:
            piece = block
        else:
            piece = lax.ppermute(block, axis, [(i, (i + shift) % count) for i in range(count)])
        gathered = lax.dynamic_update_index_in_dim(gathered, piece, (index - shift) % count, 0)
    return gathered


def gather_rows(block, axes):
    for axis in reversed(axes):
        block = gather_along(block, axis)
    return block.reshape((-1,) + block.shape[len(axes):])


def packed_ppermute(parts, axis, perm):
    packed = lax.ppermute(jnp.concatenate(parts, axis=0), axis, perm)
    result = []
    offset = 0
    for part in parts:
        result.append(lax.slice_in_dim(packed, offset, offset + part.shape[0], axis=0))
        offset += part.shape[0]
    return tuple(result)


def pair_sum(values, axis):
    if lax.axis_size(axis) != 2:
        return lax.psum(values, axis)
    other = packed_ppermute(values, axis, [(0, 1), (1, 0)])
    return tuple(mine + theirs for mine, theirs in zip(values, other))


def group_grads(back_real, back_imag, mode_real, mode_imag, axis):
    count = lax.axis_size(axis)
    index = lax.axis_index(axis)
    block = mode_real.shape[1] // count
    total = None
    for shift in range(count):
        target = (index + shift) % count
        piece = tuple(
            lax.dynamic_slice_in_dim(part, target * block, block, 1)
            for part in (back_real, back_imag, mode_real, mode_imag)
        )
        if shift:
            piece = packed_ppermute(piece, axis, [(i, (i + shift) % count) for i in range(count)])
        term = weight_grads(*piece)
        total = term if total is None else total + term
    return total


def body(
    field,
    counts,
    kappa_rows,
    kappa_cols,
    drift_rows,
    drift_cols,
    assign,
    buffer,
    lift_weight,
    lift_bias,
    point_weight,
    point_bias,
    spectral_weight,
    cotangent,
):
    above_row, below_row = halo_rows(field, ("grp", "mem", "row"))
    row_sums = solve_rows(
        field,
        above_row,
        below_row,
        counts[0],
        kappa_rows,
        drift_rows,
        kappa_cols,
        drift_cols,
    )
    lanes = 128
    grouping = (
        jnp.arange(lanes, dtype=jnp.int32)[:, None] // FACTOR
        == jnp.arange(lanes // FACTOR, dtype=jnp.int32)[None, :]
    ).astype(jnp.float32)
    grouped = jnp.dot(
        row_sums.reshape(-1, lanes), grouping, precision=lax.Precision.HIGHEST
    )
    coarse_rows = (grouped.reshape(C, SW) * (1.0 / (FACTOR * FACTOR)))[None]
    coarse_low = coarse_rows.astype(jnp.bfloat16)
    member = lax.axis_index("mem")
    member_rows = buffer.shape[1]
    total_rows = member_rows * lax.axis_size("mem")
    row_ids = member * member_rows + jnp.arange(member_rows, dtype=jnp.int32)
    owners = lax.dynamic_slice_in_dim(assign, member * member_rows, member_rows, 0)
    chosen = (owners == lax.axis_index("grp"))[:, None, None]
    forward_table = column_table()
    every_row = gather_rows(coarse_low[0], ("grp", "mem", "row"))
    fresh_rows = lax.dynamic_slice_in_dim(every_row, member * member_rows, member_rows, 0)
    sample = jnp.where(chosen, fresh_rows, buffer[0])
    hidden = lift_rows(sample, lift_weight, lift_bias)
    column_part = jnp.einsum(
        "yhx,xk->yhk", hidden, forward_table, preferred_element_type=jnp.float32
    )
    norm_scale = 1.0 / math.sqrt(total_rows * SW)
    cosine_table, sine_table = row_tables(row_ids, total_rows)
    part_real, part_imag = rows_forward(
        column_part[:, :, :MODES], column_part[:, :, MODES:], cosine_table, sine_table
    )
    mode_real, mode_imag = pair_sum((part_real * norm_scale, part_imag * norm_scale), "mem")
    mixed_real, mixed_imag = mix_modes(spectral_weight, mode_real, mode_imag)
    spatial = (
        jnp.einsum(
            "yok,kx->yox",
            rows_inverse(mixed_real, mixed_imag, cosine_table, sine_table),
            inverse_table(),
            precision=lax.Precision.HIGHEST,
        )
        * norm_scale
    )
    pre_act = (
        spatial
        + jnp.einsum("yhx,ho->yox", hidden, point_weight, preferred_element_type=jnp.float32)
        + point_bias[None, :, None]
    )
    layer_rows = jax.nn.gelu(pre_act, approximate=False).astype(jnp.bfloat16)[None]
    back_signal = (cotangent[0].astype(jnp.float32) * gelu_slope(pre_act)).astype(jnp.bfloat16)
    back_part = jnp.einsum(
        "yox,xk->yok", back_signal, forward_table, preferred_element_type=jnp.float32
    )
    back_real, back_imag = rows_forward(
        back_part[:, :, :MODES], back_part[:, :, MODES:], cosine_table, sine_table
    )
    weights_mode = jnp.where(jnp.arange(MODES) == 0, 1.0, 2.0).astype(jnp.float32) * norm_scale
    back_real, back_imag = pair_sum((back_real * weights_mode, back_imag * weights_mode), "mem")
    block_size = HID // lax.axis_size("mem")
    block_real = lax.dynamic_slice_in_dim(mode_real, member * block_size, block_size, 0)
    block_imag = lax.dynamic_slice_in_dim(mode_imag, member * block_size, block_size, 0)
    summed = group_grads(back_real, back_imag, block_real, block_imag, "grp")
    return (coarse_rows, layer_rows, summed / lax.axis_size("grp"))


def solution(mesh):
    in_specs = (
        P(None, ("grp", "mem", "row"), None),
        P(("grp", "mem", "row")),
        P(("grp", "mem", "row")),
        P(),
        P(None, ("grp", "mem", "row")),
        P(),
        P(),
        P("grp", "mem", None, None),
        P(),
        P(),
        P(None, "row"),
        P("row"),
        P(None, None, "row", None, None),
        P("grp", "mem", "row", None),
    )
    out_specs = (
        P(("grp", "mem", "row"), None, None),
        P("grp", "mem", "row", None),
        P(None, "mem", "row", "grp", None),
    )
    return jax.shard_map(body, mesh=mesh, in_specs=in_specs, out_specs=out_specs, check_vma=False)
```

```python
import math

import jax
import jax.numpy as jnp
from jax import lax
from jax.experimental import pallas as pl
from jax.experimental.pallas import tpu as pltpu
from jax.sharding import PartitionSpec as P

C = 4
SW = 1024
FACTOR = 16
HID = 32
MODES = 16


window_time = 0.24


def with_halo(block, sides, width):
    for axis, dim in sides:
        count = lax.axis_size(axis)
        forward = [(i, i + 1) for i in range(count - 1)]
        forward.append((count - 1, 0))
        backward = [(target, source) for source, target in forward]
        low = lax.ppermute(
            lax.slice_in_dim(block, block.shape[dim] - width, None, axis=dim), axis, forward
        )
        high = lax.ppermute(lax.slice_in_dim(block, 0, width, axis=dim), axis, backward)
        block = jnp.concatenate([low, block, high], axis=dim)
    return block


def halo_rows(block, axis):
    count = lax.axis_size(axis)
    forward = [(i, (i + 1) % count) for i in range(count)]
    backward = [((i + 1) % count, i) for i in range(count)]
    above = lax.ppermute(block[:, -1], axis, forward)
    below = lax.ppermute(block[:, 0], axis, backward)
    return above, below


def slab_solve(
    slab_rows, above_row, below_row, substeps, kappa_row, drift_row, kappa_col, drift_col
):
    diffusion = kappa_row[:, None] * kappa_col[None, :]
    drift_along = drift_row[0][:, None] * drift_col[0][None, :]
    drift_across = drift_row[1][:, None] * drift_col[1][None, :]
    step_size = window_time / substeps.astype(jnp.float32)

    def advance(number, current):
        stacked = jnp.concatenate([above_row, current, below_row], axis=1)
        upper_rows = stacked[:, :-2]
        lower_rows = stacked[:, 2:]
        right_cells = jnp.roll(current, -1, axis=2)
        left_cells = jnp.roll(current, 1, axis=2)
        change = diffusion * (right_cells + left_cells + upper_rows + lower_rows - 4.0 * current)
        change = (
            change
            - 0.5 * drift_along * (right_cells - left_cells)
            - 0.5 * drift_across * (lower_rows - upper_rows)
        )
        return current + step_size * change

    return lax.fori_loop(jnp.zeros((), jnp.int32), substeps, advance, slab_rows)


CHUNK = 2048
UNROLL = 8


def solve_kernel(
    step_ref, count_ref, field_ref, above_ref, below_ref, coef_ref, group_ref, out_ref, first_ref, second_ref
):
    tracers, rows, width = field_ref.shape
    chunks = width // CHUNK

    def chunk_at(index):
        return pl.ds(pl.multiple_of(index * CHUNK, CHUNK), CHUNK)

    def prepare(index, carry):
        cols = chunk_at(index)
        for tracer in range(tracers):
            first_ref[tracer, :, cols] = field_ref[tracer, :, cols].astype(jnp.float32)
        return carry

    lax.fori_loop(0, chunks, prepare, 0, unroll=UNROLL)
    row_ids = lax.broadcasted_iota(jnp.int32, (rows, CHUNK), 0)

    def sweep(source_ref, target_ref):
        def update(column, inner):
            cols = chunk_at(column)
            before = pl.ds(pl.multiple_of(((column * CHUNK - 128) % width), 128), 128)
            after = pl.ds(pl.multiple_of((((column + 1) * CHUNK) % width), 128), 128)
            diffusion = coef_ref[0, :, cols]
            along = coef_ref[1, :, cols]
            across = coef_ref[2, :, cols]
            for tracer in range(tracers):
                current = source_ref[tracer, :, cols]
                extended = jnp.concatenate(
                    [source_ref[tracer, :, before], current, source_ref[tracer, :, after]], axis=1
                )
                span = CHUNK + 256
                right_cells = pltpu.roll(extended, span - 1, 1)[:, 128 : 128 + CHUNK]
                left_cells = pltpu.roll(extended, 1, 1)[:, 128 : 128 + CHUNK]
                upper_rows = jnp.where(
                    row_ids == 0, above_ref[tracer : tracer + 1, cols].astype(jnp.float32), pltpu.roll(current, 1, 0)
                )
                lower_rows = jnp.where(
                    row_ids == rows - 1, below_ref[tracer : tracer + 1, cols].astype(jnp.float32), pltpu.roll(current, rows - 1, 0)
                )
                change = diffusion * (
                    right_cells + left_cells + upper_rows + lower_rows - 4.0 * current
                )
                change = (
                    change
                    - along * (right_cells - left_cells)
                    - across * (lower_rows - upper_rows)
                )
                target_ref[tracer, :, cols] = current + change
            return inner

        lax.fori_loop(0, chunks, update, 0, unroll=UNROLL)

    def two_steps(number, carry):
        sweep(first_ref, second_ref)
        sweep(second_ref, first_ref)
        return carry

    total = count_ref[0]
    lax.fori_loop(0, total // 2, two_steps, 0)

    def collect(final_ref):
        def store(index, carry):
            cols = chunk_at(index)
            narrow = pl.ds(pl.multiple_of(index * (CHUNK // FACTOR), CHUNK // FACTOR), CHUNK // FACTOR)
            for tracer in range(tracers):
                grouped = jnp.dot(
                    final_ref[tracer, :, cols],
                    group_ref[...],
                    precision=lax.Precision.HIGHEST,
                    preferred_element_type=jnp.float32,
                )
                out_ref[tracer : tracer + 1, narrow] = jnp.sum(grouped, axis=0, keepdims=True)
            return carry

        lax.fori_loop(0, chunks, store, 0, unroll=UNROLL)

    @pl.when(total % 2 == 1)
    def _():
        sweep(first_ref, second_ref)
        collect(second_ref)

    @pl.when(total % 2 == 0)
    def _():
        collect(first_ref)


def solve_rows(field, above_row, below_row, substeps, kappa_row, drift_row, kappa_col, drift_col):
    tracers, rows, width = field.shape
    step = (window_time / substeps.astype(jnp.float32)).reshape(1)
    grouping = (
        jnp.arange(CHUNK, dtype=jnp.int32)[:, None] // FACTOR
        == jnp.arange(CHUNK // FACTOR, dtype=jnp.int32)[None, :]
    ).astype(jnp.float32)
    kappa_col = kappa_col.astype(jnp.float32)
    drift_col = drift_col.astype(jnp.float32)
    coefficients = step * jnp.stack(
        [
            kappa_row[:, None] * kappa_col[None, :],
            0.5 * (drift_row[0][:, None] * drift_col[0][None, :]),
            0.5 * (drift_row[1][:, None] * drift_col[1][None, :]),
        ]
    )
    smem = pl.BlockSpec(memory_space=pltpu.SMEM)
    vmem = pl.BlockSpec(memory_space=pltpu.VMEM)
    return pl.pallas_call(
        solve_kernel,
        out_shape=jax.ShapeDtypeStruct((tracers, width // FACTOR), jnp.float32),
        in_specs=[smem, smem] + [vmem] * 5,
        out_specs=vmem,
        scratch_shapes=[
            pltpu.VMEM((tracers, rows, width), jnp.float32),
            pltpu.VMEM((tracers, rows, width), jnp.float32),
        ],
        compiler_params=pltpu.CompilerParams(vmem_limit_bytes=56 * 1024 * 1024),
    )(
        step,
        substeps.reshape(1),
        field,
        above_row,
        below_row,
        coefficients,
        grouping,
    )


def coarsen(stepped):
    return stepped.reshape(C, FACTOR, SW, FACTOR).mean(axis=(1, 3))


def column_table():
    columns = jnp.arange(SW, dtype=jnp.int32)
    orders = jnp.arange(MODES, dtype=jnp.int32)
    phase_angle = 2.0 * math.pi / SW * (columns[:, None] * orders[None, :] % SW).astype(jnp.float32)
    return jnp.concatenate([jnp.cos(phase_angle), -jnp.sin(phase_angle)], axis=1).astype(
        jnp.bfloat16
    )


def inverse_table():
    columns = jnp.arange(SW, dtype=jnp.int32)
    orders = jnp.arange(MODES, dtype=jnp.int32)
    phase_angle = 2.0 * math.pi / SW * (orders[:, None] * columns[None, :] % SW).astype(jnp.float32)
    weights = jnp.where(orders == 0, 1.0, 2.0).astype(jnp.float32)[:, None]
    return jnp.concatenate(
        [weights * jnp.cos(phase_angle), -weights * jnp.sin(phase_angle)], axis=0
    )


def row_tables(row_ids, total_rows):
    orders = jnp.arange(2 * MODES, dtype=jnp.int32)
    wave_numbers = jnp.where(orders < MODES, orders, total_rows - 2 * MODES + orders)
    phase_angle = (
        2.0
        * math.pi
        / total_rows
        * (wave_numbers[:, None] * row_ids[None, :] % total_rows).astype(jnp.float32)
    )
    return (jnp.cos(phase_angle), jnp.sin(phase_angle))


def rows_forward(part_real, part_imag, cosine_table, sine_table):
    highest = lax.Precision.HIGHEST
    real_part = jnp.einsum("jy,yhl->hjl", cosine_table, part_real, precision=highest) + jnp.einsum(
        "jy,yhl->hjl", sine_table, part_imag, precision=highest
    )
    imag_part = jnp.einsum("jy,yhl->hjl", cosine_table, part_imag, precision=highest) - jnp.einsum(
        "jy,yhl->hjl", sine_table, part_real, precision=highest
    )
    return (real_part, imag_part)


def rows_inverse(mixed_real, mixed_imag, cosine_table, sine_table):
    highest = lax.Precision.HIGHEST
    rows_real = jnp.einsum("jy,ojl->yol", cosine_table, mixed_real, precision=highest) - jnp.einsum(
        "jy,ojl->yol", sine_table, mixed_imag, precision=highest
    )
    rows_imag = jnp.einsum("jy,ojl->yol", sine_table, mixed_real, precision=highest) + jnp.einsum(
        "jy,ojl->yol", cosine_table, mixed_imag, precision=highest
    )
    return jnp.concatenate([rows_real, rows_imag], axis=2)


def mix_modes(spectral, mode_real, mode_imag):
    real_weight, imag_weight = spectral[0], spectral[1]
    mode_real = mode_real[:, None]
    mode_imag = mode_imag[:, None]
    mixed_real = jnp.sum(real_weight * mode_real - imag_weight * mode_imag, axis=0)
    mixed_imag = jnp.sum(real_weight * mode_imag + imag_weight * mode_real, axis=0)
    return (mixed_real, mixed_imag)


def gelu_slope(pre_act):
    normal_cdf = 0.5 * (1.0 + lax.erf(pre_act * (1.0 / math.sqrt(2.0))))
    density = jnp.exp(-0.5 * pre_act * pre_act) * (1.0 / math.sqrt(2.0 * math.pi))
    return normal_cdf + pre_act * density


def weight_grads(back_real, back_imag, mode_real, mode_imag):
    highest = lax.Precision.HIGHEST
    grad_real = jnp.einsum("ojl,hjl->hojl", back_real, mode_real, precision=highest) + jnp.einsum(
        "ojl,hjl->hojl", back_imag, mode_imag, precision=highest
    )
    grad_imag = jnp.einsum("ojl,hjl->hojl", back_imag, mode_real, precision=highest) - jnp.einsum(
        "ojl,hjl->hojl", back_real, mode_imag, precision=highest
    )
    return jnp.stack([grad_real, grad_imag])


def lift_rows(sample, lift_weight, lift_bias):
    lifted = jnp.einsum("ycx,ch->yhx", sample, lift_weight, preferred_element_type=jnp.float32)
    return (lifted + lift_bias[None, :, None]).astype(jnp.bfloat16)


def gather_along(block, axis):
    count = lax.axis_size(axis)
    index = lax.axis_index(axis)
    gathered = jnp.zeros((count,) + block.shape, block.dtype)
    for shift in range(count):
        if shift == 0:
            piece = block
        else:
            piece = lax.ppermute(block, axis, [(i, (i + shift) % count) for i in range(count)])
        gathered = lax.dynamic_update_index_in_dim(gathered, piece, (index - shift) % count, 0)
    return gathered


def gather_rows(block, axes):
    for axis in reversed(axes):
        block = gather_along(block, axis)
    return block.reshape((-1,) + block.shape[len(axes):])


def packed_ppermute(parts, axis, perm):
    packed = lax.ppermute(jnp.concatenate(parts, axis=0), axis, perm)
    result = []
    offset = 0
    for part in parts:
        result.append(lax.slice_in_dim(packed, offset, offset + part.shape[0], axis=0))
        offset += part.shape[0]
    return tuple(result)


def pair_sum(values, axis):
    if lax.axis_size(axis) != 2:
        return lax.psum(values, axis)
    other = packed_ppermute(values, axis, [(0, 1), (1, 0)])
    return tuple(mine + theirs for mine, theirs in zip(values, other))


def group_grads(back_real, back_imag, mode_real, mode_imag, axis):
    count = lax.axis_size(axis)
    index = lax.axis_index(axis)
    block = mode_real.shape[1] // count
    total = None
    for shift in range(count):
        target = (index + shift) % count
        piece = tuple(
            lax.dynamic_slice_in_dim(part, target * block, block, 1)
            for part in (back_real, back_imag, mode_real, mode_imag)
        )
        if shift:
            piece = packed_ppermute(piece, axis, [(i, (i + shift) % count) for i in range(count)])
        term = weight_grads(*piece)
        total = term if total is None else total + term
    return total


def body(
    field,
    counts,
    kappa_rows,
    kappa_cols,
    drift_rows,
    drift_cols,
    assign,
    buffer,
    lift_weight,
    lift_bias,
    point_weight,
    point_bias,
    spectral_weight,
    cotangent,
):
    above_row, below_row = halo_rows(field, ("grp", "mem", "row"))
    row_sums = solve_rows(
        field,
        above_row,
        below_row,
        counts[0],
        kappa_rows,
        drift_rows,
        kappa_cols,
        drift_cols,
    )
    coarse_rows = (row_sums * (1.0 / (FACTOR * FACTOR)))[None]
    coarse_low = coarse_rows.astype(jnp.bfloat16)
    member = lax.axis_index("mem")
    member_rows = buffer.shape[1]
    total_rows = member_rows * lax.axis_size("mem")
    row_ids = member * member_rows + jnp.arange(member_rows, dtype=jnp.int32)
    owners = lax.dynamic_slice_in_dim(assign, member * member_rows, member_rows, 0)
    chosen = (owners == lax.axis_index("grp"))[:, None, None]
    forward_table = column_table()
    every_row = gather_rows(coarse_low[0], ("grp", "mem", "row"))
    fresh_rows = lax.dynamic_slice_in_dim(every_row, member * member_rows, member_rows, 0)
    sample = jnp.where(chosen, fresh_rows, buffer[0])
    hidden = lift_rows(sample, lift_weight, lift_bias)
    column_part = jnp.einsum(
        "yhx,xk->yhk", hidden, forward_table, preferred_element_type=jnp.float32
    )
    norm_scale = 1.0 / math.sqrt(total_rows * SW)
    cosine_table, sine_table = row_tables(row_ids, total_rows)
    part_real, part_imag = rows_forward(
        column_part[:, :, :MODES], column_part[:, :, MODES:], cosine_table, sine_table
    )
    mode_real, mode_imag = pair_sum((part_real * norm_scale, part_imag * norm_scale), "mem")
    mixed_real, mixed_imag = mix_modes(spectral_weight, mode_real, mode_imag)
    spatial = (
        jnp.einsum(
            "yok,kx->yox",
            rows_inverse(mixed_real, mixed_imag, cosine_table, sine_table),
            inverse_table(),
            precision=lax.Precision.HIGHEST,
        )
        * norm_scale
    )
    pre_act = (
        spatial
        + jnp.einsum("yhx,ho->yox", hidden, point_weight, preferred_element_type=jnp.float32)
        + point_bias[None, :, None]
    )
    layer_rows = jax.nn.gelu(pre_act, approximate=False).astype(jnp.bfloat16)[None]
    back_signal = (cotangent[0].astype(jnp.float32) * gelu_slope(pre_act)).astype(jnp.bfloat16)
    back_part = jnp.einsum(
        "yox,xk->yok", back_signal, forward_table, preferred_element_type=jnp.float32
    )
    back_real, back_imag = rows_forward(
        back_part[:, :, :MODES], back_part[:, :, MODES:], cosine_table, sine_table
    )
    weights_mode = jnp.where(jnp.arange(MODES) == 0, 1.0, 2.0).astype(jnp.float32) * norm_scale
    back_real, back_imag = pair_sum((back_real * weights_mode, back_imag * weights_mode), "mem")
    block_size = HID // lax.axis_size("mem")
    block_real = lax.dynamic_slice_in_dim(mode_real, member * block_size, block_size, 0)
    block_imag = lax.dynamic_slice_in_dim(mode_imag, member * block_size, block_size, 0)
    summed = group_grads(back_real, back_imag, block_real, block_imag, "grp")
    return (coarse_rows, layer_rows, summed / lax.axis_size("grp"))


def solution(mesh):
    in_specs = (
        P(None, ("grp", "mem", "row"), None),
        P(("grp", "mem", "row")),
        P(("grp", "mem", "row")),
        P(),
        P(None, ("grp", "mem", "row")),
        P(),
        P(),
        P("grp", "mem", None, None),
        P(),
        P(),
        P(None, "row"),
        P("row"),
        P(None, None, "row", None, None),
        P("grp", "mem", "row", None),
    )
    out_specs = (
        P(("grp", "mem", "row"), None, None),
        P("grp", "mem", "row", None),
        P(None, "mem", "row", "grp", None),
    )
    return jax.shard_map(body, mesh=mesh, in_specs=in_specs, out_specs=out_specs, check_vma=False)
```
